32 devices in a mesh: groups: 2 (over y), ctx: 8 (over z, x), head: 2 (over core).
Axes of the slice: x: 2, y: 2, z: 4, core: 2. Of those that a mesh axis runs over, the one named last changes fastest.
Arguments:
- byte_states: float32 [4096, 1024], P(('groups', 'ctx'), 'head'), parts along dimension 0, may hold values from -8 to 8
- doc_length: int32 [2], P('groups'), parts along dimension 0, may hold values from 1920 to 2048
- block_ids: int32 [1024], P('groups'), parts along dimension 0, may hold values from 0 to 31, never falling along the last dimension, each value on 1 to 64 neighbouring positions
- qk_kernel: float32 [8, 4, 1024], P(None, None, 'head'), may hold values from -2 to 2
- value_kernel: float32 [8, 4, 1024], P(None, None, 'head'), may hold values from -2 to 2
- up_kernel: float32 [8, 4, 1024], P(None, None, 'head'), may hold values from -2 to 2
Outputs:
- mixed: float32 [4096, 1024], P(('groups', 'ctx'), 'head'), parts along dimension 0
The draws below stay inside these ranges and needn't reach their ends.
There are 2 independent parts, one for each index of `groups`. The reference program is written for one: setup_inputs(seed, part) draws one part's arguments, and reference() takes and returns one part's arrays. A program takes and returns all parts, laid end to end along the dimension named above; an argument that names none is the same for every part. Nothing has to cross between parts.
Inputs may be any that keep to these rules, and one draw needn't show every extreme that they name: block_ids never falls along the positions.
All inputs are finite; a program needn't handle non-finite values.
Results may differ from the reference program's by a relative error of at most 0.012.
Values may be sent and summed in bfloat16 or wider, within the bound.
No kernel may reach another device: no remote copies, remote signals or barrier semaphores. Data moves between devices by JAX's collectives and lax.ppermute only.
A program may use at most 64 MiB of HBM per device.

```python
import math
import jax
import jax.numpy as jnp
import numpy as np
from jax import lax

BW = 1024
HEADS = 32
CHANNEL_WIDTH = 128
STRIDE = 4
KERNEL = 8
B_DEV = 256
BYTES = 2048
REDUCED_STEPS = 512
SEGS = 32


def draw_byte_states(key, part):
    base_key, scale_key = jax.random.split(key, 2)
    entries = jax.random.normal(base_key, (BYTES, BW), jnp.float32)
    row_scale = jnp.exp(jax.random.uniform(scale_key, (BYTES, 1), jnp.float32, math.log(0.5), math.log(2.0)))
    states = jnp.clip(entries * row_scale, -8.0, 8.0)
    return states


def block_levels(stream_key, dims, cuts, low, top_value):
    factor_of = 1.0
    for dim, blocks in cuts:
        heights = jax.random.uniform(jax.random.fold_in(jax.random.fold_in(stream_key, 6), dim), (blocks,), jnp.float32, low / len(cuts), top_value / len(cuts))
        factor_of = factor_of * jnp.repeat(jnp.exp(heights), dims[dim] // blocks).reshape((-1,) + (1,) * (len(dims) - 1 - dim))
    return factor_of


def split_up(amount, total, reach, lean):
    portions = [(1 << 20) // math.isqrt(grade ** lean) + 1 for grade in range(2, amount + 1)]
    surplus, counts = total - reach - (amount - 1), [1] * (amount - 1)
    while surplus > 0:
        free = [i for i in range(amount - 1) if counts[i] < reach]
        pool, budget = sum([portions[i] for i in free]), surplus
        for i in free:
            more = min(reach - counts[i], max(1, budget * portions[i] // pool), surplus)
            counts[i] = counts[i] + more
            surplus = surplus - more
    return np.array([reach] + counts)


def uneven_parts(key, number_of, total, reach, lean):
    if number_of == 2:
        one = jax.random.randint(key, (), max(1, total - reach), min(reach, total - 1) + 1)
        return jnp.stack([one, total - one])
    lengths = jnp.asarray(split_up(number_of, total, reach, lean), jnp.int32)
    twos = (number_of - 1) // 2
    giver, taker = lengths[1:1 + 2 * twos:2], lengths[2:2 + 2 * twos:2]
    slack = jnp.minimum(giver - 1, reach - taker)
    moved = jax.random.randint(jax.random.fold_in(key, 1), (twos,), 0, 1 << 20) % (slack + 1)
    lengths = lengths.at[1:1 + 2 * twos:2].set(giver - moved).at[2:2 + 2 * twos:2].set(taker + moved)
    return lengths[jax.random.permutation(jax.random.fold_in(key, 2), number_of)]


def noise(key, dims, scale, bound, shards=(), kind=jnp.bfloat16):
    values = scale * jax.random.normal(key, dims, jnp.float32)
    if shards:
        values = values * block_levels(key, dims, shards, -0.22, 0.18)
    return jnp.clip(values, -bound, bound).astype(kind)


def setup_inputs(seed: int = 0, part: int = 0) -> dict:
    streams_of = jax.random.split(jax.random.key(seed), 7)
    part_splits = jax.random.split(jax.random.fold_in(streams_of[6], part), 7)
    byte_states = draw_byte_states(jax.random.fold_in(jax.random.fold_in(streams_of[6], part), 71), part)
    doc_length = jax.random.randint(part_splits[1], (1,), BYTES - B_DEV // 2, BYTES + 1).astype(jnp.int32)
    block_ids = jnp.searchsorted(jnp.cumsum(uneven_parts(part_splits[2], SEGS, REDUCED_STEPS, 64, 2)), jnp.arange(REDUCED_STEPS), side="right").astype(jnp.int32)
    qk_kernel = noise(streams_of[3], (KERNEL, STRIDE, BW), KERNEL ** -0.5, 2.0, ((2, 2),), jnp.float32)
    value_kernel = noise(streams_of[4], (KERNEL, STRIDE, BW), KERNEL ** -0.5, 2.0, ((2, 2),), jnp.float32)
    up_kernel = noise(streams_of[5], (KERNEL, STRIDE, BW), (2 * STRIDE) ** -0.5, 2.0, ((2, 2),), jnp.float32)
    return dict(byte_states=byte_states, doc_length=doc_length, block_ids=block_ids, qk_kernel=qk_kernel, value_kernel=value_kernel, up_kernel=up_kernel)


def shorten(byte_states, kernel):
    padded = jnp.concatenate([jnp.zeros((KERNEL - STRIDE, BW), jnp.float32), byte_states], 0)
    earlier = padded[:BYTES].reshape(REDUCED_STEPS, STRIDE, BW)
    current = byte_states.reshape(REDUCED_STEPS, STRIDE, BW)
    totals = jnp.zeros((REDUCED_STEPS, STRIDE, BW), jnp.float32)
    for offset in range(STRIDE):
        totals = totals + earlier[:, offset, None, :] * kernel[offset][None]
        totals = totals + current[:, offset, None, :] * kernel[offset + STRIDE][None]
    return totals.astype(jnp.bfloat16)

def reference(byte_states, doc_length, block_ids, qk_kernel, value_kernel, up_kernel):
    key_rows = shorten(byte_states, qk_kernel).reshape(REDUCED_STEPS, HEADS, CHANNEL_WIDTH)
    value_rows = shorten(byte_states, value_kernel).reshape(REDUCED_STEPS, HEADS, CHANNEL_WIDTH)
    lat_len = doc_length[0] // STRIDE
    reduced_steps = jnp.arange(REDUCED_STEPS, dtype=jnp.int32)
    sharpness_divisor = jnp.log(reduced_steps.astype(jnp.float32) + 2.0) / (jnp.sqrt(jnp.float32(CHANNEL_WIDTH)) * jnp.sqrt(jnp.log(jnp.float32(REDUCED_STEPS))))
    visible = (block_ids[None, :] <= block_ids[:, None]) & (reduced_steps[None, :] < lat_len) & ((reduced_steps[None, :] != reduced_steps[:, None]) | (reduced_steps[:, None] == 0))

    def one_head(operands):
        matched_vectors, head_values = operands
        raw_affinity = jnp.dot(matched_vectors, matched_vectors.T, preferred_element_type=jnp.float32) * sharpness_divisor[:, None]
        raw_affinity = jnp.where(visible, raw_affinity, -jnp.inf)
        weights = jnp.exp(raw_affinity - lax.optimization_barrier(jnp.max(raw_affinity, axis=1, keepdims=True)))
        totals = lax.optimization_barrier(jnp.sum(weights, axis=1, keepdims=True))
        result_rows = jnp.dot(weights.astype(jnp.bfloat16), head_values, preferred_element_type=jnp.float32)
        return (result_rows / totals).astype(jnp.bfloat16)
    attended = lax.map(one_head, (key_rows.transpose(1, 0, 2), value_rows.transpose(1, 0, 2)))
    attended = attended.transpose(1, 0, 2).reshape(REDUCED_STEPS, STRIDE, BW).astype(jnp.float32)
    zero_row = jnp.zeros((1, STRIDE, BW), jnp.float32)
    prior_one = jnp.concatenate([zero_row, attended[:-1]], 0)
    prior_two = jnp.concatenate([zero_row, zero_row, attended[:-2]], 0)
    branch = jnp.zeros((REDUCED_STEPS, STRIDE, BW), jnp.float32)
    for offset in range(STRIDE):
        branch = branch + prior_one[:, offset, None, :] * up_kernel[:STRIDE, offset][None]
        branch = branch + prior_two[:, offset, None, :] * up_kernel[STRIDE:, offset][None]
    branch = branch.reshape(BYTES, BW)
    byte_pos = jnp.arange(BYTES, dtype=jnp.int32)
    return byte_states + jnp.where(byte_pos[:, None] < doc_length[0], branch, 0.0)
```

```python
import functools
import math

import jax
import jax.numpy as jnp
from jax import lax
from jax.experimental import pallas as pl
from jax.experimental.pallas import tpu as pltpu
from jax.sharding import PartitionSpec as P

CHANNEL_WIDTH = 128
STRIDE = 4
KERNEL = 8


def shifted(x, axis, by):
    devices = lax.axis_size(axis)
    pairs = [(i, i + by) for i in range(devices) if 0 <= i + by < devices]
    return lax.ppermute(x, axis, pairs)


def shorten_kernel(x_ref, rim_ref, qk_ref, vk_ref, out_ref):
    rows, lanes = x_ref.shape
    lat = rows // STRIDE
    first_row = lax.broadcasted_iota(jnp.int32, (lat, lanes), 0) == 0
    taps = [None] * KERNEL
    for k in range(STRIDE):
        current = x_ref[pl.ds(k, lat, stride=STRIDE), :]
        earlier = pltpu.roll(current, 1, 0)
        earlier = jnp.where(first_row, rim_ref[pl.ds(k, 1), :], earlier)
        taps[k] = earlier
        taps[k + STRIDE] = current
    for which, kern_ref in enumerate((qk_ref, vk_ref)):
        for t in range(STRIDE):
            total = taps[0] * kern_ref[0, pl.ds(t, 1), :]
            for k in range(1, KERNEL):
                total = total + taps[k] * kern_ref[k, pl.ds(t, 1), :]
            out_ref[t, 0, which, 0] = total.astype(jnp.bfloat16)


def shorten_both(byte_states, rim_rows, qk_kernel, value_kernel, per_t, nq):
    rows, channels = byte_states.shape
    lat = rows // STRIDE
    lanes = CHANNEL_WIDTH
    blocks = channels // lanes
    return pl.pallas_call(
        shorten_kernel,
        grid=(blocks,),
        out_shape=jax.ShapeDtypeStruct((STRIDE, per_t, 2, nq, lat, lanes), jnp.bfloat16),
        in_specs=[
            pl.BlockSpec((rows, lanes), lambda b: (0, b)),
            pl.BlockSpec((KERNEL - STRIDE, lanes), lambda b: (0, b)),
            pl.BlockSpec((KERNEL, STRIDE, lanes), lambda b: (0, 0, b)),
            pl.BlockSpec((KERNEL, STRIDE, lanes), lambda b: (0, 0, b)),
        ],
        out_specs=pl.BlockSpec(
            (STRIDE, 1, 2, 1, lat, lanes), lambda b: (0, b // nq, 0, b % nq, 0, 0)
        ),
        cost_estimate=pl.CostEstimate(
            flops=4 * KERNEL * rows * channels,
            bytes_accessed=4 * rows * channels + 2 * KERNEL * STRIDE * channels * 4 + 2 * rows * channels * 2,
            transcendentals=0,
        ),
    )(byte_states, rim_rows, qk_kernel, value_kernel)


def body(byte_states, doc_length, block_ids, qk_kernel, value_kernel, up_kernel):
    rows_here, channels = byte_states.shape
    lat_dev = rows_here // STRIDE
    n_ctx = lax.axis_size("ctx")
    device = lax.axis_index("ctx")
    lat_total = lat_dev * n_ctx
    rim_rows = shifted(byte_states[rows_here - (KERNEL - STRIDE) :], "ctx", 1)
    local_heads = STRIDE * channels // CHANNEL_WIDTH
    copies_n = max(1, n_ctx // local_heads)
    groups_n = n_ctx // copies_n
    head_width = STRIDE * channels // groups_n
    head_here = head_width // CHANNEL_WIDTH
    query_rows = lat_dev // copies_n
    stripe = device % copies_n

    nq = head_here
    per_t = channels // head_width
    both_local = shorten_both(byte_states, rim_rows, qk_kernel, value_kernel, per_t, nq)
    both_local = both_local.reshape(groups_n, 2 * nq, lat_dev, CHANNEL_WIDTH)
    if copies_n > 1:
        both_local = jnp.broadcast_to(
            both_local[:, None], (groups_n, copies_n, 2 * nq, lat_dev, CHANNEL_WIDTH)
        ).reshape(n_ctx, 2 * nq, lat_dev, CHANNEL_WIDTH)
    both_all = lax.all_to_all(both_local, "ctx", split_axis=0, concat_axis=0, tiled=True)
    key_all = both_all[:, :nq]
    value_all = both_all[:, nq:]
    queries = key_all.reshape(n_ctx, nq, copies_n, query_rows, CHANNEL_WIDTH)[:, :, 0]
    if copies_n > 1:
        queries = lax.dynamic_index_in_dim(
            key_all.reshape(n_ctx, nq, copies_n, query_rows, CHANNEL_WIDTH), stripe, 2, keepdims=False
        )
    query_count = n_ctx * query_rows
    query_heads = queries.transpose(1, 0, 2, 3).reshape(nq, query_count, CHANNEL_WIDTH)
    key_heads = key_all.transpose(1, 0, 2, 3).reshape(nq, lat_total, CHANNEL_WIDTH)
    value_heads = value_all.transpose(1, 0, 2, 3).reshape(nq, lat_total, CHANNEL_WIDTH)
    asking_index = (
        jnp.arange(n_ctx, dtype=jnp.int32)[:, None] * lat_dev
        + stripe * query_rows
        + jnp.arange(query_rows, dtype=jnp.int32)[None, :]
    ).reshape(query_count)
    query_seg = lax.dynamic_index_in_dim(
        block_ids.reshape(n_ctx, copies_n, query_rows), stripe, 1, keepdims=False
    ).reshape(query_count)
    lat_len = doc_length[0] // STRIDE
    sharpness_divisor = jnp.log(asking_index.astype(jnp.float32) + 2.0) / (
        math.sqrt(float(CHANNEL_WIDTH)) * math.sqrt(math.log(float(lat_total)))
    )
    block_len = min(lat_total, max(512, lat_total // 16))
    block_count = lat_total // block_len

    def attend(running, key_start):
        key_block = lax.dynamic_slice_in_dim(key_heads, key_start, block_len, 1)
        value_block = lax.dynamic_slice_in_dim(value_heads, key_start, block_len, 1)
        seg_block = lax.dynamic_slice_in_dim(block_ids, key_start, block_len, 0)
        key_pos = key_start + jnp.arange(block_len, dtype=jnp.int32)
        run_max, run_sum, run_acc = running
        raw_affinity = (
            jnp.einsum("hqd,hkd->hqk", query_heads, key_block, preferred_element_type=jnp.float32)
            * sharpness_divisor[None, :, None]
        )
        visible = (
            (seg_block[None, :] <= query_seg[:, None])
            & (key_pos[None, :] < lat_len)
            & ((key_pos[None, :] != asking_index[:, None]) | (asking_index[:, None] == 0))
        )
        new_max = jnp.maximum(
            run_max, jnp.max(jnp.where(visible[None], raw_affinity, -1e30), axis=2)
        )
        weights = jnp.where(visible[None], jnp.exp(raw_affinity - new_max[:, :, None]), 0.0)
        factor = jnp.exp(run_max - new_max)
        new_sum = run_sum * factor + jnp.sum(weights, axis=2)
        new_acc = run_acc * factor[:, :, None] + jnp.einsum(
            "hqk,hkd->hqd",
            weights.astype(jnp.bfloat16),
            value_block,
            preferred_element_type=jnp.float32,
        )
        updated = (new_max, new_sum, new_acc)
        return (updated, None)

    initial = (
        jnp.full((head_here, query_count), -1e30, jnp.float32),
        jnp.zeros((head_here, query_count), jnp.float32),
        jnp.zeros((head_here, query_count, CHANNEL_WIDTH), jnp.float32),
    )
    finals, unused = lax.scan(attend, initial, jnp.arange(block_count, dtype=jnp.int32) * block_len)
    attended = (finals[2] / finals[1][:, :, None]).astype(jnp.bfloat16)
    attended = attended.reshape(nq, n_ctx, query_rows, CHANNEL_WIDTH).transpose(1, 0, 2, 3)
    rim_out = jnp.concatenate(
        [jnp.zeros((1, nq, 2, CHANNEL_WIDTH), jnp.bfloat16), attended[:-1, :, query_rows - 2 :]], 0
    )
    outgoing = jnp.concatenate([attended, rim_out], 2)
    returned = lax.all_to_all(outgoing, "ctx", split_axis=0, concat_axis=0, tiled=True)
    returned = returned.reshape(groups_n, copies_n, nq, query_rows + 2, CHANNEL_WIDTH)
    attended_local = returned[:, :, :, :query_rows].transpose(1, 3, 0, 2, 4)
    attended_local = attended_local.reshape(lat_dev, STRIDE, channels)
    rim_latent = returned[:, copies_n - 1, :, query_rows:].transpose(2, 0, 1, 3)
    rim_latent = rim_latent.reshape(2, STRIDE, channels)
    extended = jnp.concatenate([rim_latent, attended_local], 0).astype(jnp.float32)
    prior_one = extended[1:-1]
    prior_two = extended[:-2]
    branch = jnp.zeros((lat_dev, STRIDE, channels), jnp.float32)
    for offset in range(STRIDE):
        branch = branch + prior_one[:, offset, None, :] * up_kernel[:STRIDE, offset][None]
        branch = branch + prior_two[:, offset, None, :] * up_kernel[STRIDE:, offset][None]
    branch = branch.reshape(rows_here, channels)
    byte_pos = device * rows_here + jnp.arange(rows_here, dtype=jnp.int32)
    return byte_states + jnp.where(byte_pos[:, None] < doc_length[0], branch, 0.0)


def solution(mesh):
    return jax.shard_map(
        body,
        mesh=mesh,
        in_specs=(
            P(("groups", "ctx"), "head"),
            P("groups"),
            P("groups"),
            P(None, None, "head"),
            P(None, None, "head"),
            P(None, None, "head"),
        ),
        out_specs=P(("groups", "ctx"), "head"),
        check_vma=False,
    )
```

```python
import functools
import math

import jax
import jax.numpy as jnp
from jax import lax
from jax.experimental import pallas as pl
from jax.experimental.pallas import tpu as pltpu
from jax.sharding import PartitionSpec as P

CHANNEL_WIDTH = 128
STRIDE = 4
KERNEL = 8


def shifted(x, axis, by):
    devices = lax.axis_size(axis)
    pairs = [(i, i + by) for i in range(devices) if 0 <= i + by < devices]
    return lax.ppermute(x, axis, pairs)


def shorten_kernel(x_ref, rim_ref, qk_ref, vk_ref, out_ref):
    rows, lanes = x_ref.shape
    lat = rows // STRIDE
    first_row = lax.broadcasted_iota(jnp.int32, (lat, lanes), 0) == 0
    taps = [None] * KERNEL
    for k in range(STRIDE):
        current = x_ref[pl.ds(k, lat, stride=STRIDE), :]
        earlier = pltpu.roll(current, 1, 0)
        earlier = jnp.where(first_row, rim_ref[pl.ds(k, 1), :], earlier)
        taps[k] = earlier
        taps[k + STRIDE] = current
    for which, kern_ref in enumerate((qk_ref, vk_ref)):
        for t in range(STRIDE):
            total = taps[0] * kern_ref[0, pl.ds(t, 1), :]
            for k in range(1, KERNEL):
                total = total + taps[k] * kern_ref[k, pl.ds(t, 1), :]
            out_ref[t, 0, which, 0] = total.astype(jnp.bfloat16)


def shorten_both(byte_states, rim_rows, qk_kernel, value_kernel, per_t, nq):
    rows, channels = byte_states.shape
    lat = rows // STRIDE
    lanes = CHANNEL_WIDTH
    blocks = channels // lanes
    return pl.pallas_call(
        shorten_kernel,
        grid=(blocks,),
        out_shape=jax.ShapeDtypeStruct((STRIDE, per_t, 2, nq, lat, lanes), jnp.bfloat16),
        in_specs=[
            pl.BlockSpec((rows, lanes), lambda b: (0, b)),
            pl.BlockSpec((KERNEL - STRIDE, lanes), lambda b: (0, b)),
            pl.BlockSpec((KERNEL, STRIDE, lanes), lambda b: (0, 0, b)),
            pl.BlockSpec((KERNEL, STRIDE, lanes), lambda b: (0, 0, b)),
        ],
        out_specs=pl.BlockSpec(
            (STRIDE, 1, 2, 1, lat, lanes), lambda b: (0, b // nq, 0, b % nq, 0, 0)
        ),
        cost_estimate=pl.CostEstimate(
            flops=4 * KERNEL * rows * channels,
            bytes_accessed=4 * rows * channels + 2 * KERNEL * STRIDE * channels * 4 + 2 * rows * channels * 2,
            transcendentals=0,
        ),
    )(byte_states, rim_rows, qk_kernel, value_kernel)


def up_kernel_fn(copies_n, per_t, nq, qr, lim_ref, ret_ref, x_ref, up_ref, out_ref):
    rows, lanes = x_ref.shape
    lat = rows // STRIDE
    block = pl.program_id(0)
    sub = block // nq
    q = block % nq
    row = lax.broadcasted_iota(jnp.int32, (lat, lanes), 0)
    prior_one = []
    prior_two = []
    for t in range(STRIDE):
        g = t * per_t + sub
        parts = [
            ret_ref[g * copies_n + s, pl.ds(pl.multiple_of(q * qr, qr), qr), :] for s in range(copies_n)
        ]
        att = (parts[0] if copies_n == 1 else jnp.concatenate(parts, 0)).astype(jnp.float32)
        rims = ret_ref[g * copies_n + copies_n - 1, pl.ds(nq * qr, 2 * nq), :].astype(jnp.float32)
        rim = rims[0:2]
        for other in range(1, nq):
            rim = jnp.where(q == other, rims[2 * other : 2 * other + 2], rim)
        one = pltpu.roll(att, 1, 0)
        one = jnp.where(row == 0, rim[1:2], one)
        two = pltpu.roll(att, 2, 0)
        two = jnp.where(row == 0, rim[0:1], jnp.where(row == 1, rim[1:2], two))
        prior_one.append(one)
        prior_two.append(two)
    limit = lim_ref[0]
    for s in range(STRIDE):
        total = prior_one[0] * up_ref[s, pl.ds(0, 1), :] + prior_two[0] * up_ref[s + STRIDE, pl.ds(0, 1), :]
        for t in range(1, STRIDE):
            total = total + prior_one[t] * up_ref[s, pl.ds(t, 1), :]
            total = total + prior_two[t] * up_ref[s + STRIDE, pl.ds(t, 1), :]
        here = x_ref[pl.ds(s, lat, stride=STRIDE), :]
        inside = row * STRIDE + s < limit
        out_ref[pl.ds(s, lat, stride=STRIDE), :] = here + jnp.where(inside, total, 0.0)


def up_and_mix(limit, returned, byte_states, up_kernel, copies_n, per_t, nq, qr):
    rows, channels = byte_states.shape
    lanes = CHANNEL_WIDTH
    return pl.pallas_call(
        functools.partial(up_kernel_fn, copies_n, per_t, nq, qr),
        grid=(channels // lanes,),
        out_shape=jax.ShapeDtypeStruct((rows, channels), jnp.float32),
        in_specs=[
            pl.BlockSpec(memory_space=pltpu.SMEM),
            pl.BlockSpec(returned.shape, lambda b: (0, 0, 0)),
            pl.BlockSpec((rows, lanes), lambda b: (0, b)),
            pl.BlockSpec((KERNEL, STRIDE, lanes), lambda b: (0, 0, b)),
        ],
        out_specs=pl.BlockSpec((rows, lanes), lambda b: (0, b)),
        cost_estimate=pl.CostEstimate(
            flops=4 * KERNEL * rows * channels,
            bytes_accessed=8 * rows * channels + returned.size * 2,
            transcendentals=0,
        ),
    )(limit, returned, byte_states, up_kernel)


def body(byte_states, doc_length, block_ids, qk_kernel, value_kernel, up_kernel):
    rows_here, channels = byte_states.shape
    lat_dev = rows_here // STRIDE
    n_ctx = lax.axis_size("ctx")
    device = lax.axis_index("ctx")
    lat_total = lat_dev * n_ctx
    rim_rows = shifted(byte_states[rows_here - (KERNEL - STRIDE) :], "ctx", 1)
    local_heads = STRIDE * channels // CHANNEL_WIDTH
    copies_n = max(1, n_ctx // local_heads)
    groups_n = n_ctx // copies_n
    head_width = STRIDE * channels // groups_n
    head_here = head_width // CHANNEL_WIDTH
    query_rows = lat_dev // copies_n
    stripe = device % copies_n

    nq = head_here
    per_t = channels // head_width
    both_local = shorten_both(byte_states, rim_rows, qk_kernel, value_kernel, per_t, nq)
    both_local = both_local.reshape(groups_n, 2 * nq, lat_dev, CHANNEL_WIDTH)
    if copies_n > 1:
        both_local = jnp.broadcast_to(
            both_local[:, None], (groups_n, copies_n, 2 * nq, lat_dev, CHANNEL_WIDTH)
        ).reshape(n_ctx, 2 * nq, lat_dev, CHANNEL_WIDTH)
    both_all = lax.all_to_all(both_local, "ctx", split_axis=0, concat_axis=0, tiled=True)
    key_all = both_all[:, :nq]
    value_all = both_all[:, nq:]
    queries = key_all.reshape(n_ctx, nq, copies_n, query_rows, CHANNEL_WIDTH)[:, :, 0]
    if copies_n > 1:
        queries = lax.dynamic_index_in_dim(
            key_all.reshape(n_ctx, nq, copies_n, query_rows, CHANNEL_WIDTH), stripe, 2, keepdims=False
        )
    query_count = n_ctx * query_rows
    query_heads = queries.transpose(1, 0, 2, 3).reshape(nq, query_count, CHANNEL_WIDTH)
    key_heads = key_all.transpose(1, 0, 2, 3).reshape(nq, lat_total, CHANNEL_WIDTH)
    value_heads = value_all.transpose(1, 0, 2, 3).reshape(nq, lat_total, CHANNEL_WIDTH)
    asking_index = (
        jnp.arange(n_ctx, dtype=jnp.int32)[:, None] * lat_dev
        + stripe * query_rows
        + jnp.arange(query_rows, dtype=jnp.int32)[None, :]
    ).reshape(query_count)
    query_seg = lax.dynamic_index_in_dim(
        block_ids.reshape(n_ctx, copies_n, query_rows), stripe, 1, keepdims=False
    ).reshape(query_count)
    lat_len = doc_length[0] // STRIDE
    sharpness_divisor = jnp.log(asking_index.astype(jnp.float32) + 2.0) / (
        math.sqrt(float(CHANNEL_WIDTH)) * math.sqrt(math.log(float(lat_total)))
    )
    block_len = min(lat_total, max(512, lat_total // 16))
    block_count = lat_total // block_len

    def attend(running, key_start):
        key_block = lax.dynamic_slice_in_dim(key_heads, key_start, block_len, 1)
        value_block = lax.dynamic_slice_in_dim(value_heads, key_start, block_len, 1)
        seg_block = lax.dynamic_slice_in_dim(block_ids, key_start, block_len, 0)
        key_pos = key_start + jnp.arange(block_len, dtype=jnp.int32)
        run_max, run_sum, run_acc = running
        raw_affinity = (
            jnp.einsum("hqd,hkd->hqk", query_heads, key_block, preferred_element_type=jnp.float32)
            * sharpness_divisor[None, :, None]
        )
        visible = (
            (seg_block[None, :] <= query_seg[:, None])
            & (key_pos[None, :] < lat_len)
            & ((key_pos[None, :] != asking_index[:, None]) | (asking_index[:, None] == 0))
        )
        new_max = jnp.maximum(
            run_max, jnp.max(jnp.where(visible[None], raw_affinity, -1e30), axis=2)
        )
        weights = jnp.where(visible[None], jnp.exp(raw_affinity - new_max[:, :, None]), 0.0)
        factor = jnp.exp(run_max - new_max)
        new_sum = run_sum * factor + jnp.sum(weights, axis=2)
        new_acc = run_acc * factor[:, :, None] + jnp.einsum(
            "hqk,hkd->hqd",
            weights.astype(jnp.bfloat16),
            value_block,
            preferred_element_type=jnp.float32,
        )
        updated = (new_max, new_sum, new_acc)
        return (updated, None)

    initial = (
        jnp.full((head_here, query_count), -1e30, jnp.float32),
        jnp.zeros((head_here, query_count), jnp.float32),
        jnp.zeros((head_here, query_count, CHANNEL_WIDTH), jnp.float32),
    )
    finals, unused = lax.scan(attend, initial, jnp.arange(block_count, dtype=jnp.int32) * block_len)
    attended = (finals[2] / finals[1][:, :, None]).astype(jnp.bfloat16)
    attended = attended.reshape(nq, n_ctx, query_rows, CHANNEL_WIDTH).transpose(1, 0, 2, 3)
    rim_out = jnp.concatenate(
        [jnp.zeros((1, nq, 2, CHANNEL_WIDTH), jnp.bfloat16), attended[:-1, :, query_rows - 2 :]], 0
    )
    main_rows = nq * query_rows
    used_rows = main_rows + 2 * nq
    ret_rows = -(-used_rows // 16) * 16
    outgoing = jnp.concatenate(
        [
            attended.reshape(n_ctx, main_rows, CHANNEL_WIDTH),
            rim_out.reshape(n_ctx, 2 * nq, CHANNEL_WIDTH),
            jnp.zeros((n_ctx, ret_rows - used_rows, CHANNEL_WIDTH), jnp.bfloat16),
        ],
        1,
    )
    returned = lax.all_to_all(outgoing, "ctx", split_axis=0, concat_axis=0, tiled=True)
    limit = (doc_length[0] - device * rows_here).reshape(1).astype(jnp.int32)
    return up_and_mix(limit, returned, byte_states, up_kernel, copies_n, per_t, nq, query_rows)

def solution(mesh):
    return jax.shard_map(
        body,
        mesh=mesh,
        in_specs=(
            P(("groups", "ctx"), "head"),
            P("groups"),
            P("groups"),
            P(None, None, "head"),
            P(None, None, "head"),
            P(None, None, "head"),
        ),
        out_specs=P(("groups", "ctx"), "head"),
        check_vma=False,
    )
```

```python
import functools
import math

import jax
import jax.numpy as jnp
from jax import lax
from jax.experimental import pallas as pl
from jax.experimental.pallas import tpu as pltpu
from jax.sharding import PartitionSpec as P

CHANNEL_WIDTH = 128
STRIDE = 4
KERNEL = 8


def shifted(x, axis, by):
    devices = lax.axis_size(axis)
    pairs = [(i, i + by) for i in range(devices) if 0 <= i + by < devices]
    return lax.ppermute(x, axis, pairs)


def shorten_kernel(nq, x_ref, extra_ref, qk_ref, vk_ref, out_ref):
    rows, lanes = x_ref.shape
    lat = rows // STRIDE
    block = pl.program_id(0)
    sub = block // nq
    q = block % nq
    per_t = out_ref.shape[0] // STRIDE
    first_row = lax.broadcasted_iota(jnp.int32, (lat, lanes), 0) == 0
    taps = [None] * KERNEL
    for k in range(STRIDE):
        current = x_ref[pl.ds(k, lat, stride=STRIDE), :]
        taps[k] = jnp.where(first_row, 0.0, pltpu.roll(current, 1, 0))
        taps[k + STRIDE] = current
    for which, kern_ref in enumerate((qk_ref, vk_ref)):
        slot = which * nq + q
        for t in range(STRIDE):
            total = taps[0] * kern_ref[0, pl.ds(t, 1), :]
            for k in range(1, KERNEL):
                total = total + taps[k] * kern_ref[k, pl.ds(t, 1), :]
            out_ref[t * per_t + sub, pl.ds(pl.multiple_of(slot * lat, lat), lat), :] = total.astype(
                jnp.bfloat16
            )

    @pl.when(block == 0)
    def _():
        out_ref[:, pl.ds(2 * nq * lat, extra_ref.shape[1]), :] = extra_ref[...]


def shorten_both(byte_states, extras, qk_kernel, value_kernel, groups_n, nq):
    rows, channels = byte_states.shape
    lat = rows // STRIDE
    lanes = CHANNEL_WIDTH
    blocks = channels // lanes
    kv_rows = 2 * nq * lat + extras.shape[1]
    return pl.pallas_call(
        functools.partial(shorten_kernel, nq),
        grid=(blocks,),
        out_shape=jax.ShapeDtypeStruct((groups_n, kv_rows, lanes), jnp.bfloat16),
        in_specs=[
            pl.BlockSpec((rows, lanes), lambda b: (0, b)),
            pl.BlockSpec(extras.shape, lambda b: (0, 0, 0)),
            pl.BlockSpec((KERNEL, STRIDE, lanes), lambda b: (0, 0, b)),
            pl.BlockSpec((KERNEL, STRIDE, lanes), lambda b: (0, 0, b)),
        ],
        out_specs=pl.BlockSpec((groups_n, kv_rows, lanes), lambda b: (0, 0, 0)),
        cost_estimate=pl.CostEstimate(
            flops=4 * KERNEL * rows * channels,
            bytes_accessed=4 * rows * channels + 2 * KERNEL * STRIDE * channels * 4 + 2 * rows * channels * 2,
            transcendentals=0,
        ),
    )(byte_states, extras, qk_kernel, value_kernel)


def split_hi_lo(value):
    hi = value.astype(jnp.bfloat16)
    lo = (value - hi.astype(jnp.float32)).astype(jnp.bfloat16)
    return hi, lo


def edge_terms(byte_states, qk_kernel, value_kernel, per_t, nq):
    rows, channels = byte_states.shape
    kern = jnp.stack([qk_kernel, value_kernel], 0)
    first = jnp.einsum("kc,wktc->wtc", byte_states[:STRIDE], kern[:, STRIDE:], precision=lax.Precision.HIGHEST)
    last = jnp.einsum(
        "kc,wktc->wtc", byte_states[rows - STRIDE :], kern[:, :STRIDE], precision=lax.Precision.HIGHEST
    )
    pieces = jnp.stack(split_hi_lo(first) + split_hi_lo(last), 0)
    pieces = pieces.reshape(4, 2, STRIDE, per_t, nq, CHANNEL_WIDTH).transpose(2, 3, 0, 1, 4, 5)
    pieces = pieces.reshape(STRIDE * per_t, 8 * nq, CHANNEL_WIDTH)
    pad = -(-8 * nq // 16) * 16 - 8 * nq
    return jnp.pad(pieces, ((0, 0), (0, pad), (0, 0)))


def up_kernel_fn(copies_n, per_t, nq, qr, lim_ref, ret_ref, x_ref, up_ref, out_ref):
    rows, lanes = x_ref.shape
    lat = rows // STRIDE
    block = pl.program_id(0)
    sub = block // nq
    q = block % nq
    row = lax.broadcasted_iota(jnp.int32, (lat, lanes), 0)
    prior_one = []
    prior_two = []
    for t in range(STRIDE):
        g = t * per_t + sub
        parts = [
            ret_ref[g * copies_n + s, pl.ds(pl.multiple_of(q * qr, qr), qr), :] for s in range(copies_n)
        ]
        att = (parts[0] if copies_n == 1 else jnp.concatenate(parts, 0)).astype(jnp.float32)
        rims = ret_ref[g * copies_n + copies_n - 1, pl.ds(nq * qr, 2 * nq), :].astype(jnp.float32)
        rim = rims[0:2]
        for other in range(1, nq):
            rim = jnp.where(q == other, rims[2 * other : 2 * other + 2], rim)
        one = pltpu.roll(att, 1, 0)
        one = jnp.where(row == 0, rim[1:2], one)
        two = pltpu.roll(att, 2, 0)
        two = jnp.where(row == 0, rim[0:1], jnp.where(row == 1, rim[1:2], two))
        prior_one.append(one)
        prior_two.append(two)
    limit = lim_ref[0]
    for s in range(STRIDE):
        total = prior_one[0] * up_ref[s, pl.ds(0, 1), :] + prior_two[0] * up_ref[s + STRIDE, pl.ds(0, 1), :]
        for t in range(1, STRIDE):
            total = total + prior_one[t] * up_ref[s, pl.ds(t, 1), :]
            total = total + prior_two[t] * up_ref[s + STRIDE, pl.ds(t, 1), :]
        here = x_ref[pl.ds(s, lat, stride=STRIDE), :]
        inside = row * STRIDE + s < limit
        out_ref[pl.ds(s, lat, stride=STRIDE), :] = here + jnp.where(inside, total, 0.0)


def up_and_mix(limit, returned, byte_states, up_kernel, copies_n, per_t, nq, qr):
    rows, channels = byte_states.shape
    lanes = CHANNEL_WIDTH
    return pl.pallas_call(
        functools.partial(up_kernel_fn, copies_n, per_t, nq, qr),
        grid=(channels // lanes,),
        out_shape=jax.ShapeDtypeStruct((rows, channels), jnp.float32),
        in_specs=[
            pl.BlockSpec(memory_space=pltpu.SMEM),
            pl.BlockSpec(returned.shape, lambda b: (0, 0, 0)),
            pl.BlockSpec((rows, lanes), lambda b: (0, b)),
            pl.BlockSpec((KERNEL, STRIDE, lanes), lambda b: (0, 0, b)),
        ],
        out_specs=pl.BlockSpec((rows, lanes), lambda b: (0, b)),
        cost_estimate=pl.CostEstimate(
            flops=4 * KERNEL * rows * channels,
            bytes_accessed=8 * rows * channels + returned.size * 2,
            transcendentals=0,
        ),
    )(limit, returned, byte_states, up_kernel)


def body(byte_states, doc_length, block_ids, qk_kernel, value_kernel, up_kernel):
    rows_here, channels = byte_states.shape
    lat_dev = rows_here // STRIDE
    n_ctx = lax.axis_size("ctx")
    device = lax.axis_index("ctx")
    lat_total = lat_dev * n_ctx
    local_heads = STRIDE * channels // CHANNEL_WIDTH
    copies_n = max(1, n_ctx // local_heads)
    groups_n = n_ctx // copies_n
    head_width = STRIDE * channels // groups_n
    head_here = head_width // CHANNEL_WIDTH
    query_rows = lat_dev // copies_n
    stripe = device % copies_n

    nq = head_here
    per_t = channels // head_width
    extras = edge_terms(byte_states, qk_kernel, value_kernel, per_t, nq)
    both_local = shorten_both(byte_states, extras, qk_kernel, value_kernel, groups_n, nq)
    kv_rows = both_local.shape[1]
    if copies_n > 1:
        both_local = jnp.broadcast_to(
            both_local[:, None], (groups_n, copies_n, kv_rows, CHANNEL_WIDTH)
        ).reshape(n_ctx, kv_rows, CHANNEL_WIDTH)
    both_all = lax.all_to_all(both_local, "ctx", split_axis=0, concat_axis=0, tiled=True)
    main_kv = both_all[:, : 2 * nq * lat_dev].reshape(n_ctx, 2 * nq, lat_dev, CHANNEL_WIDTH)
    edge = both_all[:, 2 * nq * lat_dev : 2 * nq * lat_dev + 8 * nq].astype(jnp.float32)
    edge = edge.reshape(n_ctx, 4, 2 * nq, CHANNEL_WIDTH)
    own_first = edge[:, 0] + edge[:, 1]
    from_before = edge[:, 2] + edge[:, 3]
    from_before = jnp.concatenate([jnp.zeros_like(from_before[:1]), from_before[:-1]], 0)
    first_rows = (own_first + from_before).astype(jnp.bfloat16)
    at_first = lax.broadcasted_iota(jnp.int32, main_kv.shape, 2) == 0
    main_kv = jnp.where(at_first, first_rows[:, :, None, :], main_kv)
    key_all = main_kv[:, :nq]
    value_all = main_kv[:, nq:]
    queries = key_all.reshape(n_ctx, nq, copies_n, query_rows, CHANNEL_WIDTH)[:, :, 0]
    if copies_n > 1:
        queries = lax.dynamic_index_in_dim(
            key_all.reshape(n_ctx, nq, copies_n, query_rows, CHANNEL_WIDTH), stripe, 2, keepdims=False
        )
    query_count = n_ctx * query_rows
    query_heads = queries.transpose(1, 0, 2, 3).reshape(nq, query_count, CHANNEL_WIDTH)
    key_heads = key_all.transpose(1, 0, 2, 3).reshape(nq, lat_total, CHANNEL_WIDTH)
    value_heads = value_all.transpose(1, 0, 2, 3).reshape(nq, lat_total, CHANNEL_WIDTH)
    asking_index = (
        jnp.arange(n_ctx, dtype=jnp.int32)[:, None] * lat_dev
        + stripe * query_rows
        + jnp.arange(query_rows, dtype=jnp.int32)[None, :]
    ).reshape(query_count)
    query_seg = lax.dynamic_index_in_dim(
        block_ids.reshape(n_ctx, copies_n, query_rows), stripe, 1, keepdims=False
    ).reshape(query_count)
    lat_len = doc_length[0] // STRIDE
    sharpness_divisor = jnp.log(asking_index.astype(jnp.float32) + 2.0) / (
        math.sqrt(float(CHANNEL_WIDTH)) * math.sqrt(math.log(float(lat_total)))
    )
    block_len = min(lat_total, max(512, lat_total // 16))
    block_count = lat_total // block_len

    def attend(running, key_start):
        key_block = lax.dynamic_slice_in_dim(key_heads, key_start, block_len, 1)
        value_block = lax.dynamic_slice_in_dim(value_heads, key_start, block_len, 1)
        seg_block = lax.dynamic_slice_in_dim(block_ids, key_start, block_len, 0)
        key_pos = key_start + jnp.arange(block_len, dtype=jnp.int32)
        run_max, run_sum, run_acc = running
        raw_affinity = (
            jnp.einsum("hqd,hkd->hqk", query_heads, key_block, preferred_element_type=jnp.float32)
            * sharpness_divisor[None, :, None]
        )
        visible = (
            (seg_block[None, :] <= query_seg[:, None])
            & (key_pos[None, :] < lat_len)
            & ((key_pos[None, :] != asking_index[:, None]) | (asking_index[:, None] == 0))
        )
        new_max = jnp.maximum(
            run_max, jnp.max(jnp.where(visible[None], raw_affinity, -1e30), axis=2)
        )
        weights = jnp.where(visible[None], jnp.exp(raw_affinity - new_max[:, :, None]), 0.0)
        factor = jnp.exp(run_max - new_max)
        new_sum = run_sum * factor + jnp.sum(weights, axis=2)
        new_acc = run_acc * factor[:, :, None] + jnp.einsum(
            "hqk,hkd->hqd",
            weights.astype(jnp.bfloat16),
            value_block,
            preferred_element_type=jnp.float32,
        )
        updated = (new_max, new_sum, new_acc)
        return (updated, None)

    initial = (
        jnp.full((head_here, query_count), -1e30, jnp.float32),
        jnp.zeros((head_here, query_count), jnp.float32),
        jnp.zeros((head_here, query_count, CHANNEL_WIDTH), jnp.float32),
    )
    finals, unused = lax.scan(attend, initial, jnp.arange(block_count, dtype=jnp.int32) * block_len)
    attended = (finals[2] / finals[1][:, :, None]).astype(jnp.bfloat16)
    attended = attended.reshape(nq, n_ctx, query_rows, CHANNEL_WIDTH).transpose(1, 0, 2, 3)
    rim_out = jnp.concatenate(
        [jnp.zeros((1, nq, 2, CHANNEL_WIDTH), jnp.bfloat16), attended[:-1, :, query_rows - 2 :]], 0
    )
    main_rows = nq * query_rows
    used_rows = main_rows + 2 * nq
    ret_rows = -(-used_rows // 16) * 16
    outgoing = jnp.concatenate(
        [
            attended.reshape(n_ctx, main_rows, CHANNEL_WIDTH),
            rim_out.reshape(n_ctx, 2 * nq, CHANNEL_WIDTH),
            jnp.zeros((n_ctx, ret_rows - used_rows, CHANNEL_WIDTH), jnp.bfloat16),
        ],
        1,
    )
    returned = lax.all_to_all(outgoing, "ctx", split_axis=0, concat_axis=0, tiled=True)
    limit = (doc_length[0] - device * rows_here).reshape(1).astype(jnp.int32)
    return up_and_mix(limit, returned, byte_states, up_kernel, copies_n, per_t, nq, query_rows)

def solution(mesh):
    return jax.shard_map(
        body,
        mesh=mesh,
        in_specs=(
            P(("groups", "ctx"), "head"),
            P("groups"),
            P("groups"),
            P(None, None, "head"),
            P(None, None, "head"),
            P(None, None, "head"),
        ),
        out_specs=P(("groups", "ctx"), "head"),
        check_vma=False,
    )
```

```python
import functools
import math

import jax
import jax.numpy as jnp
from jax import lax
from jax.experimental import pallas as pl
from jax.experimental.pallas import tpu as pltpu
from jax.sharding import PartitionSpec as P

CHANNEL_WIDTH = 128
STRIDE = 4
KERNEL = 8


def shifted(x, axis, by):
    devices = lax.axis_size(axis)
    pairs = [(i, i + by) for i in range(devices) if 0 <= i + by < devices]
    return lax.ppermute(x, axis, pairs)


def three_bf16(value):
    hi = value.astype(jnp.bfloat16)
    rest = value - hi.astype(jnp.float32)
    mid = rest.astype(jnp.bfloat16)
    lo = (rest - mid.astype(jnp.float32)).astype(jnp.bfloat16)
    return hi, mid, lo


def exact_rows(select, value):
    total = None
    for piece in three_bf16(value):
        part = jnp.dot(select, piece, preferred_element_type=jnp.float32)
        total = part if total is None else total + part
    return total


def split_pair(value):
    hi = value.astype(jnp.bfloat16)
    lo = (value - hi.astype(jnp.float32)).astype(jnp.bfloat16)
    return hi, lo


def shorten_kernel(per_t, nq, x_ref, qk_ref, vk_ref, out_ref):
    rows, channels = x_ref.shape
    lat = rows // STRIDE
    lanes = CHANNEL_WIDTH
    blocks = channels // lanes
    pick_row = lax.broadcasted_iota(jnp.int32, (rows, rows), 0)
    pick_col = lax.broadcasted_iota(jnp.int32, (rows, rows), 1)
    pick = (pick_col == (pick_row % lat) * STRIDE + pick_row // lat).astype(jnp.bfloat16)
    by_phase = exact_rows(pick, x_ref[...])
    phase = [by_phase[s * lat : (s + 1) * lat] for s in range(STRIDE)]
    first_row = lax.broadcasted_iota(jnp.int32, (lat, channels), 0) == 0
    edge_row = lax.broadcasted_iota(jnp.int32, (16, lanes), 0)
    edge = [jnp.zeros((16, lanes), jnp.float32) for _ in range(STRIDE * per_t)]
    for which, kern_ref in enumerate((qk_ref, vk_ref)):
        for t in range(STRIDE):
            own = phase[0] * kern_ref[STRIDE, pl.ds(t, 1), :]
            before = phase[0] * kern_ref[0, pl.ds(t, 1), :]
            for s in range(1, STRIDE):
                own = own + phase[s] * kern_ref[STRIDE + s, pl.ds(t, 1), :]
                before = before + phase[s] * kern_ref[s, pl.ds(t, 1), :]
            total = own + jnp.where(first_row, 0.0, pltpu.roll(before, 1, 0))
            total = total.astype(jnp.bfloat16)
            own_hi, own_lo = split_pair(own[0:1])
            next_hi, next_lo = split_pair(before[lat - 1 : lat])
            for block in range(blocks):
                lane = slice(block * lanes, (block + 1) * lanes)
                g = t * per_t + block // nq
                slot = which * nq + block % nq
                out_ref[g, pl.ds(slot * lat, lat), :] = total[:, lane]
                for e, piece in enumerate((own_hi, own_lo, next_hi, next_lo)):
                    edge[g] = jnp.where(edge_row == e * 2 * nq + slot, piece[:, lane].astype(jnp.float32), edge[g])
    for g in range(STRIDE * per_t):
        out_ref[g, pl.ds(2 * nq * lat, 16), :] = edge[g].astype(jnp.bfloat16)


def shorten_both(byte_states, qk_kernel, value_kernel, groups_n, per_t, nq):
    rows, channels = byte_states.shape
    lat = rows // STRIDE
    kv_rows = 2 * nq * lat + 16
    vmem = pl.BlockSpec(memory_space=pltpu.VMEM)
    return pl.pallas_call(
        functools.partial(shorten_kernel, per_t, nq),
        out_shape=jax.ShapeDtypeStruct((groups_n, kv_rows, CHANNEL_WIDTH), jnp.bfloat16),
        in_specs=[vmem] * 3,
        out_specs=vmem,
        cost_estimate=pl.CostEstimate(
            flops=4 * KERNEL * rows * channels + 6 * rows * rows * channels,
            bytes_accessed=4 * rows * channels + 2 * KERNEL * STRIDE * channels * 4 + 2 * rows * channels * 2,
            transcendentals=0,
        ),
    )(byte_states, qk_kernel, value_kernel)


def up_kernel_fn(copies_n, per_t, nq, qr, lim_ref, ret_ref, x_ref, up_ref, out_ref):
    rows, channels = x_ref.shape
    lat = rows // STRIDE
    lanes = CHANNEL_WIDTH
    blocks = channels // lanes
    row = lax.broadcasted_iota(jnp.int32, (lat, channels), 0)
    prior_one = []
    prior_two = []
    for t in range(STRIDE):
        att_parts = []
        rim_parts = []
        for block in range(blocks):
            g = t * per_t + block // nq
            q = block % nq
            pieces = [ret_ref[g * copies_n + s, pl.ds(q * qr, qr), :] for s in range(copies_n)]
            att_parts.append(pieces[0] if copies_n == 1 else jnp.concatenate(pieces, 0))
            rim_parts.append(ret_ref[g * copies_n + copies_n - 1, pl.ds(nq * qr + 2 * q, 2), :])
        att = jnp.concatenate(att_parts, 1).astype(jnp.float32)
        rim = jnp.concatenate(rim_parts, 1).astype(jnp.float32)
        one = jnp.where(row == 0, rim[1:2], pltpu.roll(att, 1, 0))
        two = jnp.where(row == 0, rim[0:1], jnp.where(row == 1, rim[1:2], pltpu.roll(att, 2, 0)))
        prior_one.append(one)
        prior_two.append(two)
    by_phase = []
    for s in range(STRIDE):
        total = prior_one[0] * up_ref[s, pl.ds(0, 1), :] + prior_two[0] * up_ref[s + STRIDE, pl.ds(0, 1), :]
        for t in range(1, STRIDE):
            total = total + prior_one[t] * up_ref[s, pl.ds(t, 1), :]
            total = total + prior_two[t] * up_ref[s + STRIDE, pl.ds(t, 1), :]
        by_phase.append(total)
    by_phase = jnp.concatenate(by_phase, 0)
    put_row = lax.broadcasted_iota(jnp.int32, (rows, rows), 0)
    put_col = lax.broadcasted_iota(jnp.int32, (rows, rows), 1)
    put = (put_col == (put_row % STRIDE) * lat + put_row // STRIDE).astype(jnp.bfloat16)
    branch = exact_rows(put, by_phase)
    byte_row = lax.broadcasted_iota(jnp.int32, (rows, channels), 0)
    out_ref[...] = x_ref[...] + jnp.where(byte_row < lim_ref[0], branch, 0.0)


def up_and_mix(limit, returned, byte_states, up_kernel, copies_n, per_t, nq, qr):
    rows, channels = byte_states.shape
    vmem = pl.BlockSpec(memory_space=pltpu.VMEM)
    return pl.pallas_call(
        functools.partial(up_kernel_fn, copies_n, per_t, nq, qr),
        out_shape=jax.ShapeDtypeStruct((rows, channels), jnp.float32),
        in_specs=[pl.BlockSpec(memory_space=pltpu.SMEM), vmem, vmem, vmem],
        out_specs=vmem,
        cost_estimate=pl.CostEstimate(
            flops=4 * KERNEL * rows * channels + 6 * rows * rows * channels,
            bytes_accessed=8 * rows * channels + returned.size * 2,
            transcendentals=0,
        ),
    )(limit, returned, byte_states, up_kernel)


def body(byte_states, doc_length, block_ids, qk_kernel, value_kernel, up_kernel):
    rows_here, channels = byte_states.shape
    lat_dev = rows_here // STRIDE
    n_ctx = lax.axis_size("ctx")
    device = lax.axis_index("ctx")
    lat_total = lat_dev * n_ctx
    local_heads = STRIDE * channels // CHANNEL_WIDTH
    copies_n = max(1, n_ctx // local_heads)
    groups_n = n_ctx // copies_n
    head_width = STRIDE * channels // groups_n
    head_here = head_width // CHANNEL_WIDTH
    query_rows = lat_dev // copies_n
    stripe = device % copies_n

    nq = head_here
    per_t = channels // head_width
    both_local = shorten_both(byte_states, qk_kernel, value_kernel, groups_n, per_t, nq)
    kv_rows = both_local.shape[1]
    if copies_n > 1:
        both_local = jnp.broadcast_to(
            both_local[:, None], (groups_n, copies_n, kv_rows, CHANNEL_WIDTH)
        ).reshape(n_ctx, kv_rows, CHANNEL_WIDTH)
    both_all = lax.all_to_all(both_local, "ctx", split_axis=0, concat_axis=0, tiled=True)
    main_kv = both_all[:, : 2 * nq * lat_dev].reshape(n_ctx, 2 * nq, lat_dev, CHANNEL_WIDTH)
    edge = both_all[:, 2 * nq * lat_dev : 2 * nq * lat_dev + 8 * nq].astype(jnp.float32)
    edge = edge.reshape(n_ctx, 4, 2 * nq, CHANNEL_WIDTH)
    own_first = edge[:, 0] + edge[:, 1]
    from_before = edge[:, 2] + edge[:, 3]
    from_before = jnp.concatenate([jnp.zeros_like(from_before[:1]), from_before[:-1]], 0)
    first_rows = (own_first + from_before).astype(jnp.bfloat16)
    at_first = lax.broadcasted_iota(jnp.int32, main_kv.shape, 2) == 0
    main_kv = jnp.where(at_first, first_rows[:, :, None, :], main_kv)
    key_all = main_kv[:, :nq]
    value_all = main_kv[:, nq:]
    queries = key_all.reshape(n_ctx, nq, copies_n, query_rows, CHANNEL_WIDTH)[:, :, 0]
    if copies_n > 1:
        queries = lax.dynamic_index_in_dim(
            key_all.reshape(n_ctx, nq, copies_n, query_rows, CHANNEL_WIDTH), stripe, 2, keepdims=False
        )
    query_count = n_ctx * query_rows
    query_heads = queries.transpose(1, 0, 2, 3).reshape(nq, query_count, CHANNEL_WIDTH)
    key_heads = key_all.transpose(1, 0, 2, 3).reshape(nq, lat_total, CHANNEL_WIDTH)
    value_heads = value_all.transpose(1, 0, 2, 3).reshape(nq, lat_total, CHANNEL_WIDTH)
    asking_index = (
        jnp.arange(n_ctx, dtype=jnp.int32)[:, None] * lat_dev
        + stripe * query_rows
        + jnp.arange(query_rows, dtype=jnp.int32)[None, :]
    ).reshape(query_count)
    query_seg = lax.dynamic_index_in_dim(
        block_ids.reshape(n_ctx, copies_n, query_rows), stripe, 1, keepdims=False
    ).reshape(query_count)
    lat_len = doc_length[0] // STRIDE
    sharpness_divisor = jnp.log(asking_index.astype(jnp.float32) + 2.0) / (
        math.sqrt(float(CHANNEL_WIDTH)) * math.sqrt(math.log(float(lat_total)))
    )
    block_len = min(lat_total, max(512, lat_total // 16))
    block_count = lat_total // block_len

    def attend(running, key_start):
        key_block = lax.dynamic_slice_in_dim(key_heads, key_start, block_len, 1)
        value_block = lax.dynamic_slice_in_dim(value_heads, key_start, block_len, 1)
        seg_block = lax.dynamic_slice_in_dim(block_ids, key_start, block_len, 0)
        key_pos = key_start + jnp.arange(block_len, dtype=jnp.int32)
        run_max, run_sum, run_acc = running
        raw_affinity = (
            jnp.einsum("hqd,hkd->hqk", query_heads, key_block, preferred_element_type=jnp.float32)
            * sharpness_divisor[None, :, None]
        )
        visible = (
            (seg_block[None, :] <= query_seg[:, None])
            & (key_pos[None, :] < lat_len)
            & ((key_pos[None, :] != asking_index[:, None]) | (asking_index[:, None] == 0))
        )
        new_max = jnp.maximum(
            run_max, jnp.max(jnp.where(visible[None], raw_affinity, -1e30), axis=2)
        )
        weights = jnp.where(visible[None], jnp.exp(raw_affinity - new_max[:, :, None]), 0.0)
        factor = jnp.exp(run_max - new_max)
        new_sum = run_sum * factor + jnp.sum(weights, axis=2)
        new_acc = run_acc * factor[:, :, None] + jnp.einsum(
            "hqk,hkd->hqd",
            weights.astype(jnp.bfloat16),
            value_block,
            preferred_element_type=jnp.float32,
        )
        updated = (new_max, new_sum, new_acc)
        return (updated, None)

    initial = (
        jnp.full((head_here, query_count), -1e30, jnp.float32),
        jnp.zeros((head_here, query_count), jnp.float32),
        jnp.zeros((head_here, query_count, CHANNEL_WIDTH), jnp.float32),
    )
    finals, unused = lax.scan(attend, initial, jnp.arange(block_count, dtype=jnp.int32) * block_len)
    attended = (finals[2] / finals[1][:, :, None]).astype(jnp.bfloat16)
    attended = attended.reshape(nq, n_ctx, query_rows, CHANNEL_WIDTH).transpose(1, 0, 2, 3)
    rim_out = jnp.concatenate(
        [jnp.zeros((1, nq, 2, CHANNEL_WIDTH), jnp.bfloat16), attended[:-1, :, query_rows - 2 :]], 0
    )
    main_rows = nq * query_rows
    used_rows = main_rows + 2 * nq
    ret_rows = -(-used_rows // 16) * 16
    outgoing = jnp.concatenate(
        [
            attended.reshape(n_ctx, main_rows, CHANNEL_WIDTH),
            rim_out.reshape(n_ctx, 2 * nq, CHANNEL_WIDTH),
            jnp.zeros((n_ctx, ret_rows - used_rows, CHANNEL_WIDTH), jnp.bfloat16),
        ],
        1,
    )
    returned = lax.all_to_all(outgoing, "ctx", split_axis=0, concat_axis=0, tiled=True)
    limit = (doc_length[0] - device * rows_here).reshape(1).astype(jnp.int32)
    return up_and_mix(limit, returned, byte_states, up_kernel, copies_n, per_t, nq, query_rows)

def solution(mesh):
    return jax.shard_map(
        body,
        mesh=mesh,
        in_specs=(
            P(("groups", "ctx"), "head"),
            P("groups"),
            P("groups"),
            P(None, None, "head"),
            P(None, None, "head"),
            P(None, None, "head"),
        ),
        out_specs=P(("groups", "ctx"), "head"),
        check_vma=False,
    )
```

```python
import functools
import math

import jax
import jax.numpy as jnp
from jax import lax
from jax.experimental import pallas as pl
from jax.experimental.pallas import tpu as pltpu
from jax.sharding import PartitionSpec as P

CHANNEL_WIDTH = 128
STRIDE = 4
KERNEL = 8


def shifted(x, axis, by):
    devices = lax.axis_size(axis)
    pairs = [(i, i + by) for i in range(devices) if 0 <= i + by < devices]
    return lax.ppermute(x, axis, pairs)


def three_bf16(value):
    hi = value.astype(jnp.bfloat16)
    rest = value - hi.astype(jnp.float32)
    mid = rest.astype(jnp.bfloat16)
    lo = (rest - mid.astype(jnp.float32)).astype(jnp.bfloat16)
    return hi, mid, lo


def exact_rows(select, value):
    total = None
    for piece in three_bf16(value):
        part = jnp.dot(select, piece, preferred_element_type=jnp.float32)
        total = part if total is None else total + part
    return total


def split_pair(value):
    hi = value.astype(jnp.bfloat16)
    lo = (value - hi.astype(jnp.float32)).astype(jnp.bfloat16)
    return hi, lo


def shorten_kernel(per_t, nq, x_ref, qk_ref, vk_ref, out_ref):
    rows, channels = x_ref.shape
    lat = rows // STRIDE
    lanes = CHANNEL_WIDTH
    blocks = channels // lanes
    pick_row = lax.broadcasted_iota(jnp.int32, (rows, rows), 0)
    pick_col = lax.broadcasted_iota(jnp.int32, (rows, rows), 1)
    pick = (pick_col == (pick_row % lat) * STRIDE + pick_row // lat).astype(jnp.bfloat16)
    by_phase = exact_rows(pick, x_ref[...])
    phase = [by_phase[s * lat : (s + 1) * lat] for s in range(STRIDE)]
    first_row = lax.broadcasted_iota(jnp.int32, (lat, channels), 0) == 0
    edge_row = lax.broadcasted_iota(jnp.int32, (16, lanes), 0)
    edge = [jnp.zeros((16, lanes), jnp.float32) for _ in range(STRIDE * per_t)]
    for which, kern_ref in enumerate((qk_ref, vk_ref)):
        for t in range(STRIDE):
            own = phase[0] * kern_ref[STRIDE, pl.ds(t, 1), :]
            before = phase[0] * kern_ref[0, pl.ds(t, 1), :]
            for s in range(1, STRIDE):
                own = own + phase[s] * kern_ref[STRIDE + s, pl.ds(t, 1), :]
                before = before + phase[s] * kern_ref[s, pl.ds(t, 1), :]
            total = own + jnp.where(first_row, 0.0, pltpu.roll(before, 1, 0))
            total = total.astype(jnp.bfloat16)
            own_hi, own_lo = split_pair(own[0:1])
            next_hi, next_lo = split_pair(before[lat - 1 : lat])
            for block in range(blocks):
                lane = slice(block * lanes, (block + 1) * lanes)
                g = t * per_t + block // nq
                slot = which * nq + block % nq
                out_ref[g, pl.ds(slot * lat, lat), :] = total[:, lane]
                for e, piece in enumerate((own_hi, own_lo, next_hi, next_lo)):
                    edge[g] = jnp.where(edge_row == e * 2 * nq + slot, piece[:, lane].astype(jnp.float32), edge[g])
    for g in range(STRIDE * per_t):
        out_ref[g, pl.ds(2 * nq * lat, 16), :] = edge[g].astype(jnp.bfloat16)


def shorten_both(byte_states, qk_kernel, value_kernel, groups_n, per_t, nq):
    rows, channels = byte_states.shape
    lat = rows // STRIDE
    kv_rows = 2 * nq * lat + 16
    vmem = pl.BlockSpec(memory_space=pltpu.VMEM)
    return pl.pallas_call(
        functools.partial(shorten_kernel, per_t, nq),
        out_shape=jax.ShapeDtypeStruct((groups_n, kv_rows, CHANNEL_WIDTH), jnp.bfloat16),
        in_specs=[vmem] * 3,
        out_specs=vmem,
        cost_estimate=pl.CostEstimate(
            flops=4 * KERNEL * rows * channels + 6 * rows * rows * channels,
            bytes_accessed=4 * rows * channels + 2 * KERNEL * STRIDE * channels * 4 + 2 * rows * channels * 2,
            transcendentals=0,
        ),
    )(byte_states, qk_kernel, value_kernel)


def up_kernel_fn(copies_n, per_t, nq, qr, lim_ref, ret_ref, x_ref, up_ref, out_ref):
    rows, channels = x_ref.shape
    lat = rows // STRIDE
    lanes = CHANNEL_WIDTH
    blocks = channels // lanes
    row = lax.broadcasted_iota(jnp.int32, (lat, channels), 0)
    prior_one = []
    prior_two = []
    for t in range(STRIDE):
        att_parts = []
        rim_parts = []
        for block in range(blocks):
            g = t * per_t + block // nq
            q = block % nq
            pieces = [ret_ref[g * copies_n + s, pl.ds(q * qr, qr), :] for s in range(copies_n)]
            att_parts.append(pieces[0] if copies_n == 1 else jnp.concatenate(pieces, 0))
            rim_parts.append(ret_ref[g * copies_n + copies_n - 1, pl.ds(nq * qr + 2 * q, 2), :])
        att = jnp.concatenate(att_parts, 1).astype(jnp.float32)
        rim = jnp.concatenate(rim_parts, 1).astype(jnp.float32)
        one = jnp.where(row == 0, rim[1:2], pltpu.roll(att, 1, 0))
        two = jnp.where(row == 0, rim[0:1], jnp.where(row == 1, rim[1:2], pltpu.roll(att, 2, 0)))
        prior_one.append(one)
        prior_two.append(two)
    by_phase = []
    for s in range(STRIDE):
        total = prior_one[0] * up_ref[s, pl.ds(0, 1), :] + prior_two[0] * up_ref[s + STRIDE, pl.ds(0, 1), :]
        for t in range(1, STRIDE):
            total = total + prior_one[t] * up_ref[s, pl.ds(t, 1), :]
            total = total + prior_two[t] * up_ref[s + STRIDE, pl.ds(t, 1), :]
        by_phase.append(total)
    by_phase = jnp.concatenate(by_phase, 0)
    put_row = lax.broadcasted_iota(jnp.int32, (rows, rows), 0)
    put_col = lax.broadcasted_iota(jnp.int32, (rows, rows), 1)
    put = (put_col == (put_row % STRIDE) * lat + put_row // STRIDE).astype(jnp.bfloat16)
    branch = exact_rows(put, by_phase)
    byte_row = lax.broadcasted_iota(jnp.int32, (rows, channels), 0)
    out_ref[...] = x_ref[...] + jnp.where(byte_row < lim_ref[0], branch, 0.0)


def up_and_mix(limit, returned, byte_states, up_kernel, copies_n, per_t, nq, qr):
    rows, channels = byte_states.shape
    vmem = pl.BlockSpec(memory_space=pltpu.VMEM)
    return pl.pallas_call(
        functools.partial(up_kernel_fn, copies_n, per_t, nq, qr),
        out_shape=jax.ShapeDtypeStruct((rows, channels), jnp.float32),
        in_specs=[pl.BlockSpec(memory_space=pltpu.SMEM), vmem, vmem, vmem],
        out_specs=vmem,
        cost_estimate=pl.CostEstimate(
            flops=4 * KERNEL * rows * channels + 6 * rows * rows * channels,
            bytes_accessed=8 * rows * channels + returned.size * 2,
            transcendentals=0,
        ),
    )(limit, returned, byte_states, up_kernel)


def attend_kernel(lat, qr, nq, denom, lim_ref, kv_ref, segq_ref, segk_ref, out_ref):
    n_ctx = kv_ref.shape[0]
    total = n_ctx * lat
    lanes = CHANNEL_WIDTH
    lat_len = lim_ref[0]
    qpos = lax.broadcasted_iota(jnp.int32, (total, total), 0)
    kpos = lax.broadcasted_iota(jnp.int32, (total, total), 1)
    visible = (
        (segk_ref[...] <= segq_ref[...])
        & (kpos < lat_len)
        & ((kpos != qpos) | (qpos == 0))
    )
    sharp = jnp.log(lax.broadcasted_iota(jnp.int32, (total, 1), 0).astype(jnp.float32) + 2.0) / denom
    tile_row = lax.broadcasted_iota(jnp.int32, (16, lanes), 0)
    tiles = [jnp.zeros((16, lanes), jnp.float32) for _ in range(n_ctx)]
    for q in range(nq):
        keys = jnp.concatenate([kv_ref[i, q] for i in range(n_ctx)], 0)
        values = jnp.concatenate([kv_ref[i, nq + q] for i in range(n_ctx)], 0)
        scores = lax.dot_general(
            keys, keys, (((1,), (1,)), ((), ())), preferred_element_type=jnp.float32
        ) * sharp
        scores = jnp.where(visible, scores, -1e30)
        top = jnp.max(scores, axis=1, keepdims=True)
        weights = jnp.where(visible, jnp.exp(scores - top), 0.0)
        sums = jnp.sum(weights, axis=1, keepdims=True)
        rows = jnp.dot(weights.astype(jnp.bfloat16), values, preferred_element_type=jnp.float32)
        rows = (rows / sums).astype(jnp.bfloat16)
        for d in range(n_ctx):
            out_ref[d, pl.ds(q * qr, qr), :] = rows[d * lat : (d + 1) * lat]
        wide = rows.astype(jnp.float32)
        for d in range(1, n_ctx):
            for e in range(2):
                at = d * lat - 2 + e
                tiles[d] = jnp.where(tile_row == 2 * q + e, wide[at : at + 1], tiles[d])
    for d in range(n_ctx):
        out_ref[d, pl.ds(nq * qr, 16), :] = tiles[d].astype(jnp.bfloat16)


def attend_whole(lat_len, main_kv, block_ids, nq, denom):
    n_ctx, _, lat, lanes = main_kv.shape
    total = n_ctx * lat
    vmem = pl.BlockSpec(memory_space=pltpu.VMEM)
    ret_rows = nq * lat + 16
    return pl.pallas_call(
        functools.partial(attend_kernel, lat, lat, nq, denom),
        out_shape=jax.ShapeDtypeStruct((n_ctx, ret_rows, lanes), jnp.bfloat16),
        in_specs=[pl.BlockSpec(memory_space=pltpu.SMEM), vmem, vmem, vmem],
        out_specs=vmem,
        cost_estimate=pl.CostEstimate(
            flops=4 * nq * total * total * lanes,
            bytes_accessed=main_kv.size * 2 + n_ctx * ret_rows * lanes * 2,
            transcendentals=nq * total * total,
        ),
    )(lat_len, main_kv, block_ids.reshape(total, 1), block_ids.reshape(1, total))


def body(byte_states, doc_length, block_ids, qk_kernel, value_kernel, up_kernel):
    rows_here, channels = byte_states.shape
    lat_dev = rows_here // STRIDE
    n_ctx = lax.axis_size("ctx")
    device = lax.axis_index("ctx")
    lat_total = lat_dev * n_ctx
    local_heads = STRIDE * channels // CHANNEL_WIDTH
    copies_n = max(1, n_ctx // local_heads)
    groups_n = n_ctx // copies_n
    head_width = STRIDE * channels // groups_n
    head_here = head_width // CHANNEL_WIDTH
    query_rows = lat_dev // copies_n
    stripe = device % copies_n

    nq = head_here
    per_t = channels // head_width
    both_local = shorten_both(byte_states, qk_kernel, value_kernel, groups_n, per_t, nq)
    kv_rows = both_local.shape[1]
    if copies_n > 1:
        both_local = jnp.broadcast_to(
            both_local[:, None], (groups_n, copies_n, kv_rows, CHANNEL_WIDTH)
        ).reshape(n_ctx, kv_rows, CHANNEL_WIDTH)
    both_all = lax.all_to_all(both_local, "ctx", split_axis=0, concat_axis=0, tiled=True)
    main_kv = both_all[:, : 2 * nq * lat_dev].reshape(n_ctx, 2 * nq, lat_dev, CHANNEL_WIDTH)
    edge = both_all[:, 2 * nq * lat_dev : 2 * nq * lat_dev + 8 * nq].astype(jnp.float32)
    edge = edge.reshape(n_ctx, 4, 2 * nq, CHANNEL_WIDTH)
    own_first = edge[:, 0] + edge[:, 1]
    from_before = edge[:, 2] + edge[:, 3]
    from_before = jnp.concatenate([jnp.zeros_like(from_before[:1]), from_before[:-1]], 0)
    first_rows = (own_first + from_before).astype(jnp.bfloat16)
    at_first = lax.broadcasted_iota(jnp.int32, main_kv.shape, 2) == 0
    main_kv = jnp.where(at_first, first_rows[:, :, None, :], main_kv)
    lat_len = doc_length[0] // STRIDE
    if copies_n == 1 and lat_total <= 1024 and nq <= 8 and query_rows % 16 == 0:
        denom = math.sqrt(float(CHANNEL_WIDTH)) * math.sqrt(math.log(float(lat_total)))
        outgoing = attend_whole(lat_len.reshape(1), main_kv, block_ids, nq, denom)
    else:
        outgoing = attend_scan(
            main_kv, block_ids, lat_len, n_ctx, nq, copies_n, query_rows, lat_dev, lat_total, stripe
        )
    returned = lax.all_to_all(outgoing, "ctx", split_axis=0, concat_axis=0, tiled=True)
    limit = (doc_length[0] - device * rows_here).reshape(1).astype(jnp.int32)
    return up_and_mix(limit, returned, byte_states, up_kernel, copies_n, per_t, nq, query_rows)


def attend_scan(main_kv, block_ids, lat_len, n_ctx, nq, copies_n, query_rows, lat_dev, lat_total, stripe):
    key_all = main_kv[:, :nq]
    value_all = main_kv[:, nq:]
    queries = key_all.reshape(n_ctx, nq, copies_n, query_rows, CHANNEL_WIDTH)[:, :, 0]
    if copies_n > 1:
        queries = lax.dynamic_index_in_dim(
            key_all.reshape(n_ctx, nq, copies_n, query_rows, CHANNEL_WIDTH), stripe, 2, keepdims=False
        )
    query_count = n_ctx * query_rows
    query_heads = queries.transpose(1, 0, 2, 3).reshape(nq, query_count, CHANNEL_WIDTH)
    key_heads = key_all.transpose(1, 0, 2, 3).reshape(nq, lat_total, CHANNEL_WIDTH)
    value_heads = value_all.transpose(1, 0, 2, 3).reshape(nq, lat_total, CHANNEL_WIDTH)
    asking_index = (
        jnp.arange(n_ctx, dtype=jnp.int32)[:, None] * lat_dev
        + stripe * query_rows
        + jnp.arange(query_rows, dtype=jnp.int32)[None, :]
    ).reshape(query_count)
    query_seg = lax.dynamic_index_in_dim(
        block_ids.reshape(n_ctx, copies_n, query_rows), stripe, 1, keepdims=False
    ).reshape(query_count)
    sharpness_divisor = jnp.log(asking_index.astype(jnp.float32) + 2.0) / (
        math.sqrt(float(CHANNEL_WIDTH)) * math.sqrt(math.log(float(lat_total)))
    )
    block_len = min(lat_total, max(512, lat_total // 16))
    block_count = lat_total // block_len

    def attend(running, key_start):
        key_block = lax.dynamic_slice_in_dim(key_heads, key_start, block_len, 1)
        value_block = lax.dynamic_slice_in_dim(value_heads, key_start, block_len, 1)
        seg_block = lax.dynamic_slice_in_dim(block_ids, key_start, block_len, 0)
        key_pos = key_start + jnp.arange(block_len, dtype=jnp.int32)
        run_max, run_sum, run_acc = running
        raw_affinity = (
            jnp.einsum("hqd,hkd->hqk", query_heads, key_block, preferred_element_type=jnp.float32)
            * sharpness_divisor[None, :, None]
        )
        visible = (
            (seg_block[None, :] <= query_seg[:, None])
            & (key_pos[None, :] < lat_len)
            & ((key_pos[None, :] != asking_index[:, None]) | (asking_index[:, None] == 0))
        )
        new_max = jnp.maximum(
            run_max, jnp.max(jnp.where(visible[None], raw_affinity, -1e30), axis=2)
        )
        weights = jnp.where(visible[None], jnp.exp(raw_affinity - new_max[:, :, None]), 0.0)
        factor = jnp.exp(run_max - new_max)
        new_sum = run_sum * factor + jnp.sum(weights, axis=2)
        new_acc = run_acc * factor[:, :, None] + jnp.einsum(
            "hqk,hkd->hqd",
            weights.astype(jnp.bfloat16),
            value_block,
            preferred_element_type=jnp.float32,
        )
        updated = (new_max, new_sum, new_acc)
        return (updated, None)

    initial = (
        jnp.full((nq, query_count), -1e30, jnp.float32),
        jnp.zeros((nq, query_count), jnp.float32),
        jnp.zeros((nq, query_count, CHANNEL_WIDTH), jnp.float32),
    )
    finals, unused = lax.scan(attend, initial, jnp.arange(block_count, dtype=jnp.int32) * block_len)
    attended = (finals[2] / finals[1][:, :, None]).astype(jnp.bfloat16)
    attended = attended.reshape(nq, n_ctx, query_rows, CHANNEL_WIDTH).transpose(1, 0, 2, 3)
    rim_out = jnp.concatenate(
        [jnp.zeros((1, nq, 2, CHANNEL_WIDTH), jnp.bfloat16), attended[:-1, :, query_rows - 2 :]], 0
    )
    main_rows = nq * query_rows
    used_rows = main_rows + 2 * nq
    ret_rows = -(-used_rows // 16) * 16
    outgoing = jnp.concatenate(
        [
            attended.reshape(n_ctx, main_rows, CHANNEL_WIDTH),
            rim_out.reshape(n_ctx, 2 * nq, CHANNEL_WIDTH),
            jnp.zeros((n_ctx, ret_rows - used_rows, CHANNEL_WIDTH), jnp.bfloat16),
        ],
        1,
    )
    return outgoing


def solution(mesh):
    return jax.shard_map(
        body,
        mesh=mesh,
        in_specs=(
            P(("groups", "ctx"), "head"),
            P("groups"),
            P("groups"),
            P(None, None, "head"),
            P(None, None, "head"),
            P(None, None, "head"),
        ),
        out_specs=P(("groups", "ctx"), "head"),
        check_vma=False,
    )
```

```python
import functools
import math

import jax
import jax.numpy as jnp
from jax import lax
from jax.experimental import pallas as pl
from jax.experimental.pallas import tpu as pltpu
from jax.sharding import PartitionSpec as P

CHANNEL_WIDTH = 128
STRIDE = 4
KERNEL = 8


def shifted(x, axis, by):
    devices = lax.axis_size(axis)
    pairs = [(i, i + by) for i in range(devices) if 0 <= i + by < devices]
    return lax.ppermute(x, axis, pairs)


def three_bf16(value):
    hi = value.astype(jnp.bfloat16)
    rest = value - hi.astype(jnp.float32)
    mid = rest.astype(jnp.bfloat16)
    lo = (rest - mid.astype(jnp.float32)).astype(jnp.bfloat16)
    return hi, mid, lo


def exact_rows(select, value):
    total = None
    for piece in three_bf16(value):
        part = jnp.dot(select, piece, preferred_element_type=jnp.float32)
        total = part if total is None else total + part
    return total


def split_pair(value):
    hi = value.astype(jnp.bfloat16)
    lo = (value - hi.astype(jnp.float32)).astype(jnp.bfloat16)
    return hi, lo


def shorten_kernel(per_t, nq, x_ref, qk_ref, vk_ref, out_ref):
    rows, channels = x_ref.shape
    lat = rows // STRIDE
    lanes = CHANNEL_WIDTH
    blocks = channels // lanes
    pick_row = lax.broadcasted_iota(jnp.int32, (rows, rows), 0)
    pick_col = lax.broadcasted_iota(jnp.int32, (rows, rows), 1)
    pick = (pick_col == (pick_row % lat) * STRIDE + pick_row // lat).astype(jnp.bfloat16)
    by_phase = exact_rows(pick, x_ref[...])
    phase = [by_phase[s * lat : (s + 1) * lat] for s in range(STRIDE)]
    first_row = lax.broadcasted_iota(jnp.int32, (lat, channels), 0) == 0
    edge_row = lax.broadcasted_iota(jnp.int32, (16, lanes), 0)
    edge = [jnp.zeros((16, lanes), jnp.float32) for _ in range(STRIDE * per_t)]
    for which, kern_ref in enumerate((qk_ref, vk_ref)):
        for t in range(STRIDE):
            own = phase[0] * kern_ref[STRIDE, pl.ds(t, 1), :]
            before = phase[0] * kern_ref[0, pl.ds(t, 1), :]
            for s in range(1, STRIDE):
                own = own + phase[s] * kern_ref[STRIDE + s, pl.ds(t, 1), :]
                before = before + phase[s] * kern_ref[s, pl.ds(t, 1), :]
            total = own + jnp.where(first_row, 0.0, pltpu.roll(before, 1, 0))
            total = total.astype(jnp.bfloat16)
            own_hi, own_lo = split_pair(own[0:1])
            next_hi, next_lo = split_pair(before[lat - 1 : lat])
            for block in range(blocks):
                lane = slice(block * lanes, (block + 1) * lanes)
                g = t * per_t + block // nq
                slot = which * nq + block % nq
                out_ref[g, pl.ds(slot * lat, lat), :] = total[:, lane]
                for e, piece in enumerate((own_hi, own_lo, next_hi, next_lo)):
                    edge[g] = jnp.where(edge_row == e * 2 * nq + slot, piece[:, lane].astype(jnp.float32), edge[g])
    for g in range(STRIDE * per_t):
        out_ref[g, pl.ds(2 * nq * lat, 16), :] = edge[g].astype(jnp.bfloat16)


def shorten_both(byte_states, qk_kernel, value_kernel, groups_n, per_t, nq):
    rows, channels = byte_states.shape
    lat = rows // STRIDE
    kv_rows = 2 * nq * lat + 16
    vmem = pl.BlockSpec(memory_space=pltpu.VMEM)
    return pl.pallas_call(
        functools.partial(shorten_kernel, per_t, nq),
        out_shape=jax.ShapeDtypeStruct((groups_n, kv_rows, CHANNEL_WIDTH), jnp.bfloat16),
        in_specs=[vmem] * 3,
        out_specs=vmem,
        cost_estimate=pl.CostEstimate(
            flops=4 * KERNEL * rows * channels + 6 * rows * rows * channels,
            bytes_accessed=4 * rows * channels + 2 * KERNEL * STRIDE * channels * 4 + 2 * rows * channels * 2,
            transcendentals=0,
        ),
    )(byte_states, qk_kernel, value_kernel)


def up_kernel_fn(copies_n, per_t, nq, qr, lim_ref, ret_ref, x_ref, up_ref, out_ref):
    rows, channels = x_ref.shape
    lat = rows // STRIDE
    lanes = CHANNEL_WIDTH
    blocks = channels // lanes
    row = lax.broadcasted_iota(jnp.int32, (lat, channels), 0)
    sources = ret_ref.shape[0]
    me = lim_ref[1]

    sign = lim_ref[2]

    def where(source):
        return (me - sign * source + sources) % sources

    prior_one = []
    prior_two = []
    for t in range(STRIDE):
        att_parts = []
        rim_parts = []
        for block in range(blocks):
            g = t * per_t + block // nq
            q = block % nq
            pieces = [ret_ref[where(g * copies_n + s), pl.ds(q * qr, qr), :] for s in range(copies_n)]
            att_parts.append(pieces[0] if copies_n == 1 else jnp.concatenate(pieces, 0))
            rim_parts.append(ret_ref[where(g * copies_n + copies_n - 1), pl.ds(nq * qr + 2 * q, 2), :])
        att = jnp.concatenate(att_parts, 1).astype(jnp.float32)
        rim = jnp.concatenate(rim_parts, 1).astype(jnp.float32)
        one = jnp.where(row == 0, rim[1:2], pltpu.roll(att, 1, 0))
        two = jnp.where(row == 0, rim[0:1], jnp.where(row == 1, rim[1:2], pltpu.roll(att, 2, 0)))
        prior_one.append(one)
        prior_two.append(two)
    by_phase = []
    for s in range(STRIDE):
        total = prior_one[0] * up_ref[s, pl.ds(0, 1), :] + prior_two[0] * up_ref[s + STRIDE, pl.ds(0, 1), :]
        for t in range(1, STRIDE):
            total = total + prior_one[t] * up_ref[s, pl.ds(t, 1), :]
            total = total + prior_two[t] * up_ref[s + STRIDE, pl.ds(t, 1), :]
        by_phase.append(total)
    by_phase = jnp.concatenate(by_phase, 0)
    put_row = lax.broadcasted_iota(jnp.int32, (rows, rows), 0)
    put_col = lax.broadcasted_iota(jnp.int32, (rows, rows), 1)
    put = (put_col == (put_row % STRIDE) * lat + put_row // STRIDE).astype(jnp.bfloat16)
    branch = exact_rows(put, by_phase)
    byte_row = lax.broadcasted_iota(jnp.int32, (rows, channels), 0)
    out_ref[...] = x_ref[...] + jnp.where(byte_row < lim_ref[0], branch, 0.0)


def up_and_mix(limit, returned, byte_states, up_kernel, copies_n, per_t, nq, qr):
    rows, channels = byte_states.shape
    vmem = pl.BlockSpec(memory_space=pltpu.VMEM)
    return pl.pallas_call(
        functools.partial(up_kernel_fn, copies_n, per_t, nq, qr),
        out_shape=jax.ShapeDtypeStruct((rows, channels), jnp.float32),
        in_specs=[pl.BlockSpec(memory_space=pltpu.SMEM), vmem, vmem, vmem],
        out_specs=vmem,
        cost_estimate=pl.CostEstimate(
            flops=4 * KERNEL * rows * channels + 6 * rows * rows * channels,
            bytes_accessed=8 * rows * channels + returned.size * 2,
            transcendentals=0,
        ),
    )(limit, returned, byte_states, up_kernel)


def body(byte_states, doc_length, block_ids, qk_kernel, value_kernel, up_kernel):
    rows_here, channels = byte_states.shape
    lat_dev = rows_here // STRIDE
    n_ctx = lax.axis_size("ctx")
    device = lax.axis_index("ctx")
    lat_total = lat_dev * n_ctx
    local_heads = STRIDE * channels // CHANNEL_WIDTH
    copies_n = max(1, n_ctx // local_heads)
    groups_n = n_ctx // copies_n
    head_width = STRIDE * channels // groups_n
    head_here = head_width // CHANNEL_WIDTH
    query_rows = lat_dev // copies_n
    stripe = device % copies_n

    nq = head_here
    per_t = channels // head_width
    both_local = shorten_both(byte_states, qk_kernel, value_kernel, groups_n, per_t, nq)
    kv_rows = both_local.shape[1]
    if copies_n > 1:
        both_local = jnp.broadcast_to(
            both_local[:, None], (groups_n, copies_n, kv_rows, CHANNEL_WIDTH)
        ).reshape(n_ctx, kv_rows, CHANNEL_WIDTH)
    both_all = lax.all_to_all(both_local, "ctx", split_axis=0, concat_axis=0, tiled=True)
    main_kv = both_all[:, : 2 * nq * lat_dev].reshape(n_ctx, 2 * nq, lat_dev, CHANNEL_WIDTH)
    edge = both_all[:, 2 * nq * lat_dev : 2 * nq * lat_dev + 8 * nq].astype(jnp.float32)
    edge = edge.reshape(n_ctx, 4, 2 * nq, CHANNEL_WIDTH)
    own_first = edge[:, 0] + edge[:, 1]
    from_before = edge[:, 2] + edge[:, 3]
    from_before = jnp.concatenate([jnp.zeros_like(from_before[:1]), from_before[:-1]], 0)
    first_rows = (own_first + from_before).astype(jnp.bfloat16)
    at_first = lax.broadcasted_iota(jnp.int32, main_kv.shape, 2) == 0
    main_kv = jnp.where(at_first, first_rows[:, :, None, :], main_kv)
    key_all = main_kv[:, :nq]
    value_all = main_kv[:, nq:]
    queries = key_all.reshape(n_ctx, nq, copies_n, query_rows, CHANNEL_WIDTH)[:, :, 0]
    if copies_n > 1:
        queries = lax.dynamic_index_in_dim(
            key_all.reshape(n_ctx, nq, copies_n, query_rows, CHANNEL_WIDTH), stripe, 2, keepdims=False
        )
    query_count = n_ctx * query_rows
    query_heads = queries.transpose(1, 0, 2, 3).reshape(nq, query_count, CHANNEL_WIDTH)
    key_heads = key_all.transpose(1, 0, 2, 3).reshape(nq, lat_total, CHANNEL_WIDTH)
    value_heads = value_all.transpose(1, 0, 2, 3).reshape(nq, lat_total, CHANNEL_WIDTH)
    asking_index = (
        jnp.arange(n_ctx, dtype=jnp.int32)[:, None] * lat_dev
        + stripe * query_rows
        + jnp.arange(query_rows, dtype=jnp.int32)[None, :]
    ).reshape(query_count)
    query_seg = lax.dynamic_index_in_dim(
        block_ids.reshape(n_ctx, copies_n, query_rows), stripe, 1, keepdims=False
    ).reshape(query_count)
    lat_len = doc_length[0] // STRIDE
    sharpness_divisor = jnp.log(asking_index.astype(jnp.float32) + 2.0) / (
        math.sqrt(float(CHANNEL_WIDTH)) * math.sqrt(math.log(float(lat_total)))
    )
    block_len = min(lat_total, max(512, lat_total // 16))
    block_count = lat_total // block_len

    def attend(running, key_start):
        key_block = lax.dynamic_slice_in_dim(key_heads, key_start, block_len, 1)
        value_block = lax.dynamic_slice_in_dim(value_heads, key_start, block_len, 1)
        seg_block = lax.dynamic_slice_in_dim(block_ids, key_start, block_len, 0)
        key_pos = key_start + jnp.arange(block_len, dtype=jnp.int32)
        run_max, run_sum, run_acc = running
        raw_affinity = (
            jnp.einsum("hqd,hkd->hqk", query_heads, key_block, preferred_element_type=jnp.float32)
            * sharpness_divisor[None, :, None]
        )
        visible = (
            (seg_block[None, :] <= query_seg[:, None])
            & (key_pos[None, :] < lat_len)
            & ((key_pos[None, :] != asking_index[:, None]) | (asking_index[:, None] == 0))
        )
        new_max = jnp.maximum(
            run_max, jnp.max(jnp.where(visible[None], raw_affinity, -1e30), axis=2)
        )
        weights = jnp.where(visible[None], jnp.exp(raw_affinity - new_max[:, :, None]), 0.0)
        factor = jnp.exp(run_max - new_max)
        new_sum = run_sum * factor + jnp.sum(weights, axis=2)
        new_acc = run_acc * factor[:, :, None] + jnp.einsum(
            "hqk,hkd->hqd",
            weights.astype(jnp.bfloat16),
            value_block,
            preferred_element_type=jnp.float32,
        )
        updated = (new_max, new_sum, new_acc)
        return (updated, None)

    initial = (
        jnp.full((head_here, query_count), -1e30, jnp.float32),
        jnp.zeros((head_here, query_count), jnp.float32),
        jnp.zeros((head_here, query_count, CHANNEL_WIDTH), jnp.float32),
    )
    finals, unused = lax.scan(attend, initial, jnp.arange(block_count, dtype=jnp.int32) * block_len)
    attended = (finals[2] / finals[1][:, :, None]).astype(jnp.bfloat16)
    attended = attended.reshape(nq, n_ctx, query_rows, CHANNEL_WIDTH).transpose(1, 0, 2, 3)
    rim_out = jnp.concatenate(
        [jnp.zeros((1, nq, 2, CHANNEL_WIDTH), jnp.bfloat16), attended[:-1, :, query_rows - 2 :]], 0
    )
    main_rows = nq * query_rows
    used_rows = main_rows + 2 * nq
    ret_rows = -(-used_rows // 16) * 16
    outgoing = jnp.concatenate(
        [
            attended.reshape(n_ctx, main_rows, CHANNEL_WIDTH),
            rim_out.reshape(n_ctx, 2 * nq, CHANNEL_WIDTH),
            jnp.zeros((n_ctx, ret_rows - used_rows, CHANNEL_WIDTH), jnp.bfloat16),
        ],
        1,
    )
    if n_ctx <= 8:
        pieces = [lax.dynamic_index_in_dim(outgoing, device, 0, keepdims=False)]
        for s in range(1, n_ctx):
            send = lax.dynamic_index_in_dim(outgoing, (device + s) % n_ctx, 0, keepdims=False)
            pieces.append(lax.ppermute(send, "ctx", [(i, (i + s) % n_ctx) for i in range(n_ctx)]))
        returned = jnp.stack(pieces, 0)
        shifted_by, sign = 1, 1
    else:
        returned = lax.all_to_all(outgoing, "ctx", split_axis=0, concat_axis=0, tiled=True)
        shifted_by, sign = 0, -1
    info = jnp.stack([doc_length[0] - device * rows_here, device * shifted_by, jnp.int32(sign)]).astype(jnp.int32)
    return up_and_mix(info, returned, byte_states, up_kernel, copies_n, per_t, nq, query_rows)

def solution(mesh):
    return jax.shard_map(
        body,
        mesh=mesh,
        in_specs=(
            P(("groups", "ctx"), "head"),
            P("groups"),
            P("groups"),
            P(None, None, "head"),
            P(None, None, "head"),
            P(None, None, "head"),
        ),
        out_specs=P(("groups", "ctx"), "head"),
        check_vma=False,
    )
```

```python
import functools
import math

import jax
import jax.numpy as jnp
from jax import lax
from jax.experimental import pallas as pl
from jax.experimental.pallas import tpu as pltpu
from jax.sharding import PartitionSpec as P

CHANNEL_WIDTH = 128
STRIDE = 4
KERNEL = 8


def shifted(x, axis, by):
    devices = lax.axis_size(axis)
    pairs = [(i, i + by) for i in range(devices) if 0 <= i + by < devices]
    return lax.ppermute(x, axis, pairs)


def three_bf16(value):
    hi = value.astype(jnp.bfloat16)
    rest = value - hi.astype(jnp.float32)
    mid = rest.astype(jnp.bfloat16)
    lo = (rest - mid.astype(jnp.float32)).astype(jnp.bfloat16)
    return hi, mid, lo


def exact_rows(select, value):
    total = None
    for piece in three_bf16(value):
        part = jnp.dot(select, piece, preferred_element_type=jnp.float32)
        total = part if total is None else total + part
    return total


def split_pair(value):
    hi = value.astype(jnp.bfloat16)
    lo = (value - hi.astype(jnp.float32)).astype(jnp.bfloat16)
    return hi, lo


def shorten_kernel(per_t, nq, x_ref, qk_ref, vk_ref, out_ref):
    rows, channels = x_ref.shape
    lat = rows // STRIDE
    lanes = CHANNEL_WIDTH
    blocks = channels // lanes
    pick_row = lax.broadcasted_iota(jnp.int32, (rows, rows), 0)
    pick_col = lax.broadcasted_iota(jnp.int32, (rows, rows), 1)
    pick = (pick_col == (pick_row % lat) * STRIDE + pick_row // lat).astype(jnp.bfloat16)
    by_phase = exact_rows(pick, x_ref[...])
    phase = [by_phase[s * lat : (s + 1) * lat] for s in range(STRIDE)]
    first_row = lax.broadcasted_iota(jnp.int32, (lat, channels), 0) == 0
    edge_row = lax.broadcasted_iota(jnp.int32, (16, lanes), 0)
    edge = [jnp.zeros((16, lanes), jnp.float32) for _ in range(STRIDE * per_t)]
    for which, kern_ref in enumerate((qk_ref, vk_ref)):
        for t in range(STRIDE):
            own = phase[0] * kern_ref[STRIDE, pl.ds(t, 1), :]
            before = phase[0] * kern_ref[0, pl.ds(t, 1), :]
            for s in range(1, STRIDE):
                own = own + phase[s] * kern_ref[STRIDE + s, pl.ds(t, 1), :]
                before = before + phase[s] * kern_ref[s, pl.ds(t, 1), :]
            total = own + jnp.where(first_row, 0.0, pltpu.roll(before, 1, 0))
            total = total.astype(jnp.bfloat16)
            own_hi, own_lo = split_pair(own[0:1])
            next_hi, next_lo = split_pair(before[lat - 1 : lat])
            for block in range(blocks):
                lane = slice(block * lanes, (block + 1) * lanes)
                g = t * per_t + block // nq
                slot = which * nq + block % nq
                out_ref[g, pl.ds(slot * lat, lat), :] = total[:, lane]
                for e, piece in enumerate((own_hi, own_lo, next_hi, next_lo)):
                    edge[g] = jnp.where(edge_row == e * 2 * nq + slot, piece[:, lane].astype(jnp.float32), edge[g])
    for g in range(STRIDE * per_t):
        out_ref[g, pl.ds(2 * nq * lat, 16), :] = edge[g].astype(jnp.bfloat16)


def shorten_both(byte_states, qk_kernel, value_kernel, groups_n, per_t, nq):
    rows, channels = byte_states.shape
    lat = rows // STRIDE
    kv_rows = 2 * nq * lat + 16
    vmem = pl.BlockSpec(memory_space=pltpu.VMEM)
    return pl.pallas_call(
        functools.partial(shorten_kernel, per_t, nq),
        out_shape=jax.ShapeDtypeStruct((groups_n, kv_rows, CHANNEL_WIDTH), jnp.bfloat16),
        in_specs=[vmem] * 3,
        out_specs=vmem,
        cost_estimate=pl.CostEstimate(
            flops=4 * KERNEL * rows * channels + 6 * rows * rows * channels,
            bytes_accessed=4 * rows * channels + 2 * KERNEL * STRIDE * channels * 4 + 2 * rows * channels * 2,
            transcendentals=0,
        ),
    )(byte_states, qk_kernel, value_kernel)


def up_kernel_fn(copies_n, per_t, nq, qr, lim_ref, ret_ref, x_ref, up_ref, out_ref):
    rows, channels = x_ref.shape
    lat = rows // STRIDE
    lanes = CHANNEL_WIDTH
    blocks = channels // lanes
    wide = lat + 16
    pick_row = lax.broadcasted_iota(jnp.int32, (rows, wide), 0)
    pick_col = lax.broadcasted_iota(jnp.int32, (rows, wide), 1)
    latent = pick_row // STRIDE
    col_one = jnp.where(latent >= 1, latent - 1, lat + 1)
    col_two = jnp.where(latent >= 2, latent - 2, lat + latent)
    take_one = jnp.where(pick_col == col_one, 1.0, 0.0).astype(jnp.bfloat16)
    take_two = jnp.where(pick_col == col_two, 1.0, 0.0).astype(jnp.bfloat16)
    phase_row = lax.broadcasted_iota(jnp.int32, (8, channels), 0) % STRIDE
    branch = None
    for t in range(STRIDE):
        att_parts = []
        rim_parts = []
        for block in range(blocks):
            g = t * per_t + block // nq
            q = block % nq
            pieces = [ret_ref[g * copies_n + s, pl.ds(q * qr, qr), :] for s in range(copies_n)]
            att_parts.append(pieces[0] if copies_n == 1 else jnp.concatenate(pieces, 0))
            rim_parts.append(ret_ref[g * copies_n + copies_n - 1, pl.ds(nq * qr + 2 * q, 2), :])
        att = jnp.concatenate(att_parts, 1).astype(jnp.float32)
        rim = jnp.concatenate(rim_parts, 1).astype(jnp.float32)
        extended = jnp.concatenate([att, rim, jnp.zeros((14, channels), jnp.float32)], 0).astype(jnp.bfloat16)
        one = jnp.dot(take_one, extended, preferred_element_type=jnp.float32)
        two = jnp.dot(take_two, extended, preferred_element_type=jnp.float32)
        w_one = up_ref[0, pl.ds(t, 1), :]
        w_two = up_ref[STRIDE, pl.ds(t, 1), :]
        for s in range(1, STRIDE):
            w_one = jnp.where(phase_row == s, up_ref[s, pl.ds(t, 1), :], w_one)
            w_two = jnp.where(phase_row == s, up_ref[s + STRIDE, pl.ds(t, 1), :], w_two)
        term = one.reshape(rows // 8, 8, channels) * w_one[None] + two.reshape(rows // 8, 8, channels) * w_two[None]
        branch = term if branch is None else branch + term
    branch = branch.reshape(rows, channels)
    byte_row = lax.broadcasted_iota(jnp.int32, (rows, channels), 0)
    out_ref[...] = x_ref[...] + jnp.where(byte_row < lim_ref[0], branch, 0.0)


def up_and_mix(limit, returned, byte_states, up_kernel, copies_n, per_t, nq, qr):
    rows, channels = byte_states.shape
    vmem = pl.BlockSpec(memory_space=pltpu.VMEM)
    return pl.pallas_call(
        functools.partial(up_kernel_fn, copies_n, per_t, nq, qr),
        out_shape=jax.ShapeDtypeStruct((rows, channels), jnp.float32),
        in_specs=[pl.BlockSpec(memory_space=pltpu.SMEM), vmem, vmem, vmem],
        out_specs=vmem,
        cost_estimate=pl.CostEstimate(
            flops=4 * KERNEL * rows * channels + 6 * rows * rows * channels,
            bytes_accessed=8 * rows * channels + returned.size * 2,
            transcendentals=0,
        ),
    )(limit, returned, byte_states, up_kernel)


def body(byte_states, doc_length, block_ids, qk_kernel, value_kernel, up_kernel):
    rows_here, channels = byte_states.shape
    lat_dev = rows_here // STRIDE
    n_ctx = lax.axis_size("ctx")
    device = lax.axis_index("ctx")
    lat_total = lat_dev * n_ctx
    local_heads = STRIDE * channels // CHANNEL_WIDTH
    copies_n = max(1, n_ctx // local_heads)
    groups_n = n_ctx // copies_n
    head_width = STRIDE * channels // groups_n
    head_here = head_width // CHANNEL_WIDTH
    query_rows = lat_dev // copies_n
    stripe = device % copies_n

    nq = head_here
    per_t = channels // head_width
    both_local = shorten_both(byte_states, qk_kernel, value_kernel, groups_n, per_t, nq)
    kv_rows = both_local.shape[1]
    if copies_n > 1:
        both_local = jnp.broadcast_to(
            both_local[:, None], (groups_n, copies_n, kv_rows, CHANNEL_WIDTH)
        ).reshape(n_ctx, kv_rows, CHANNEL_WIDTH)
    both_all = lax.all_to_all(both_local, "ctx", split_axis=0, concat_axis=0, tiled=True)
    main_kv = both_all[:, : 2 * nq * lat_dev].reshape(n_ctx, 2 * nq, lat_dev, CHANNEL_WIDTH)
    edge = both_all[:, 2 * nq * lat_dev : 2 * nq * lat_dev + 8 * nq].astype(jnp.float32)
    edge = edge.reshape(n_ctx, 4, 2 * nq, CHANNEL_WIDTH)
    own_first = edge[:, 0] + edge[:, 1]
    from_before = edge[:, 2] + edge[:, 3]
    from_before = jnp.concatenate([jnp.zeros_like(from_before[:1]), from_before[:-1]], 0)
    first_rows = (own_first + from_before).astype(jnp.bfloat16)
    at_first = lax.broadcasted_iota(jnp.int32, main_kv.shape, 2) == 0
    main_kv = jnp.where(at_first, first_rows[:, :, None, :], main_kv)
    key_all = main_kv[:, :nq]
    value_all = main_kv[:, nq:]
    queries = key_all.reshape(n_ctx, nq, copies_n, query_rows, CHANNEL_WIDTH)[:, :, 0]
    if copies_n > 1:
        queries = lax.dynamic_index_in_dim(
            key_all.reshape(n_ctx, nq, copies_n, query_rows, CHANNEL_WIDTH), stripe, 2, keepdims=False
        )
    query_count = n_ctx * query_rows
    query_heads = queries.transpose(1, 0, 2, 3).reshape(nq, query_count, CHANNEL_WIDTH)
    key_heads = key_all.transpose(1, 0, 2, 3).reshape(nq, lat_total, CHANNEL_WIDTH)
    value_heads = value_all.transpose(1, 0, 2, 3).reshape(nq, lat_total, CHANNEL_WIDTH)
    asking_index = (
        jnp.arange(n_ctx, dtype=jnp.int32)[:, None] * lat_dev
        + stripe * query_rows
        + jnp.arange(query_rows, dtype=jnp.int32)[None, :]
    ).reshape(query_count)
    query_seg = lax.dynamic_index_in_dim(
        block_ids.reshape(n_ctx, copies_n, query_rows), stripe, 1, keepdims=False
    ).reshape(query_count)
    lat_len = doc_length[0] // STRIDE
    sharpness_divisor = jnp.log(asking_index.astype(jnp.float32) + 2.0) / (
        math.sqrt(float(CHANNEL_WIDTH)) * math.sqrt(math.log(float(lat_total)))
    )
    block_len = min(lat_total, max(512, lat_total // 16))
    block_count = lat_total // block_len

    def attend(running, key_start):
        key_block = lax.dynamic_slice_in_dim(key_heads, key_start, block_len, 1)
        value_block = lax.dynamic_slice_in_dim(value_heads, key_start, block_len, 1)
        seg_block = lax.dynamic_slice_in_dim(block_ids, key_start, block_len, 0)
        key_pos = key_start + jnp.arange(block_len, dtype=jnp.int32)
        run_max, run_sum, run_acc = running
        raw_affinity = (
            jnp.einsum("hqd,hkd->hqk", query_heads, key_block, preferred_element_type=jnp.float32)
            * sharpness_divisor[None, :, None]
        )
        visible = (
            (seg_block[None, :] <= query_seg[:, None])
            & (key_pos[None, :] < lat_len)
            & ((key_pos[None, :] != asking_index[:, None]) | (asking_index[:, None] == 0))
        )
        new_max = jnp.maximum(
            run_max, jnp.max(jnp.where(visible[None], raw_affinity, -1e30), axis=2)
        )
        weights = jnp.where(visible[None], jnp.exp(raw_affinity - new_max[:, :, None]), 0.0)
        factor = jnp.exp(run_max - new_max)
        new_sum = run_sum * factor + jnp.sum(weights, axis=2)
        new_acc = run_acc * factor[:, :, None] + jnp.einsum(
            "hqk,hkd->hqd",
            weights.astype(jnp.bfloat16),
            value_block,
            preferred_element_type=jnp.float32,
        )
        updated = (new_max, new_sum, new_acc)
        return (updated, None)

    initial = (
        jnp.full((head_here, query_count), -1e30, jnp.float32),
        jnp.zeros((head_here, query_count), jnp.float32),
        jnp.zeros((head_here, query_count, CHANNEL_WIDTH), jnp.float32),
    )
    finals, unused = lax.scan(attend, initial, jnp.arange(block_count, dtype=jnp.int32) * block_len)
    attended = (finals[2] / finals[1][:, :, None]).astype(jnp.bfloat16)
    attended = attended.reshape(nq, n_ctx, query_rows, CHANNEL_WIDTH).transpose(1, 0, 2, 3)
    rim_out = jnp.concatenate(
        [jnp.zeros((1, nq, 2, CHANNEL_WIDTH), jnp.bfloat16), attended[:-1, :, query_rows - 2 :]], 0
    )
    main_rows = nq * query_rows
    used_rows = main_rows + 2 * nq
    ret_rows = -(-used_rows // 16) * 16
    outgoing = jnp.concatenate(
        [
            attended.reshape(n_ctx, main_rows, CHANNEL_WIDTH),
            rim_out.reshape(n_ctx, 2 * nq, CHANNEL_WIDTH),
            jnp.zeros((n_ctx, ret_rows - used_rows, CHANNEL_WIDTH), jnp.bfloat16),
        ],
        1,
    )
    returned = lax.all_to_all(outgoing, "ctx", split_axis=0, concat_axis=0, tiled=True)
    limit = (doc_length[0] - device * rows_here).reshape(1).astype(jnp.int32)
    return up_and_mix(limit, returned, byte_states, up_kernel, copies_n, per_t, nq, query_rows)

def solution(mesh):
    return jax.shard_map(
        body,
        mesh=mesh,
        in_specs=(
            P(("groups", "ctx"), "head"),
            P("groups"),
            P("groups"),
            P(None, None, "head"),
            P(None, None, "head"),
            P(None, None, "head"),
        ),
        out_specs=P(("groups", "ctx"), "head"),
        check_vma=False,
    )
```

```python
import functools
import math

import jax
import jax.numpy as jnp
from jax import lax
from jax.experimental import pallas as pl
from jax.experimental.pallas import tpu as pltpu
from jax.sharding import PartitionSpec as P

CHANNEL_WIDTH = 128
STRIDE = 4
KERNEL = 8


def shifted(x, axis, by):
    devices = lax.axis_size(axis)
    pairs = [(i, i + by) for i in range(devices) if 0 <= i + by < devices]
    return lax.ppermute(x, axis, pairs)


def three_bf16(value):
    hi = value.astype(jnp.bfloat16)
    rest = value - hi.astype(jnp.float32)
    mid = rest.astype(jnp.bfloat16)
    lo = (rest - mid.astype(jnp.float32)).astype(jnp.bfloat16)
    return hi, mid, lo


def exact_rows(select, value):
    total = None
    for piece in three_bf16(value):
        part = jnp.dot(select, piece, preferred_element_type=jnp.float32)
        total = part if total is None else total + part
    return total


def split_pair(value):
    hi = value.astype(jnp.bfloat16)
    lo = (value - hi.astype(jnp.float32)).astype(jnp.bfloat16)
    return hi, lo


def shorten_kernel(per_t, nq, x_ref, qk_ref, vk_ref, out_ref):
    rows, channels = x_ref.shape
    lat = rows // STRIDE
    lanes = CHANNEL_WIDTH
    blocks = channels // lanes
    pick_row = lax.broadcasted_iota(jnp.int32, (rows, rows), 0)
    pick_col = lax.broadcasted_iota(jnp.int32, (rows, rows), 1)
    pick = (pick_col == (pick_row % lat) * STRIDE + pick_row // lat).astype(jnp.bfloat16)
    by_phase = exact_rows(pick, x_ref[...])
    phase = [by_phase[s * lat : (s + 1) * lat] for s in range(STRIDE)]
    first_row = lax.broadcasted_iota(jnp.int32, (lat, channels), 0) == 0
    edge_row = lax.broadcasted_iota(jnp.int32, (16, lanes), 0)
    edge = [jnp.zeros((16, lanes), jnp.float32) for _ in range(STRIDE * per_t)]
    for which, kern_ref in enumerate((qk_ref, vk_ref)):
        for t in range(STRIDE):
            own = phase[0] * kern_ref[STRIDE, pl.ds(t, 1), :]
            before = phase[0] * kern_ref[0, pl.ds(t, 1), :]
            for s in range(1, STRIDE):
                own = own + phase[s] * kern_ref[STRIDE + s, pl.ds(t, 1), :]
                before = before + phase[s] * kern_ref[s, pl.ds(t, 1), :]
            total = own + jnp.where(first_row, 0.0, pltpu.roll(before, 1, 0))
            total = total.astype(jnp.bfloat16)
            own_hi, own_lo = split_pair(own[0:1])
            next_hi, next_lo = split_pair(before[lat - 1 : lat])
            for block in range(blocks):
                lane = slice(block * lanes, (block + 1) * lanes)
                g = t * per_t + block // nq
                slot = which * nq + block % nq
                out_ref[g, pl.ds(slot * lat, lat), :] = total[:, lane]
                for e, piece in enumerate((own_hi, own_lo, next_hi, next_lo)):
                    edge[g] = jnp.where(edge_row == e * 2 * nq + slot, piece[:, lane].astype(jnp.float32), edge[g])
    for g in range(STRIDE * per_t):
        out_ref[g, pl.ds(2 * nq * lat, 16), :] = edge[g].astype(jnp.bfloat16)


def shorten_both(byte_states, qk_kernel, value_kernel, groups_n, per_t, nq):
    rows, channels = byte_states.shape
    lat = rows // STRIDE
    kv_rows = 2 * nq * lat + 16
    vmem = pl.BlockSpec(memory_space=pltpu.VMEM)
    return pl.pallas_call(
        functools.partial(shorten_kernel, per_t, nq),
        out_shape=jax.ShapeDtypeStruct((groups_n, kv_rows, CHANNEL_WIDTH), jnp.bfloat16),
        in_specs=[vmem] * 3,
        out_specs=vmem,
        cost_estimate=pl.CostEstimate(
            flops=4 * KERNEL * rows * channels + 6 * rows * rows * channels,
            bytes_accessed=4 * rows * channels + 2 * KERNEL * STRIDE * channels * 4 + 2 * rows * channels * 2,
            transcendentals=0,
        ),
    )(byte_states, qk_kernel, value_kernel)


def up_kernel_fn(copies_n, per_t, nq, qr, lat, lim_ref, ret_ref, x_ref, up_ref, out_ref):
    rows, channels = x_ref.shape
    lanes = CHANNEL_WIDTH
    blocks = channels // lanes
    first = pl.program_id(0) * rows
    wide = lat + 16
    pick_row = lax.broadcasted_iota(jnp.int32, (rows, wide), 0) + first
    pick_col = lax.broadcasted_iota(jnp.int32, (rows, wide), 1)
    latent = pick_row // STRIDE
    col_one = jnp.where(latent >= 1, latent - 1, lat + 1)
    col_two = jnp.where(latent >= 2, latent - 2, lat + latent)
    take_one = jnp.where(pick_col == col_one, 1.0, 0.0).astype(jnp.bfloat16)
    take_two = jnp.where(pick_col == col_two, 1.0, 0.0).astype(jnp.bfloat16)
    phase_row = lax.broadcasted_iota(jnp.int32, (8, channels), 0) % STRIDE
    branch = None
    for t in range(STRIDE):
        att_parts = []
        rim_parts = []
        for block in range(blocks):
            g = t * per_t + block // nq
            q = block % nq
            pieces = [ret_ref[g * copies_n + s, pl.ds(q * qr, qr), :] for s in range(copies_n)]
            att_parts.append(pieces[0] if copies_n == 1 else jnp.concatenate(pieces, 0))
            rim_parts.append(ret_ref[g * copies_n + copies_n - 1, pl.ds(nq * qr + 2 * q, 2), :])
        att = jnp.concatenate(att_parts, 1).astype(jnp.float32)
        rim = jnp.concatenate(rim_parts, 1).astype(jnp.float32)
        extended = jnp.concatenate([att, rim, jnp.zeros((14, channels), jnp.float32)], 0).astype(jnp.bfloat16)
        one = jnp.dot(take_one, extended, preferred_element_type=jnp.float32)
        two = jnp.dot(take_two, extended, preferred_element_type=jnp.float32)
        w_one = up_ref[0, pl.ds(t, 1), :]
        w_two = up_ref[STRIDE, pl.ds(t, 1), :]
        for s in range(1, STRIDE):
            w_one = jnp.where(phase_row == s, up_ref[s, pl.ds(t, 1), :], w_one)
            w_two = jnp.where(phase_row == s, up_ref[s + STRIDE, pl.ds(t, 1), :], w_two)
        term = one.reshape(rows // 8, 8, channels) * w_one[None] + two.reshape(rows // 8, 8, channels) * w_two[None]
        branch = term if branch is None else branch + term
    branch = branch.reshape(rows, channels)
    byte_row = lax.broadcasted_iota(jnp.int32, (rows, channels), 0) + first
    out_ref[...] = x_ref[...] + jnp.where(byte_row < lim_ref[0], branch, 0.0)


def up_and_mix(limit, returned, byte_states, up_kernel, copies_n, per_t, nq, qr):
    rows, channels = byte_states.shape
    lat = rows // STRIDE
    steps = 4 if rows % 32 == 0 else 1
    part = rows // steps
    return pl.pallas_call(
        functools.partial(up_kernel_fn, copies_n, per_t, nq, qr, lat),
        grid=(steps,),
        out_shape=jax.ShapeDtypeStruct((rows, channels), jnp.float32),
        in_specs=[
            pl.BlockSpec(memory_space=pltpu.SMEM),
            pl.BlockSpec(returned.shape, lambda b: (0, 0, 0)),
            pl.BlockSpec((part, channels), lambda b: (b, 0)),
            pl.BlockSpec(up_kernel.shape, lambda b: (0, 0, 0)),
        ],
        out_specs=pl.BlockSpec((part, channels), lambda b: (b, 0)),
        cost_estimate=pl.CostEstimate(
            flops=4 * KERNEL * rows * channels + 4 * STRIDE * rows * (lat + 16) * channels,
            bytes_accessed=8 * rows * channels + returned.size * 2,
            transcendentals=0,
        ),
    )(limit, returned, byte_states, up_kernel)


def body(byte_states, doc_length, block_ids, qk_kernel, value_kernel, up_kernel):
    rows_here, channels = byte_states.shape
    lat_dev = rows_here // STRIDE
    n_ctx = lax.axis_size("ctx")
    device = lax.axis_index("ctx")
    lat_total = lat_dev * n_ctx
    local_heads = STRIDE * channels // CHANNEL_WIDTH
    copies_n = max(1, n_ctx // local_heads)
    groups_n = n_ctx // copies_n
    head_width = STRIDE * channels // groups_n
    head_here = head_width // CHANNEL_WIDTH
    query_rows = lat_dev // copies_n
    stripe = device % copies_n

    nq = head_here
    per_t = channels // head_width
    both_local = shorten_both(byte_states, qk_kernel, value_kernel, groups_n, per_t, nq)
    kv_rows = both_local.shape[1]
    if copies_n > 1:
        both_local = jnp.broadcast_to(
            both_local[:, None], (groups_n, copies_n, kv_rows, CHANNEL_WIDTH)
        ).reshape(n_ctx, kv_rows, CHANNEL_WIDTH)
    both_all = lax.all_to_all(both_local, "ctx", split_axis=0, concat_axis=0, tiled=True)
    main_kv = both_all[:, : 2 * nq * lat_dev].reshape(n_ctx, 2 * nq, lat_dev, CHANNEL_WIDTH)
    edge = both_all[:, 2 * nq * lat_dev : 2 * nq * lat_dev + 8 * nq].astype(jnp.float32)
    edge = edge.reshape(n_ctx, 4, 2 * nq, CHANNEL_WIDTH)
    own_first = edge[:, 0] + edge[:, 1]
    from_before = edge[:, 2] + edge[:, 3]
    from_before = jnp.concatenate([jnp.zeros_like(from_before[:1]), from_before[:-1]], 0)
    first_rows = (own_first + from_before).astype(jnp.bfloat16)
    at_first = lax.broadcasted_iota(jnp.int32, main_kv.shape, 2) == 0
    main_kv = jnp.where(at_first, first_rows[:, :, None, :], main_kv)
    key_all = main_kv[:, :nq]
    value_all = main_kv[:, nq:]
    queries = key_all.reshape(n_ctx, nq, copies_n, query_rows, CHANNEL_WIDTH)[:, :, 0]
    if copies_n > 1:
        queries = lax.dynamic_index_in_dim(
            key_all.reshape(n_ctx, nq, copies_n, query_rows, CHANNEL_WIDTH), stripe, 2, keepdims=False
        )
    query_count = n_ctx * query_rows
    query_heads = queries.transpose(1, 0, 2, 3).reshape(nq, query_count, CHANNEL_WIDTH)
    key_heads = key_all.transpose(1, 0, 2, 3).reshape(nq, lat_total, CHANNEL_WIDTH)
    value_heads = value_all.transpose(1, 0, 2, 3).reshape(nq, lat_total, CHANNEL_WIDTH)
    asking_index = (
        jnp.arange(n_ctx, dtype=jnp.int32)[:, None] * lat_dev
        + stripe * query_rows
        + jnp.arange(query_rows, dtype=jnp.int32)[None, :]
    ).reshape(query_count)
    query_seg = lax.dynamic_index_in_dim(
        block_ids.reshape(n_ctx, copies_n, query_rows), stripe, 1, keepdims=False
    ).reshape(query_count)
    lat_len = doc_length[0] // STRIDE
    sharpness_divisor = jnp.log(asking_index.astype(jnp.float32) + 2.0) / (
        math.sqrt(float(CHANNEL_WIDTH)) * math.sqrt(math.log(float(lat_total)))
    )
    block_len = min(lat_total, max(512, lat_total // 16))
    block_count = lat_total // block_len

    def attend(running, key_start):
        key_block = lax.dynamic_slice_in_dim(key_heads, key_start, block_len, 1)
        value_block = lax.dynamic_slice_in_dim(value_heads, key_start, block_len, 1)
        seg_block = lax.dynamic_slice_in_dim(block_ids, key_start, block_len, 0)
        key_pos = key_start + jnp.arange(block_len, dtype=jnp.int32)
        run_max, run_sum, run_acc = running
        raw_affinity = (
            jnp.einsum("hqd,hkd->hqk", query_heads, key_block, preferred_element_type=jnp.float32)
            * sharpness_divisor[None, :, None]
        )
        visible = (
            (seg_block[None, :] <= query_seg[:, None])
            & (key_pos[None, :] < lat_len)
            & ((key_pos[None, :] != asking_index[:, None]) | (asking_index[:, None] == 0))
        )
        new_max = jnp.maximum(
            run_max, jnp.max(jnp.where(visible[None], raw_affinity, -1e30), axis=2)
        )
        weights = jnp.where(visible[None], jnp.exp(raw_affinity - new_max[:, :, None]), 0.0)
        factor = jnp.exp(run_max - new_max)
        new_sum = run_sum * factor + jnp.sum(weights, axis=2)
        new_acc = run_acc * factor[:, :, None] + jnp.einsum(
            "hqk,hkd->hqd",
            weights.astype(jnp.bfloat16),
            value_block,
            preferred_element_type=jnp.float32,
        )
        updated = (new_max, new_sum, new_acc)
        return (updated, None)

    initial = (
        jnp.full((head_here, query_count), -1e30, jnp.float32),
        jnp.zeros((head_here, query_count), jnp.float32),
        jnp.zeros((head_here, query_count, CHANNEL_WIDTH), jnp.float32),
    )
    finals, unused = lax.scan(attend, initial, jnp.arange(block_count, dtype=jnp.int32) * block_len)
    attended = (finals[2] / finals[1][:, :, None]).astype(jnp.bfloat16)
    attended = attended.reshape(nq, n_ctx, query_rows, CHANNEL_WIDTH).transpose(1, 0, 2, 3)
    rim_out = jnp.concatenate(
        [jnp.zeros((1, nq, 2, CHANNEL_WIDTH), jnp.bfloat16), attended[:-1, :, query_rows - 2 :]], 0
    )
    main_rows = nq * query_rows
    used_rows = main_rows + 2 * nq
    ret_rows = -(-used_rows // 16) * 16
    outgoing = jnp.concatenate(
        [
            attended.reshape(n_ctx, main_rows, CHANNEL_WIDTH),
            rim_out.reshape(n_ctx, 2 * nq, CHANNEL_WIDTH),
            jnp.zeros((n_ctx, ret_rows - used_rows, CHANNEL_WIDTH), jnp.bfloat16),
        ],
        1,
    )
    returned = lax.all_to_all(outgoing, "ctx", split_axis=0, concat_axis=0, tiled=True)
    limit = (doc_length[0] - device * rows_here).reshape(1).astype(jnp.int32)
    return up_and_mix(limit, returned, byte_states, up_kernel, copies_n, per_t, nq, query_rows)

def solution(mesh):
    return jax.shard_map(
        body,
        mesh=mesh,
        in_specs=(
            P(("groups", "ctx"), "head"),
            P("groups"),
            P("groups"),
            P(None, None, "head"),
            P(None, None, "head"),
            P(None, None, "head"),
        ),
        out_specs=P(("groups", "ctx"), "head"),
        check_vma=False,
    )
```

```python
import functools
import math

import jax
import jax.numpy as jnp
from jax import lax
from jax.experimental import pallas as pl
from jax.experimental.pallas import tpu as pltpu
from jax.sharding import PartitionSpec as P

CHANNEL_WIDTH = 128
STRIDE = 4
KERNEL = 8


def shifted(x, axis, by):
    devices = lax.axis_size(axis)
    pairs = [(i, i + by) for i in range(devices) if 0 <= i + by < devices]
    return lax.ppermute(x, axis, pairs)


def three_bf16(value):
    hi = value.astype(jnp.bfloat16)
    rest = value - hi.astype(jnp.float32)
    mid = rest.astype(jnp.bfloat16)
    lo = (rest - mid.astype(jnp.float32)).astype(jnp.bfloat16)
    return hi, mid, lo


def exact_rows(select, value):
    total = None
    for piece in three_bf16(value):
        part = jnp.dot(select, piece, preferred_element_type=jnp.float32)
        total = part if total is None else total + part
    return total


def split_pair(value):
    hi = value.astype(jnp.bfloat16)
    lo = (value - hi.astype(jnp.float32)).astype(jnp.bfloat16)
    return hi, lo


def shorten_kernel(per_t, nq, x_ref, qk_ref, vk_ref, out_ref):
    rows, channels = x_ref.shape
    lat = rows // STRIDE
    lanes = CHANNEL_WIDTH
    blocks = channels // lanes
    pick_row = lax.broadcasted_iota(jnp.int32, (rows, rows), 0)
    pick_col = lax.broadcasted_iota(jnp.int32, (rows, rows), 1)
    pick = (pick_col == (pick_row % lat) * STRIDE + pick_row // lat).astype(jnp.bfloat16)
    by_phase = exact_rows(pick, x_ref[...])
    phase = [by_phase[s * lat : (s + 1) * lat] for s in range(STRIDE)]
    first_row = lax.broadcasted_iota(jnp.int32, (lat, channels), 0) == 0
    edge_row = lax.broadcasted_iota(jnp.int32, (16, lanes), 0)
    edge = [jnp.zeros((16, lanes), jnp.float32) for _ in range(STRIDE * per_t)]
    for which, kern_ref in enumerate((qk_ref, vk_ref)):
        for t in range(STRIDE):
            own = phase[0] * kern_ref[STRIDE, pl.ds(t, 1), :]
            before = phase[0] * kern_ref[0, pl.ds(t, 1), :]
            for s in range(1, STRIDE):
                own = own + phase[s] * kern_ref[STRIDE + s, pl.ds(t, 1), :]
                before = before + phase[s] * kern_ref[s, pl.ds(t, 1), :]
            total = own + jnp.where(first_row, 0.0, pltpu.roll(before, 1, 0))
            total = total.astype(jnp.bfloat16)
            own_hi, own_lo = split_pair(own[0:1])
            next_hi, next_lo = split_pair(before[lat - 1 : lat])
            for block in range(blocks):
                lane = slice(block * lanes, (block + 1) * lanes)
                g = t * per_t + block // nq
                slot = which * nq + block % nq
                out_ref[g, pl.ds(slot * lat, lat), :] = total[:, lane]
                for e, piece in enumerate((own_hi, own_lo, next_hi, next_lo)):
                    edge[g] = jnp.where(edge_row == e * 2 * nq + slot, piece[:, lane].astype(jnp.float32), edge[g])
    for g in range(STRIDE * per_t):
        out_ref[g, pl.ds(2 * nq * lat, 16), :] = edge[g].astype(jnp.bfloat16)


def shorten_both(byte_states, qk_kernel, value_kernel, groups_n, per_t, nq):
    rows, channels = byte_states.shape
    lat = rows // STRIDE
    kv_rows = 2 * nq * lat + 16
    vmem = pl.BlockSpec(memory_space=pltpu.VMEM)
    return pl.pallas_call(
        functools.partial(shorten_kernel, per_t, nq),
        out_shape=jax.ShapeDtypeStruct((groups_n, kv_rows, CHANNEL_WIDTH), jnp.bfloat16),
        in_specs=[vmem] * 3,
        out_specs=vmem,
        cost_estimate=pl.CostEstimate(
            flops=4 * KERNEL * rows * channels + 6 * rows * rows * channels,
            bytes_accessed=4 * rows * channels + 2 * KERNEL * STRIDE * channels * 4 + 2 * rows * channels * 2,
            transcendentals=0,
        ),
    )(byte_states, qk_kernel, value_kernel)


def up_kernel_fn(copies_n, per_t, nq, qr, lim_ref, ret_ref, x_ref, up_ref, out_ref):
    rows, channels = x_ref.shape
    lat = rows // STRIDE
    lanes = CHANNEL_WIDTH
    blocks = channels // lanes
    row = lax.broadcasted_iota(jnp.int32, (lat, channels), 0)
    prior_one = []
    prior_two = []
    for t in range(STRIDE):
        att_parts = []
        rim_parts = []
        for block in range(blocks):
            g = t * per_t + block // nq
            q = block % nq
            pieces = [ret_ref[g * copies_n + s, pl.ds(q * qr, qr), :] for s in range(copies_n)]
            att_parts.append(pieces[0] if copies_n == 1 else jnp.concatenate(pieces, 0))
            rim_parts.append(ret_ref[g * copies_n + copies_n - 1, pl.ds(nq * qr + 2 * q, 2), :])
        att = jnp.concatenate(att_parts, 1).astype(jnp.float32)
        rim = jnp.concatenate(rim_parts, 1).astype(jnp.float32)
        one = jnp.where(row == 0, rim[1:2], pltpu.roll(att, 1, 0))
        two = jnp.where(row == 0, rim[0:1], jnp.where(row == 1, rim[1:2], pltpu.roll(att, 2, 0)))
        prior_one.append(one)
        prior_two.append(two)
    by_phase = []
    for s in range(STRIDE):
        total = prior_one[0] * up_ref[s, pl.ds(0, 1), :] + prior_two[0] * up_ref[s + STRIDE, pl.ds(0, 1), :]
        for t in range(1, STRIDE):
            total = total + prior_one[t] * up_ref[s, pl.ds(t, 1), :]
            total = total + prior_two[t] * up_ref[s + STRIDE, pl.ds(t, 1), :]
        by_phase.append(total)
    by_phase = jnp.concatenate(by_phase, 0)
    put_row = lax.broadcasted_iota(jnp.int32, (rows, rows), 0)
    put_col = lax.broadcasted_iota(jnp.int32, (rows, rows), 1)
    put = (put_col == (put_row % STRIDE) * lat + put_row // STRIDE).astype(jnp.bfloat16)
    branch = exact_rows(put, by_phase)
    byte_row = lax.broadcasted_iota(jnp.int32, (rows, channels), 0)
    out_ref[...] = x_ref[...] + jnp.where(byte_row < lim_ref[0], branch, 0.0)


def up_and_mix(limit, returned, byte_states, up_kernel, copies_n, per_t, nq, qr):
    rows, channels = byte_states.shape
    vmem = pl.BlockSpec(memory_space=pltpu.VMEM)
    return pl.pallas_call(
        functools.partial(up_kernel_fn, copies_n, per_t, nq, qr),
        out_shape=jax.ShapeDtypeStruct((rows, channels), jnp.float32),
        in_specs=[pl.BlockSpec(memory_space=pltpu.SMEM), vmem, vmem, vmem],
        out_specs=vmem,
        cost_estimate=pl.CostEstimate(
            flops=4 * KERNEL * rows * channels + 6 * rows * rows * channels,
            bytes_accessed=8 * rows * channels + returned.size * 2,
            transcendentals=0,
        ),
    )(limit, returned, byte_states, up_kernel)


def attend_kernel(lat, nq, denom, kv_ref, bias_ref, out_ref):
    n_ctx = kv_ref.shape[0]
    total = n_ctx * lat
    lanes = CHANNEL_WIDTH
    edge_at = 2 * nq * lat
    edges = kv_ref[:, pl.ds(edge_at, 16), :].astype(jnp.float32)
    first_row = lax.broadcasted_iota(jnp.int32, (lat, lanes), 0) == 0
    sharp = jnp.log(lax.broadcasted_iota(jnp.int32, (total, 1), 0).astype(jnp.float32) + 2.0) / denom
    tile_row = lax.broadcasted_iota(jnp.int32, (16, lanes), 0)
    tiles = [jnp.zeros((16, lanes), jnp.float32) for _ in range(n_ctx)]

    def gathered(slot):
        pieces = []
        for i in range(n_ctx):
            own = edges[i, 0 * 2 * nq + slot : 0 * 2 * nq + slot + 1] + edges[i, 1 * 2 * nq + slot : 1 * 2 * nq + slot + 1]
            if i > 0:
                before = edges[i - 1, 2 * 2 * nq + slot : 2 * 2 * nq + slot + 1] + edges[
                    i - 1, 3 * 2 * nq + slot : 3 * 2 * nq + slot + 1
                ]
            else:
                before = jnp.zeros_like(own)
            fixed = (own + before).astype(jnp.bfloat16).astype(jnp.float32)
            piece = kv_ref[i, pl.ds(slot * lat, lat), :].astype(jnp.float32)
            pieces.append(jnp.where(first_row, fixed, piece))
        return jnp.concatenate(pieces, 0).astype(jnp.bfloat16)

    for q in range(nq):
        keys = gathered(q)
        values = gathered(nq + q)
        scores = lax.dot_general(
            keys, keys, (((1,), (1,)), ((), ())), preferred_element_type=jnp.float32
        ) * sharp
        scores = scores + bias_ref[...]
        top = jnp.max(scores, axis=1, keepdims=True)
        weights = jnp.exp(scores - top)
        sums = jnp.sum(weights, axis=1, keepdims=True)
        rows = jnp.dot(weights.astype(jnp.bfloat16), values, preferred_element_type=jnp.float32)
        rows = (rows / sums).astype(jnp.bfloat16)
        for d in range(n_ctx):
            out_ref[d, pl.ds(q * lat, lat), :] = rows[d * lat : (d + 1) * lat]
        wide = rows.astype(jnp.float32)
        for d in range(1, n_ctx):
            for e in range(2):
                at = d * lat - 2 + e
                tiles[d] = jnp.where(tile_row == 2 * q + e, wide[at : at + 1], tiles[d])
    for d in range(n_ctx):
        out_ref[d, pl.ds(nq * lat, 16), :] = tiles[d].astype(jnp.bfloat16)


def attend_whole(both_all, bias, nq, lat, denom):
    n_ctx, _, lanes = both_all.shape
    total = n_ctx * lat
    vmem = pl.BlockSpec(memory_space=pltpu.VMEM)
    ret_rows = nq * lat + 16
    return pl.pallas_call(
        functools.partial(attend_kernel, lat, nq, denom),
        out_shape=jax.ShapeDtypeStruct((n_ctx, ret_rows, lanes), jnp.bfloat16),
        in_specs=[vmem, vmem],
        out_specs=vmem,
        cost_estimate=pl.CostEstimate(
            flops=4 * nq * total * total * lanes,
            bytes_accessed=both_all.size * 2 + total * total * 4 + n_ctx * ret_rows * lanes * 2,
            transcendentals=nq * total * total,
        ),
    )(both_all, bias)


def body(byte_states, doc_length, block_ids, qk_kernel, value_kernel, up_kernel):
    rows_here, channels = byte_states.shape
    lat_dev = rows_here // STRIDE
    n_ctx = lax.axis_size("ctx")
    device = lax.axis_index("ctx")
    lat_total = lat_dev * n_ctx
    local_heads = STRIDE * channels // CHANNEL_WIDTH
    copies_n = max(1, n_ctx // local_heads)
    groups_n = n_ctx // copies_n
    head_width = STRIDE * channels // groups_n
    head_here = head_width // CHANNEL_WIDTH
    query_rows = lat_dev // copies_n
    stripe = device % copies_n

    nq = head_here
    per_t = channels // head_width
    both_local = shorten_both(byte_states, qk_kernel, value_kernel, groups_n, per_t, nq)
    kv_rows = both_local.shape[1]
    if copies_n > 1:
        both_local = jnp.broadcast_to(
            both_local[:, None], (groups_n, copies_n, kv_rows, CHANNEL_WIDTH)
        ).reshape(n_ctx, kv_rows, CHANNEL_WIDTH)
    both_all = lax.all_to_all(both_local, "ctx", split_axis=0, concat_axis=0, tiled=True)
    if copies_n == 1 and lat_total <= 1024 and nq <= 8 and lat_dev % 16 == 0:
        lat_len = doc_length[0] // STRIDE
        places = jnp.arange(lat_total, dtype=jnp.int32)
        visible = (
            (block_ids[None, :] <= block_ids[:, None])
            & (places[None, :] < lat_len)
            & ((places[None, :] != places[:, None]) | (places[:, None] == 0))
        )
        bias = jnp.where(visible, 0.0, -1e30).astype(jnp.float32)
        denom = math.sqrt(float(CHANNEL_WIDTH)) * math.sqrt(math.log(float(lat_total)))
        outgoing = attend_whole(both_all, bias, nq, lat_dev, denom)
        returned = lax.all_to_all(outgoing, "ctx", split_axis=0, concat_axis=0, tiled=True)
        limit = (doc_length[0] - device * rows_here).reshape(1).astype(jnp.int32)
        return up_and_mix(limit, returned, byte_states, up_kernel, copies_n, per_t, nq, query_rows)
    main_kv = both_all[:, : 2 * nq * lat_dev].reshape(n_ctx, 2 * nq, lat_dev, CHANNEL_WIDTH)
    edge = both_all[:, 2 * nq * lat_dev : 2 * nq * lat_dev + 8 * nq].astype(jnp.float32)
    edge = edge.reshape(n_ctx, 4, 2 * nq, CHANNEL_WIDTH)
    own_first = edge[:, 0] + edge[:, 1]
    from_before = edge[:, 2] + edge[:, 3]
    from_before = jnp.concatenate([jnp.zeros_like(from_before[:1]), from_before[:-1]], 0)
    first_rows = (own_first + from_before).astype(jnp.bfloat16)
    at_first = lax.broadcasted_iota(jnp.int32, main_kv.shape, 2) == 0
    main_kv = jnp.where(at_first, first_rows[:, :, None, :], main_kv)
    key_all = main_kv[:, :nq]
    value_all = main_kv[:, nq:]
    queries = key_all.reshape(n_ctx, nq, copies_n, query_rows, CHANNEL_WIDTH)[:, :, 0]
    if copies_n > 1:
        queries = lax.dynamic_index_in_dim(
            key_all.reshape(n_ctx, nq, copies_n, query_rows, CHANNEL_WIDTH), stripe, 2, keepdims=False
        )
    query_count = n_ctx * query_rows
    query_heads = queries.transpose(1, 0, 2, 3).reshape(nq, query_count, CHANNEL_WIDTH)
    key_heads = key_all.transpose(1, 0, 2, 3).reshape(nq, lat_total, CHANNEL_WIDTH)
    value_heads = value_all.transpose(1, 0, 2, 3).reshape(nq, lat_total, CHANNEL_WIDTH)
    asking_index = (
        jnp.arange(n_ctx, dtype=jnp.int32)[:, None] * lat_dev
        + stripe * query_rows
        + jnp.arange(query_rows, dtype=jnp.int32)[None, :]
    ).reshape(query_count)
    query_seg = lax.dynamic_index_in_dim(
        block_ids.reshape(n_ctx, copies_n, query_rows), stripe, 1, keepdims=False
    ).reshape(query_count)
    lat_len = doc_length[0] // STRIDE
    sharpness_divisor = jnp.log(asking_index.astype(jnp.float32) + 2.0) / (
        math.sqrt(float(CHANNEL_WIDTH)) * math.sqrt(math.log(float(lat_total)))
    )
    block_len = min(lat_total, max(512, lat_total // 16))
    block_count = lat_total // block_len

    def attend(running, key_start):
        key_block = lax.dynamic_slice_in_dim(key_heads, key_start, block_len, 1)
        value_block = lax.dynamic_slice_in_dim(value_heads, key_start, block_len, 1)
        seg_block = lax.dynamic_slice_in_dim(block_ids, key_start, block_len, 0)
        key_pos = key_start + jnp.arange(block_len, dtype=jnp.int32)
        run_max, run_sum, run_acc = running
        raw_affinity = (
            jnp.einsum("hqd,hkd->hqk", query_heads, key_block, preferred_element_type=jnp.float32)
            * sharpness_divisor[None, :, None]
        )
        visible = (
            (seg_block[None, :] <= query_seg[:, None])
            & (key_pos[None, :] < lat_len)
            & ((key_pos[None, :] != asking_index[:, None]) | (asking_index[:, None] == 0))
        )
        new_max = jnp.maximum(
            run_max, jnp.max(jnp.where(visible[None], raw_affinity, -1e30), axis=2)
        )
        weights = jnp.where(visible[None], jnp.exp(raw_affinity - new_max[:, :, None]), 0.0)
        factor = jnp.exp(run_max - new_max)
        new_sum = run_sum * factor + jnp.sum(weights, axis=2)
        new_acc = run_acc * factor[:, :, None] + jnp.einsum(
            "hqk,hkd->hqd",
            weights.astype(jnp.bfloat16),
            value_block,
            preferred_element_type=jnp.float32,
        )
        updated = (new_max, new_sum, new_acc)
        return (updated, None)

    initial = (
        jnp.full((head_here, query_count), -1e30, jnp.float32),
        jnp.zeros((head_here, query_count), jnp.float32),
        jnp.zeros((head_here, query_count, CHANNEL_WIDTH), jnp.float32),
    )
    finals, unused = lax.scan(attend, initial, jnp.arange(block_count, dtype=jnp.int32) * block_len)
    attended = (finals[2] / finals[1][:, :, None]).astype(jnp.bfloat16)
    attended = attended.reshape(nq, n_ctx, query_rows, CHANNEL_WIDTH).transpose(1, 0, 2, 3)
    rim_out = jnp.concatenate(
        [jnp.zeros((1, nq, 2, CHANNEL_WIDTH), jnp.bfloat16), attended[:-1, :, query_rows - 2 :]], 0
    )
    main_rows = nq * query_rows
    used_rows = main_rows + 2 * nq
    ret_rows = -(-used_rows // 16) * 16
    outgoing = jnp.concatenate(
        [
            attended.reshape(n_ctx, main_rows, CHANNEL_WIDTH),
            rim_out.reshape(n_ctx, 2 * nq, CHANNEL_WIDTH),
            jnp.zeros((n_ctx, ret_rows - used_rows, CHANNEL_WIDTH), jnp.bfloat16),
        ],
        1,
    )
    returned = lax.all_to_all(outgoing, "ctx", split_axis=0, concat_axis=0, tiled=True)
    limit = (doc_length[0] - device * rows_here).reshape(1).astype(jnp.int32)
    return up_and_mix(limit, returned, byte_states, up_kernel, copies_n, per_t, nq, query_rows)

def solution(mesh):
    return jax.shard_map(
        body,
        mesh=mesh,
        in_specs=(
            P(("groups", "ctx"), "head"),
            P("groups"),
            P("groups"),
            P(None, None, "head"),
            P(None, None, "head"),
            P(None, None, "head"),
        ),
        out_specs=P(("groups", "ctx"), "head"),
        check_vma=False,
    )
```

```python
import functools
import math

import jax
import jax.numpy as jnp
from jax import lax
from jax.experimental import pallas as pl
from jax.experimental.pallas import tpu as pltpu
from jax.sharding import PartitionSpec as P

CHANNEL_WIDTH = 128
STRIDE = 4
KERNEL = 8


def shifted(x, axis, by):
    devices = lax.axis_size(axis)
    pairs = [(i, i + by) for i in range(devices) if 0 <= i + by < devices]
    return lax.ppermute(x, axis, pairs)


def three_bf16(value):
    hi = value.astype(jnp.bfloat16)
    rest = value - hi.astype(jnp.float32)
    mid = rest.astype(jnp.bfloat16)
    lo = (rest - mid.astype(jnp.float32)).astype(jnp.bfloat16)
    return hi, mid, lo


def exact_rows(select, value):
    total = None
    for piece in three_bf16(value):
        part = jnp.dot(select, piece, preferred_element_type=jnp.float32)
        total = part if total is None else total + part
    return total


def split_pair(value):
    hi = value.astype(jnp.bfloat16)
    lo = (value - hi.astype(jnp.float32)).astype(jnp.bfloat16)
    return hi, lo


def shorten_kernel(per_t, nq, x_ref, qk_ref, vk_ref, out_ref):
    rows, channels = x_ref.shape
    lat = rows // STRIDE
    lanes = CHANNEL_WIDTH
    blocks = channels // lanes
    pick_row = lax.broadcasted_iota(jnp.int32, (rows, rows), 0)
    pick_col = lax.broadcasted_iota(jnp.int32, (rows, rows), 1)
    pick = (pick_col == (pick_row % lat) * STRIDE + pick_row // lat).astype(jnp.bfloat16)
    by_phase = exact_rows(pick, x_ref[...])
    phase = [by_phase[s * lat : (s + 1) * lat] for s in range(STRIDE)]
    first_row = lax.broadcasted_iota(jnp.int32, (lat, channels), 0) == 0
    edge_row = lax.broadcasted_iota(jnp.int32, (16, lanes), 0)
    edge = [jnp.zeros((16, lanes), jnp.float32) for _ in range(STRIDE * per_t)]
    for which, kern_ref in enumerate((qk_ref, vk_ref)):
        for t in range(STRIDE):
            own = phase[0] * kern_ref[STRIDE, pl.ds(t, 1), :]
            before = phase[0] * kern_ref[0, pl.ds(t, 1), :]
            for s in range(1, STRIDE):
                own = own + phase[s] * kern_ref[STRIDE + s, pl.ds(t, 1), :]
                before = before + phase[s] * kern_ref[s, pl.ds(t, 1), :]
            total = own + jnp.where(first_row, 0.0, pltpu.roll(before, 1, 0))
            total = total.astype(jnp.bfloat16)
            own_hi, own_lo = split_pair(own[0:1])
            next_hi, next_lo = split_pair(before[lat - 1 : lat])
            for block in range(blocks):
                lane = slice(block * lanes, (block + 1) * lanes)
                g = t * per_t + block // nq
                slot = which * nq + block % nq
                out_ref[g, pl.ds(slot * lat, lat), :] = total[:, lane]
                for e, piece in enumerate((own_hi, own_lo, next_hi, next_lo)):
                    edge[g] = jnp.where(edge_row == e * 2 * nq + slot, piece[:, lane].astype(jnp.float32), edge[g])
    for g in range(STRIDE * per_t):
        out_ref[g, pl.ds(2 * nq * lat, 16), :] = edge[g].astype(jnp.bfloat16)


def shorten_both(byte_states, qk_kernel, value_kernel, groups_n, per_t, nq):
    rows, channels = byte_states.shape
    lat = rows // STRIDE
    kv_rows = 2 * nq * lat + 16
    vmem = pl.BlockSpec(memory_space=pltpu.VMEM)
    return pl.pallas_call(
        functools.partial(shorten_kernel, per_t, nq),
        out_shape=jax.ShapeDtypeStruct((groups_n, kv_rows, CHANNEL_WIDTH), jnp.bfloat16),
        in_specs=[vmem] * 3,
        out_specs=vmem,
        cost_estimate=pl.CostEstimate(
            flops=4 * KERNEL * rows * channels + 6 * rows * rows * channels,
            bytes_accessed=4 * rows * channels + 2 * KERNEL * STRIDE * channels * 4 + 2 * rows * channels * 2,
            transcendentals=0,
        ),
    )(byte_states, qk_kernel, value_kernel)


def up_kernel_fn(lim_ref, ext_ref, x_ref, up_ref, out_ref):
    rows, channels = x_ref.shape
    lat = rows // STRIDE
    wide = ext_ref.shape[1]
    pick_row = lax.broadcasted_iota(jnp.int32, (rows, wide), 0)
    pick_col = lax.broadcasted_iota(jnp.int32, (rows, wide), 1)
    latent = pick_row // STRIDE
    col_one = jnp.where(latent >= 1, latent - 1, lat + 1)
    col_two = jnp.where(latent >= 2, latent - 2, lat + latent)
    take_one = jnp.where(pick_col == col_one, 1.0, 0.0).astype(jnp.bfloat16)
    take_two = jnp.where(pick_col == col_two, 1.0, 0.0).astype(jnp.bfloat16)
    phase_row = lax.broadcasted_iota(jnp.int32, (8, channels), 0) % STRIDE
    branch = None
    for t in range(STRIDE):
        extended = ext_ref[t]
        one = jnp.dot(take_one, extended, preferred_element_type=jnp.float32)
        two = jnp.dot(take_two, extended, preferred_element_type=jnp.float32)
        w_one = up_ref[0, pl.ds(t, 1), :]
        w_two = up_ref[STRIDE, pl.ds(t, 1), :]
        for s in range(1, STRIDE):
            w_one = jnp.where(phase_row == s, up_ref[s, pl.ds(t, 1), :], w_one)
            w_two = jnp.where(phase_row == s, up_ref[s + STRIDE, pl.ds(t, 1), :], w_two)
        term = one.reshape(rows // 8, 8, channels) * w_one[None] + two.reshape(rows // 8, 8, channels) * w_two[None]
        branch = term if branch is None else branch + term
    branch = branch.reshape(rows, channels)
    byte_row = lax.broadcasted_iota(jnp.int32, (rows, channels), 0)
    out_ref[...] = x_ref[...] + jnp.where(byte_row < lim_ref[0], branch, 0.0)


def up_and_mix(limit, returned, byte_states, up_kernel, copies_n, per_t, nq, qr):
    rows, channels = byte_states.shape
    lat = rows // STRIDE
    lanes = CHANNEL_WIDTH
    groups_n = returned.shape[0] // copies_n
    by_source = returned.reshape(STRIDE, per_t, copies_n, returned.shape[1], lanes)
    main = by_source[:, :, :, : nq * qr].reshape(STRIDE, per_t, copies_n, nq, qr, lanes)
    main = main.transpose(0, 2, 4, 1, 3, 5).reshape(STRIDE, lat, channels)
    rim = by_source[:, :, copies_n - 1, nq * qr : nq * qr + 2 * nq].reshape(STRIDE, per_t, nq, 2, lanes)
    rim = rim.transpose(0, 3, 1, 2, 4).reshape(STRIDE, 2, channels)
    extended = jnp.concatenate([main, rim, jnp.zeros((STRIDE, 14, channels), jnp.bfloat16)], 1)
    vmem = pl.BlockSpec(memory_space=pltpu.VMEM)
    return pl.pallas_call(
        up_kernel_fn,
        out_shape=jax.ShapeDtypeStruct((rows, channels), jnp.float32),
        in_specs=[pl.BlockSpec(memory_space=pltpu.SMEM), vmem, vmem, vmem],
        out_specs=vmem,
        cost_estimate=pl.CostEstimate(
            flops=4 * KERNEL * rows * channels + 4 * STRIDE * rows * (lat + 16) * channels,
            bytes_accessed=8 * rows * channels + extended.size * 2,
            transcendentals=0,
        ),
    )(limit, extended, byte_states, up_kernel)


def body(byte_states, doc_length, block_ids, qk_kernel, value_kernel, up_kernel):
    rows_here, channels = byte_states.shape
    lat_dev = rows_here // STRIDE
    n_ctx = lax.axis_size("ctx")
    device = lax.axis_index("ctx")
    lat_total = lat_dev * n_ctx
    local_heads = STRIDE * channels // CHANNEL_WIDTH
    copies_n = max(1, n_ctx // local_heads)
    groups_n = n_ctx // copies_n
    head_width = STRIDE * channels // groups_n
    head_here = head_width // CHANNEL_WIDTH
    query_rows = lat_dev // copies_n
    stripe = device % copies_n

    nq = head_here
    per_t = channels // head_width
    both_local = shorten_both(byte_states, qk_kernel, value_kernel, groups_n, per_t, nq)
    kv_rows = both_local.shape[1]
    if copies_n > 1:
        both_local = jnp.broadcast_to(
            both_local[:, None], (groups_n, copies_n, kv_rows, CHANNEL_WIDTH)
        ).reshape(n_ctx, kv_rows, CHANNEL_WIDTH)
    both_all = lax.all_to_all(both_local, "ctx", split_axis=0, concat_axis=0, tiled=True)
    main_kv = both_all[:, : 2 * nq * lat_dev].reshape(n_ctx, 2 * nq, lat_dev, CHANNEL_WIDTH)
    edge = both_all[:, 2 * nq * lat_dev : 2 * nq * lat_dev + 8 * nq].astype(jnp.float32)
    edge = edge.reshape(n_ctx, 4, 2 * nq, CHANNEL_WIDTH)
    own_first = edge[:, 0] + edge[:, 1]
    from_before = edge[:, 2] + edge[:, 3]
    from_before = jnp.concatenate([jnp.zeros_like(from_before[:1]), from_before[:-1]], 0)
    first_rows = (own_first + from_before).astype(jnp.bfloat16)
    at_first = lax.broadcasted_iota(jnp.int32, main_kv.shape, 2) == 0
    main_kv = jnp.where(at_first, first_rows[:, :, None, :], main_kv)
    key_all = main_kv[:, :nq]
    value_all = main_kv[:, nq:]
    queries = key_all.reshape(n_ctx, nq, copies_n, query_rows, CHANNEL_WIDTH)[:, :, 0]
    if copies_n > 1:
        queries = lax.dynamic_index_in_dim(
            key_all.reshape(n_ctx, nq, copies_n, query_rows, CHANNEL_WIDTH), stripe, 2, keepdims=False
        )
    query_count = n_ctx * query_rows
    query_heads = queries.transpose(1, 0, 2, 3).reshape(nq, query_count, CHANNEL_WIDTH)
    key_heads = key_all.transpose(1, 0, 2, 3).reshape(nq, lat_total, CHANNEL_WIDTH)
    value_heads = value_all.transpose(1, 0, 2, 3).reshape(nq, lat_total, CHANNEL_WIDTH)
    asking_index = (
        jnp.arange(n_ctx, dtype=jnp.int32)[:, None] * lat_dev
        + stripe * query_rows
        + jnp.arange(query_rows, dtype=jnp.int32)[None, :]
    ).reshape(query_count)
    query_seg = lax.dynamic_index_in_dim(
        block_ids.reshape(n_ctx, copies_n, query_rows), stripe, 1, keepdims=False
    ).reshape(query_count)
    lat_len = doc_length[0] // STRIDE
    sharpness_divisor = jnp.log(asking_index.astype(jnp.float32) + 2.0) / (
        math.sqrt(float(CHANNEL_WIDTH)) * math.sqrt(math.log(float(lat_total)))
    )
    block_len = min(lat_total, max(512, lat_total // 16))
    block_count = lat_total // block_len

    def attend(running, key_start):
        key_block = lax.dynamic_slice_in_dim(key_heads, key_start, block_len, 1)
        value_block = lax.dynamic_slice_in_dim(value_heads, key_start, block_len, 1)
        seg_block = lax.dynamic_slice_in_dim(block_ids, key_start, block_len, 0)
        key_pos = key_start + jnp.arange(block_len, dtype=jnp.int32)
        run_max, run_sum, run_acc = running
        raw_affinity = (
            jnp.einsum("hqd,hkd->hqk", query_heads, key_block, preferred_element_type=jnp.float32)
            * sharpness_divisor[None, :, None]
        )
        visible = (
            (seg_block[None, :] <= query_seg[:, None])
            & (key_pos[None, :] < lat_len)
            & ((key_pos[None, :] != asking_index[:, None]) | (asking_index[:, None] == 0))
        )
        new_max = jnp.maximum(
            run_max, jnp.max(jnp.where(visible[None], raw_affinity, -1e30), axis=2)
        )
        weights = jnp.where(visible[None], jnp.exp(raw_affinity - new_max[:, :, None]), 0.0)
        factor = jnp.exp(run_max - new_max)
        new_sum = run_sum * factor + jnp.sum(weights, axis=2)
        new_acc = run_acc * factor[:, :, None] + jnp.einsum(
            "hqk,hkd->hqd",
            weights.astype(jnp.bfloat16),
            value_block,
            preferred_element_type=jnp.float32,
        )
        updated = (new_max, new_sum, new_acc)
        return (updated, None)

    initial = (
        jnp.full((head_here, query_count), -1e30, jnp.float32),
        jnp.zeros((head_here, query_count), jnp.float32),
        jnp.zeros((head_here, query_count, CHANNEL_WIDTH), jnp.float32),
    )
    finals, unused = lax.scan(attend, initial, jnp.arange(block_count, dtype=jnp.int32) * block_len)
    attended = (finals[2] / finals[1][:, :, None]).astype(jnp.bfloat16)
    attended = attended.reshape(nq, n_ctx, query_rows, CHANNEL_WIDTH).transpose(1, 0, 2, 3)
    rim_out = jnp.concatenate(
        [jnp.zeros((1, nq, 2, CHANNEL_WIDTH), jnp.bfloat16), attended[:-1, :, query_rows - 2 :]], 0
    )
    main_rows = nq * query_rows
    used_rows = main_rows + 2 * nq
    ret_rows = -(-used_rows // 16) * 16
    outgoing = jnp.concatenate(
        [
            attended.reshape(n_ctx, main_rows, CHANNEL_WIDTH),
            rim_out.reshape(n_ctx, 2 * nq, CHANNEL_WIDTH),
            jnp.zeros((n_ctx, ret_rows - used_rows, CHANNEL_WIDTH), jnp.bfloat16),
        ],
        1,
    )
    returned = lax.all_to_all(outgoing, "ctx", split_axis=0, concat_axis=0, tiled=True)
    limit = (doc_length[0] - device * rows_here).reshape(1).astype(jnp.int32)
    return up_and_mix(limit, returned, byte_states, up_kernel, copies_n, per_t, nq, query_rows)

def solution(mesh):
    return jax.shard_map(
        body,
        mesh=mesh,
        in_specs=(
            P(("groups", "ctx"), "head"),
            P("groups"),
            P("groups"),
            P(None, None, "head"),
            P(None, None, "head"),
            P(None, None, "head"),
        ),
        out_specs=P(("groups", "ctx"), "head"),
        check_vma=False,
    )
```

```python
import functools
import math

import jax
import jax.numpy as jnp
from jax import lax
from jax.experimental import pallas as pl
from jax.experimental.pallas import tpu as pltpu
from jax.sharding import PartitionSpec as P

CHANNEL_WIDTH = 128
STRIDE = 4
KERNEL = 8


def shifted(x, axis, by):
    devices = lax.axis_size(axis)
    pairs = [(i, i + by) for i in range(devices) if 0 <= i + by < devices]
    return lax.ppermute(x, axis, pairs)


def three_bf16(value):
    hi = value.astype(jnp.bfloat16)
    rest = value - hi.astype(jnp.float32)
    mid = rest.astype(jnp.bfloat16)
    lo = (rest - mid.astype(jnp.float32)).astype(jnp.bfloat16)
    return hi, mid, lo


def exact_rows(select, value):
    total = None
    for piece in three_bf16(value):
        part = jnp.dot(select, piece, preferred_element_type=jnp.float32)
        total = part if total is None else total + part
    return total


def split_pair(value):
    hi = value.astype(jnp.bfloat16)
    lo = (value - hi.astype(jnp.float32)).astype(jnp.bfloat16)
    return hi, lo


def shorten_kernel(per_t, nq, x_ref, qk_ref, vk_ref, out_ref):
    rows, channels = x_ref.shape
    lat = rows // STRIDE
    lanes = CHANNEL_WIDTH
    blocks = channels // lanes
    pick_row = lax.broadcasted_iota(jnp.int32, (rows, rows), 0)
    pick_col = lax.broadcasted_iota(jnp.int32, (rows, rows), 1)
    pick = (pick_col == (pick_row % lat) * STRIDE + pick_row // lat).astype(jnp.bfloat16)
    by_phase = exact_rows(pick, x_ref[...])
    phase = [by_phase[s * lat : (s + 1) * lat] for s in range(STRIDE)]
    first_row = lax.broadcasted_iota(jnp.int32, (lat, channels), 0) == 0
    edge_row = lax.broadcasted_iota(jnp.int32, (16, lanes), 0)
    edge = [jnp.zeros((16, lanes), jnp.float32) for _ in range(STRIDE * per_t)]
    for which, kern_ref in enumerate((qk_ref, vk_ref)):
        for t in range(STRIDE):
            own = phase[0] * kern_ref[STRIDE, pl.ds(t, 1), :]
            before = phase[0] * kern_ref[0, pl.ds(t, 1), :]
            for s in range(1, STRIDE):
                own = own + phase[s] * kern_ref[STRIDE + s, pl.ds(t, 1), :]
                before = before + phase[s] * kern_ref[s, pl.ds(t, 1), :]
            total = own + jnp.where(first_row, 0.0, pltpu.roll(before, 1, 0))
            total = total.astype(jnp.bfloat16)
            own_hi, own_lo = split_pair(own[0:1])
            next_hi, next_lo = split_pair(before[lat - 1 : lat])
            for block in range(blocks):
                lane = slice(block * lanes, (block + 1) * lanes)
                g = t * per_t + block // nq
                slot = which * nq + block % nq
                out_ref[g, pl.ds(slot * lat, lat), :] = total[:, lane]
                for e, piece in enumerate((own_hi, own_lo, next_hi, next_lo)):
                    edge[g] = jnp.where(edge_row == e * 2 * nq + slot, piece[:, lane].astype(jnp.float32), edge[g])
    for g in range(STRIDE * per_t):
        out_ref[g, pl.ds(2 * nq * lat, 16), :] = edge[g].astype(jnp.bfloat16)


def shorten_both(byte_states, qk_kernel, value_kernel, groups_n, per_t, nq):
    rows, channels = byte_states.shape
    lat = rows // STRIDE
    kv_rows = 2 * nq * lat + 16
    vmem = pl.BlockSpec(memory_space=pltpu.VMEM)
    return pl.pallas_call(
        functools.partial(shorten_kernel, per_t, nq),
        out_shape=jax.ShapeDtypeStruct((groups_n, kv_rows, CHANNEL_WIDTH), jnp.bfloat16),
        in_specs=[vmem] * 3,
        out_specs=vmem,
        cost_estimate=pl.CostEstimate(
            flops=4 * KERNEL * rows * channels + 6 * rows * rows * channels,
            bytes_accessed=4 * rows * channels + 2 * KERNEL * STRIDE * channels * 4 + 2 * rows * channels * 2,
            transcendentals=0,
        ),
    )(byte_states, qk_kernel, value_kernel)


def up_kernel_fn(copies_n, per_t, nq, qr, lim_ref, ret_ref, x_ref, up_ref, out_ref):
    rows, channels = x_ref.shape
    lat = rows // STRIDE
    lanes = CHANNEL_WIDTH
    blocks = channels // lanes
    row = lax.broadcasted_iota(jnp.int32, (lat, channels), 0)
    sources = ret_ref.shape[0]
    me = lim_ref[1]

    sign = lim_ref[2]

    def where(source):
        return (me - sign * source + sources) % sources

    prior_one = []
    prior_two = []
    for t in range(STRIDE):
        att_parts = []
        rim_parts = []
        for block in range(blocks):
            g = t * per_t + block // nq
            q = block % nq
            pieces = [ret_ref[where(g * copies_n + s), pl.ds(q * qr, qr), :] for s in range(copies_n)]
            att_parts.append(pieces[0] if copies_n == 1 else jnp.concatenate(pieces, 0))
            rim_parts.append(ret_ref[where(g * copies_n + copies_n - 1), pl.ds(nq * qr + 2 * q, 2), :])
        att = jnp.concatenate(att_parts, 1).astype(jnp.float32)
        rim = jnp.concatenate(rim_parts, 1).astype(jnp.float32)
        one = jnp.where(row == 0, rim[1:2], pltpu.roll(att, 1, 0))
        two = jnp.where(row == 0, rim[0:1], jnp.where(row == 1, rim[1:2], pltpu.roll(att, 2, 0)))
        prior_one.append(one)
        prior_two.append(two)
    by_phase = []
    for s in range(STRIDE):
        total = prior_one[0] * up_ref[s, pl.ds(0, 1), :] + prior_two[0] * up_ref[s + STRIDE, pl.ds(0, 1), :]
        for t in range(1, STRIDE):
            total = total + prior_one[t] * up_ref[s, pl.ds(t, 1), :]
            total = total + prior_two[t] * up_ref[s + STRIDE, pl.ds(t, 1), :]
        by_phase.append(total)
    by_phase = jnp.concatenate(by_phase, 0)
    put_row = lax.broadcasted_iota(jnp.int32, (rows, rows), 0)
    put_col = lax.broadcasted_iota(jnp.int32, (rows, rows), 1)
    put = (put_col == (put_row % STRIDE) * lat + put_row // STRIDE).astype(jnp.bfloat16)
    branch = exact_rows(put, by_phase)
    byte_row = lax.broadcasted_iota(jnp.int32, (rows, channels), 0)
    out_ref[...] = x_ref[...] + jnp.where(byte_row < lim_ref[0], branch, 0.0)


def up_and_mix(limit, returned, byte_states, up_kernel, copies_n, per_t, nq, qr):
    rows, channels = byte_states.shape
    vmem = pl.BlockSpec(memory_space=pltpu.VMEM)
    return pl.pallas_call(
        functools.partial(up_kernel_fn, copies_n, per_t, nq, qr),
        out_shape=jax.ShapeDtypeStruct((rows, channels), jnp.float32),
        in_specs=[pl.BlockSpec(memory_space=pltpu.SMEM), vmem, vmem, vmem],
        out_specs=vmem,
        cost_estimate=pl.CostEstimate(
            flops=4 * KERNEL * rows * channels + 6 * rows * rows * channels,
            bytes_accessed=8 * rows * channels + returned.size * 2,
            transcendentals=0,
        ),
    )(limit, returned, byte_states, up_kernel)


def body(byte_states, doc_length, block_ids, qk_kernel, value_kernel, up_kernel):
    rows_here, channels = byte_states.shape
    lat_dev = rows_here // STRIDE
    n_ctx = lax.axis_size("ctx")
    device = lax.axis_index("ctx")
    lat_total = lat_dev * n_ctx
    local_heads = STRIDE * channels // CHANNEL_WIDTH
    copies_n = max(1, n_ctx // local_heads)
    groups_n = n_ctx // copies_n
    head_width = STRIDE * channels // groups_n
    head_here = head_width // CHANNEL_WIDTH
    query_rows = lat_dev // copies_n
    stripe = device % copies_n

    nq = head_here
    per_t = channels // head_width
    both_local = shorten_both(byte_states, qk_kernel, value_kernel, groups_n, per_t, nq)
    kv_rows = both_local.shape[1]
    if copies_n > 1:
        both_local = jnp.broadcast_to(
            both_local[:, None], (groups_n, copies_n, kv_rows, CHANNEL_WIDTH)
        ).reshape(n_ctx, kv_rows, CHANNEL_WIDTH)
    both_all = lax.all_to_all(both_local, "ctx", split_axis=0, concat_axis=0, tiled=True)
    main_kv = both_all[:, : 2 * nq * lat_dev].reshape(n_ctx, 2 * nq, lat_dev, CHANNEL_WIDTH)
    edge = both_all[:, 2 * nq * lat_dev : 2 * nq * lat_dev + 8 * nq].astype(jnp.float32)
    edge = edge.reshape(n_ctx, 4, 2 * nq, CHANNEL_WIDTH)
    own_first = edge[:, 0] + edge[:, 1]
    from_before = edge[:, 2] + edge[:, 3]
    from_before = jnp.concatenate([jnp.zeros_like(from_before[:1]), from_before[:-1]], 0)
    first_rows = (own_first + from_before).astype(jnp.bfloat16)
    at_first = lax.broadcasted_iota(jnp.int32, main_kv.shape, 2) == 0
    main_kv = jnp.where(at_first, first_rows[:, :, None, :], main_kv)
    key_all = main_kv[:, :nq]
    value_all = main_kv[:, nq:]
    queries = key_all.reshape(n_ctx, nq, copies_n, query_rows, CHANNEL_WIDTH)[:, :, 0]
    if copies_n > 1:
        queries = lax.dynamic_index_in_dim(
            key_all.reshape(n_ctx, nq, copies_n, query_rows, CHANNEL_WIDTH), stripe, 2, keepdims=False
        )
    query_count = n_ctx * query_rows
    query_heads = queries.transpose(1, 0, 2, 3).reshape(nq, query_count, CHANNEL_WIDTH)
    key_heads = key_all.transpose(1, 0, 2, 3).reshape(nq, lat_total, CHANNEL_WIDTH)
    value_heads = value_all.transpose(1, 0, 2, 3).reshape(nq, lat_total, CHANNEL_WIDTH)
    asking_index = (
        jnp.arange(n_ctx, dtype=jnp.int32)[:, None] * lat_dev
        + stripe * query_rows
        + jnp.arange(query_rows, dtype=jnp.int32)[None, :]
    ).reshape(query_count)
    query_seg = lax.dynamic_index_in_dim(
        block_ids.reshape(n_ctx, copies_n, query_rows), stripe, 1, keepdims=False
    ).reshape(query_count)
    lat_len = doc_length[0] // STRIDE
    sharpness_divisor = jnp.log(asking_index.astype(jnp.float32) + 2.0) / (
        math.sqrt(float(CHANNEL_WIDTH)) * math.sqrt(math.log(float(lat_total)))
    )
    block_len = min(lat_total, max(512, lat_total // 16))
    block_count = lat_total // block_len

    def attend(running, key_start):
        key_block = lax.dynamic_slice_in_dim(key_heads, key_start, block_len, 1)
        value_block = lax.dynamic_slice_in_dim(value_heads, key_start, block_len, 1)
        seg_block = lax.dynamic_slice_in_dim(block_ids, key_start, block_len, 0)
        key_pos = key_start + jnp.arange(block_len, dtype=jnp.int32)
        run_max, run_sum, run_acc = running
        raw_affinity = (
            jnp.einsum("hqd,hkd->hqk", query_heads, key_block, preferred_element_type=jnp.float32)
            * sharpness_divisor[None, :, None]
        )
        visible = (
            (seg_block[None, :] <= query_seg[:, None])
            & (key_pos[None, :] < lat_len)
            & ((key_pos[None, :] != asking_index[:, None]) | (asking_index[:, None] == 0))
        )
        new_max = jnp.maximum(
            run_max, jnp.max(jnp.where(visible[None], raw_affinity, -1e30), axis=2)
        )
        weights = jnp.where(visible[None], jnp.exp(raw_affinity - new_max[:, :, None]), 0.0)
        factor = jnp.exp(run_max - new_max)
        new_sum = run_sum * factor + jnp.sum(weights, axis=2)
        new_acc = run_acc * factor[:, :, None] + jnp.einsum(
            "hqk,hkd->hqd",
            weights.astype(jnp.bfloat16),
            value_block,
            preferred_element_type=jnp.float32,
        )
        updated = (new_max, new_sum, new_acc)
        return (updated, None)

    initial = (
        jnp.full((head_here, query_count), -1e30, jnp.float32),
        jnp.zeros((head_here, query_count), jnp.float32),
        jnp.zeros((head_here, query_count, CHANNEL_WIDTH), jnp.float32),
    )
    if block_count == 1:
        raw_affinity = (
            jnp.einsum("hqd,hkd->hqk", query_heads, key_heads, preferred_element_type=jnp.float32)
            * sharpness_divisor[None, :, None]
        )
        key_pos = jnp.arange(lat_total, dtype=jnp.int32)
        visible = (
            (block_ids[None, :] <= query_seg[:, None])
            & (key_pos[None, :] < lat_len)
            & ((key_pos[None, :] != asking_index[:, None]) | (asking_index[:, None] == 0))
        )
        raw_affinity = jnp.where(visible[None], raw_affinity, -1e30)
        top = jnp.max(raw_affinity, axis=2, keepdims=True)
        weights = jnp.where(visible[None], jnp.exp(raw_affinity - top), 0.0)
        sums = jnp.sum(weights, axis=2, keepdims=True)
        attended = jnp.einsum(
            "hqk,hkd->hqd", weights.astype(jnp.bfloat16), value_heads, preferred_element_type=jnp.float32
        )
        attended = (attended / sums).astype(jnp.bfloat16)
    else:
        finals, unused = lax.scan(attend, initial, jnp.arange(block_count, dtype=jnp.int32) * block_len)
        attended = (finals[2] / finals[1][:, :, None]).astype(jnp.bfloat16)
    attended = attended.reshape(nq, n_ctx, query_rows, CHANNEL_WIDTH).transpose(1, 0, 2, 3)
    rim_out = jnp.concatenate(
        [jnp.zeros((1, nq, 2, CHANNEL_WIDTH), jnp.bfloat16), attended[:-1, :, query_rows - 2 :]], 0
    )
    main_rows = nq * query_rows
    used_rows = main_rows + 2 * nq
    ret_rows = -(-used_rows // 16) * 16
    outgoing = jnp.concatenate(
        [
            attended.reshape(n_ctx, main_rows, CHANNEL_WIDTH),
            rim_out.reshape(n_ctx, 2 * nq, CHANNEL_WIDTH),
            jnp.zeros((n_ctx, ret_rows - used_rows, CHANNEL_WIDTH), jnp.bfloat16),
        ],
        1,
    )
    if n_ctx <= 8:
        pieces = [lax.dynamic_index_in_dim(outgoing, device, 0, keepdims=False)]
        for s in range(1, n_ctx):
            send = lax.dynamic_index_in_dim(outgoing, (device + s) % n_ctx, 0, keepdims=False)
            pieces.append(lax.ppermute(send, "ctx", [(i, (i + s) % n_ctx) for i in range(n_ctx)]))
        returned = jnp.stack(pieces, 0)
        shifted_by, sign = 1, 1
    else:
        returned = lax.all_to_all(outgoing, "ctx", split_axis=0, concat_axis=0, tiled=True)
        shifted_by, sign = 0, -1
    info = jnp.stack([doc_length[0] - device * rows_here, device * shifted_by, jnp.int32(sign)]).astype(jnp.int32)
    return up_and_mix(info, returned, byte_states, up_kernel, copies_n, per_t, nq, query_rows)

def solution(mesh):
    return jax.shard_map(
        body,
        mesh=mesh,
        in_specs=(
            P(("groups", "ctx"), "head"),
            P("groups"),
            P("groups"),
            P(None, None, "head"),
            P(None, None, "head"),
            P(None, None, "head"),
        ),
        out_specs=P(("groups", "ctx"), "head"),
        check_vma=False,
    )
```

```python
import functools
import math

import jax
import jax.numpy as jnp
from jax import lax
from jax.experimental import pallas as pl
from jax.experimental.pallas import tpu as pltpu
from jax.sharding import PartitionSpec as P

CHANNEL_WIDTH = 128
STRIDE = 4
KERNEL = 8


def shifted(x, axis, by):
    devices = lax.axis_size(axis)
    pairs = [(i, i + by) for i in range(devices) if 0 <= i + by < devices]
    return lax.ppermute(x, axis, pairs)


def three_bf16(value):
    hi = value.astype(jnp.bfloat16)
    rest = value - hi.astype(jnp.float32)
    mid = rest.astype(jnp.bfloat16)
    lo = (rest - mid.astype(jnp.float32)).astype(jnp.bfloat16)
    return hi, mid, lo


def exact_rows(select, value):
    total = None
    for piece in three_bf16(value):
        part = jnp.dot(select, piece, preferred_element_type=jnp.float32)
        total = part if total is None else total + part
    return total


def split_pair(value):
    hi = value.astype(jnp.bfloat16)
    lo = (value - hi.astype(jnp.float32)).astype(jnp.bfloat16)
    return hi, lo


def shorten_kernel(per_t, nq, x_ref, qk_ref, vk_ref, out_hbm, out_ref, sems):
    rows, channels = x_ref.shape
    lat = rows // STRIDE
    lanes = CHANNEL_WIDTH
    blocks = channels // lanes
    pick_row = lax.broadcasted_iota(jnp.int32, (rows, rows), 0)
    pick_col = lax.broadcasted_iota(jnp.int32, (rows, rows), 1)
    pick = (pick_col == (pick_row % lat) * STRIDE + pick_row // lat).astype(jnp.bfloat16)
    by_phase = exact_rows(pick, x_ref[...])
    phase = [by_phase[s * lat : (s + 1) * lat] for s in range(STRIDE)]
    first_row = lax.broadcasted_iota(jnp.int32, (lat, channels), 0) == 0
    edge_row = lax.broadcasted_iota(jnp.int32, (16, lanes), 0)
    copies = []
    for t in range(STRIDE):
        edge = [jnp.zeros((16, lanes), jnp.float32) for _ in range(per_t)]
        for which, kern_ref in enumerate((qk_ref, vk_ref)):
            own = phase[0] * kern_ref[STRIDE, pl.ds(t, 1), :]
            before = phase[0] * kern_ref[0, pl.ds(t, 1), :]
            for s in range(1, STRIDE):
                own = own + phase[s] * kern_ref[STRIDE + s, pl.ds(t, 1), :]
                before = before + phase[s] * kern_ref[s, pl.ds(t, 1), :]
            total = own + jnp.where(first_row, 0.0, pltpu.roll(before, 1, 0))
            total = total.astype(jnp.bfloat16)
            own_hi, own_lo = split_pair(own[0:1])
            next_hi, next_lo = split_pair(before[lat - 1 : lat])
            for block in range(blocks):
                lane = slice(block * lanes, (block + 1) * lanes)
                sub = block // nq
                slot = which * nq + block % nq
                out_ref[t * per_t + sub, pl.ds(slot * lat, lat), :] = total[:, lane]
                for e, piece in enumerate((own_hi, own_lo, next_hi, next_lo)):
                    edge[sub] = jnp.where(edge_row == e * 2 * nq + slot, piece[:, lane].astype(jnp.float32), edge[sub])
        for sub in range(per_t):
            g = t * per_t + sub
            out_ref[g, pl.ds(2 * nq * lat, 16), :] = edge[sub].astype(jnp.bfloat16)
        group = pl.ds(t * per_t, per_t)
        copy = pltpu.make_async_copy(out_ref.at[group], out_hbm.at[group], sems.at[t])
        copy.start()
        copies.append(copy)
    for copy in copies:
        copy.wait()


def shorten_both(byte_states, qk_kernel, value_kernel, groups_n, per_t, nq):
    rows, channels = byte_states.shape
    lat = rows // STRIDE
    kv_rows = 2 * nq * lat + 16
    vmem = pl.BlockSpec(memory_space=pltpu.VMEM)
    return pl.pallas_call(
        functools.partial(shorten_kernel, per_t, nq),
        out_shape=jax.ShapeDtypeStruct((groups_n, kv_rows, CHANNEL_WIDTH), jnp.bfloat16),
        in_specs=[vmem] * 3,
        out_specs=pl.BlockSpec(memory_space=pl.ANY),
        scratch_shapes=[
            pltpu.VMEM((groups_n, kv_rows, CHANNEL_WIDTH), jnp.bfloat16),
            pltpu.SemaphoreType.DMA((STRIDE,)),
        ],
        cost_estimate=pl.CostEstimate(
            flops=4 * KERNEL * rows * channels + 6 * rows * rows * channels,
            bytes_accessed=4 * rows * channels + 2 * KERNEL * STRIDE * channels * 4 + 2 * rows * channels * 2,
            transcendentals=0,
        ),
    )(byte_states, qk_kernel, value_kernel)


def up_kernel_fn(copies_n, per_t, nq, qr, lim_ref, ret_ref, x_hbm, up_ref, out_ref, x_ref, sems):
    x_copy = pltpu.make_async_copy(x_hbm, x_ref, sems.at[0])
    x_copy.start()
    rows, channels = x_ref.shape
    lat = rows // STRIDE
    lanes = CHANNEL_WIDTH
    blocks = channels // lanes
    row = lax.broadcasted_iota(jnp.int32, (lat, channels), 0)
    prior_one = []
    prior_two = []
    for t in range(STRIDE):
        att_parts = []
        rim_parts = []
        for block in range(blocks):
            g = t * per_t + block // nq
            q = block % nq
            pieces = [ret_ref[g * copies_n + s, pl.ds(q * qr, qr), :] for s in range(copies_n)]
            att_parts.append(pieces[0] if copies_n == 1 else jnp.concatenate(pieces, 0))
            rim_parts.append(ret_ref[g * copies_n + copies_n - 1, pl.ds(nq * qr + 2 * q, 2), :])
        att = jnp.concatenate(att_parts, 1).astype(jnp.float32)
        rim = jnp.concatenate(rim_parts, 1).astype(jnp.float32)
        one = jnp.where(row == 0, rim[1:2], pltpu.roll(att, 1, 0))
        two = jnp.where(row == 0, rim[0:1], jnp.where(row == 1, rim[1:2], pltpu.roll(att, 2, 0)))
        prior_one.append(one)
        prior_two.append(two)
    by_phase = []
    for s in range(STRIDE):
        total = prior_one[0] * up_ref[s, pl.ds(0, 1), :] + prior_two[0] * up_ref[s + STRIDE, pl.ds(0, 1), :]
        for t in range(1, STRIDE):
            total = total + prior_one[t] * up_ref[s, pl.ds(t, 1), :]
            total = total + prior_two[t] * up_ref[s + STRIDE, pl.ds(t, 1), :]
        by_phase.append(total)
    by_phase = jnp.concatenate(by_phase, 0)
    put_row = lax.broadcasted_iota(jnp.int32, (rows, rows), 0)
    put_col = lax.broadcasted_iota(jnp.int32, (rows, rows), 1)
    put = (put_col == (put_row % STRIDE) * lat + put_row // STRIDE).astype(jnp.bfloat16)
    branch = exact_rows(put, by_phase)
    byte_row = lax.broadcasted_iota(jnp.int32, (rows, channels), 0)
    x_copy.wait()
    out_ref[...] = x_ref[...] + jnp.where(byte_row < lim_ref[0], branch, 0.0)


def up_and_mix(limit, returned, byte_states, up_kernel, copies_n, per_t, nq, qr):
    rows, channels = byte_states.shape
    vmem = pl.BlockSpec(memory_space=pltpu.VMEM)
    return pl.pallas_call(
        functools.partial(up_kernel_fn, copies_n, per_t, nq, qr),
        out_shape=jax.ShapeDtypeStruct((rows, channels), jnp.float32),
        in_specs=[pl.BlockSpec(memory_space=pltpu.SMEM), vmem, pl.BlockSpec(memory_space=pl.ANY), vmem],
        out_specs=vmem,
        scratch_shapes=[pltpu.VMEM((rows, channels), jnp.float32), pltpu.SemaphoreType.DMA((1,))],
        cost_estimate=pl.CostEstimate(
            flops=4 * KERNEL * rows * channels + 6 * rows * rows * channels,
            bytes_accessed=8 * rows * channels + returned.size * 2,
            transcendentals=0,
        ),
    )(limit, returned, byte_states, up_kernel)


def body(byte_states, doc_length, block_ids, qk_kernel, value_kernel, up_kernel):
    rows_here, channels = byte_states.shape
    lat_dev = rows_here // STRIDE
    n_ctx = lax.axis_size("ctx")
    device = lax.axis_index("ctx")
    lat_total = lat_dev * n_ctx
    local_heads = STRIDE * channels // CHANNEL_WIDTH
    copies_n = max(1, n_ctx // local_heads)
    groups_n = n_ctx // copies_n
    head_width = STRIDE * channels // groups_n
    head_here = head_width // CHANNEL_WIDTH
    query_rows = lat_dev // copies_n
    stripe = device % copies_n

    nq = head_here
    per_t = channels // head_width
    both_local = shorten_both(byte_states, qk_kernel, value_kernel, groups_n, per_t, nq)
    kv_rows = both_local.shape[1]
    if copies_n > 1:
        both_local = jnp.broadcast_to(
            both_local[:, None], (groups_n, copies_n, kv_rows, CHANNEL_WIDTH)
        ).reshape(n_ctx, kv_rows, CHANNEL_WIDTH)
    both_all = lax.all_to_all(both_local, "ctx", split_axis=0, concat_axis=0, tiled=True)
    main_kv = both_all[:, : 2 * nq * lat_dev].reshape(n_ctx, 2 * nq, lat_dev, CHANNEL_WIDTH)
    edge = both_all[:, 2 * nq * lat_dev : 2 * nq * lat_dev + 8 * nq].astype(jnp.float32)
    edge = edge.reshape(n_ctx, 4, 2 * nq, CHANNEL_WIDTH)
    own_first = edge[:, 0] + edge[:, 1]
    from_before = edge[:, 2] + edge[:, 3]
    from_before = jnp.concatenate([jnp.zeros_like(from_before[:1]), from_before[:-1]], 0)
    first_rows = (own_first + from_before).astype(jnp.bfloat16)
    at_first = lax.broadcasted_iota(jnp.int32, main_kv.shape, 2) == 0
    main_kv = jnp.where(at_first, first_rows[:, :, None, :], main_kv)
    key_all = main_kv[:, :nq]
    value_all = main_kv[:, nq:]
    queries = key_all.reshape(n_ctx, nq, copies_n, query_rows, CHANNEL_WIDTH)[:, :, 0]
    if copies_n > 1:
        queries = lax.dynamic_index_in_dim(
            key_all.reshape(n_ctx, nq, copies_n, query_rows, CHANNEL_WIDTH), stripe, 2, keepdims=False
        )
    query_count = n_ctx * query_rows
    query_heads = queries.transpose(1, 0, 2, 3).reshape(nq, query_count, CHANNEL_WIDTH)
    key_heads = key_all.transpose(1, 0, 2, 3).reshape(nq, lat_total, CHANNEL_WIDTH)
    value_heads = value_all.transpose(1, 0, 2, 3).reshape(nq, lat_total, CHANNEL_WIDTH)
    asking_index = (
        jnp.arange(n_ctx, dtype=jnp.int32)[:, None] * lat_dev
        + stripe * query_rows
        + jnp.arange(query_rows, dtype=jnp.int32)[None, :]
    ).reshape(query_count)
    query_seg = lax.dynamic_index_in_dim(
        block_ids.reshape(n_ctx, copies_n, query_rows), stripe, 1, keepdims=False
    ).reshape(query_count)
    lat_len = doc_length[0] // STRIDE
    sharpness_divisor = jnp.log(asking_index.astype(jnp.float32) + 2.0) / (
        math.sqrt(float(CHANNEL_WIDTH)) * math.sqrt(math.log(float(lat_total)))
    )
    block_len = min(lat_total, max(512, lat_total // 16))
    block_count = lat_total // block_len

    def attend(running, key_start):
        key_block = lax.dynamic_slice_in_dim(key_heads, key_start, block_len, 1)
        value_block = lax.dynamic_slice_in_dim(value_heads, key_start, block_len, 1)
        seg_block = lax.dynamic_slice_in_dim(block_ids, key_start, block_len, 0)
        key_pos = key_start + jnp.arange(block_len, dtype=jnp.int32)
        run_max, run_sum, run_acc = running
        raw_affinity = (
            jnp.einsum("hqd,hkd->hqk", query_heads, key_block, preferred_element_type=jnp.float32)
            * sharpness_divisor[None, :, None]
        )
        visible = (
            (seg_block[None, :] <= query_seg[:, None])
            & (key_pos[None, :] < lat_len)
            & ((key_pos[None, :] != asking_index[:, None]) | (asking_index[:, None] == 0))
        )
        new_max = jnp.maximum(
            run_max, jnp.max(jnp.where(visible[None], raw_affinity, -1e30), axis=2)
        )
        weights = jnp.where(visible[None], jnp.exp(raw_affinity - new_max[:, :, None]), 0.0)
        factor = jnp.exp(run_max - new_max)
        new_sum = run_sum * factor + jnp.sum(weights, axis=2)
        new_acc = run_acc * factor[:, :, None] + jnp.einsum(
            "hqk,hkd->hqd",
            weights.astype(jnp.bfloat16),
            value_block,
            preferred_element_type=jnp.float32,
        )
        updated = (new_max, new_sum, new_acc)
        return (updated, None)

    initial = (
        jnp.full((head_here, query_count), -1e30, jnp.float32),
        jnp.zeros((head_here, query_count), jnp.float32),
        jnp.zeros((head_here, query_count, CHANNEL_WIDTH), jnp.float32),
    )
    finals, unused = lax.scan(attend, initial, jnp.arange(block_count, dtype=jnp.int32) * block_len)
    attended = (finals[2] / finals[1][:, :, None]).astype(jnp.bfloat16)
    attended = attended.reshape(nq, n_ctx, query_rows, CHANNEL_WIDTH).transpose(1, 0, 2, 3)
    rim_out = jnp.concatenate(
        [jnp.zeros((1, nq, 2, CHANNEL_WIDTH), jnp.bfloat16), attended[:-1, :, query_rows - 2 :]], 0
    )
    main_rows = nq * query_rows
    used_rows = main_rows + 2 * nq
    ret_rows = -(-used_rows // 16) * 16
    outgoing = jnp.concatenate(
        [
            attended.reshape(n_ctx, main_rows, CHANNEL_WIDTH),
            rim_out.reshape(n_ctx, 2 * nq, CHANNEL_WIDTH),
            jnp.zeros((n_ctx, ret_rows - used_rows, CHANNEL_WIDTH), jnp.bfloat16),
        ],
        1,
    )
    returned = lax.all_to_all(outgoing, "ctx", split_axis=0, concat_axis=0, tiled=True)
    limit = (doc_length[0] - device * rows_here).reshape(1).astype(jnp.int32)
    return up_and_mix(limit, returned, byte_states, up_kernel, copies_n, per_t, nq, query_rows)

def solution(mesh):
    return jax.shard_map(
        body,
        mesh=mesh,
        in_specs=(
            P(("groups", "ctx"), "head"),
            P("groups"),
            P("groups"),
            P(None, None, "head"),
            P(None, None, "head"),
            P(None, None, "head"),
        ),
        out_specs=P(("groups", "ctx"), "head"),
        check_vma=False,
    )
```

```python
import functools
import math

import jax
import jax.numpy as jnp
from jax import lax
from jax.experimental import pallas as pl
from jax.experimental.pallas import tpu as pltpu
from jax.sharding import PartitionSpec as P

CHANNEL_WIDTH = 128
STRIDE = 4
KERNEL = 8


def shifted(x, axis, by):
    devices = lax.axis_size(axis)
    pairs = [(i, i + by) for i in range(devices) if 0 <= i + by < devices]
    return lax.ppermute(x, axis, pairs)


def three_bf16(value):
    hi = value.astype(jnp.bfloat16)
    rest = value - hi.astype(jnp.float32)
    mid = rest.astype(jnp.bfloat16)
    lo = (rest - mid.astype(jnp.float32)).astype(jnp.bfloat16)
    return hi, mid, lo


def exact_rows(select, value):
    total = None
    for piece in three_bf16(value):
        part = jnp.dot(select, piece, preferred_element_type=jnp.float32)
        total = part if total is None else total + part
    return total


def split_pair(value):
    hi = value.astype(jnp.bfloat16)
    lo = (value - hi.astype(jnp.float32)).astype(jnp.bfloat16)
    return hi, lo


def shorten_kernel(per_t, nq, x_ref, qk_ref, vk_ref, out_ref):
    rows, channels = x_ref.shape
    lat = rows // STRIDE
    lanes = CHANNEL_WIDTH
    blocks = channels // lanes
    pick_row = lax.broadcasted_iota(jnp.int32, (rows, rows), 0)
    pick_col = lax.broadcasted_iota(jnp.int32, (rows, rows), 1)
    pick = (pick_col == (pick_row % lat) * STRIDE + pick_row // lat).astype(jnp.bfloat16)
    by_phase = exact_rows(pick, x_ref[...])
    phase = [by_phase[s * lat : (s + 1) * lat] for s in range(STRIDE)]
    first_row = lax.broadcasted_iota(jnp.int32, (lat, channels), 0) == 0
    edge_rows = -(-6 * nq // 8) * 8
    edge_row = lax.broadcasted_iota(jnp.int32, (edge_rows, lanes), 0)
    edge = [jnp.zeros((edge_rows, lanes), jnp.float32) for _ in range(STRIDE * per_t)]
    for which, kern_ref in enumerate((qk_ref, vk_ref)):
        for t in range(STRIDE):
            own = phase[0] * kern_ref[STRIDE, pl.ds(t, 1), :]
            before = phase[0] * kern_ref[0, pl.ds(t, 1), :]
            for s in range(1, STRIDE):
                own = own + phase[s] * kern_ref[STRIDE + s, pl.ds(t, 1), :]
                before = before + phase[s] * kern_ref[s, pl.ds(t, 1), :]
            total = own + jnp.where(first_row, 0.0, pltpu.roll(before, 1, 0))
            total = total.astype(jnp.bfloat16)
            own_hi, own_lo = split_pair(own[0:1])
            next_hi, next_lo = split_pair(before[lat - 1 : lat])
            for block in range(blocks):
                lane = slice(block * lanes, (block + 1) * lanes)
                g = t * per_t + block // nq
                slot = which * nq + block % nq
                out_ref[g, pl.ds(slot * lat, lat), :] = total[:, lane]
                for e, piece in enumerate((own_lo, next_hi, next_lo)):
                    edge[g] = jnp.where(edge_row == e * 2 * nq + slot, piece[:, lane].astype(jnp.float32), edge[g])
    for g in range(STRIDE * per_t):
        out_ref[g, pl.ds(2 * nq * lat, 6 * nq), :] = edge[g][: 6 * nq].astype(jnp.bfloat16)


def shorten_both(byte_states, qk_kernel, value_kernel, groups_n, per_t, nq):
    rows, channels = byte_states.shape
    lat = rows // STRIDE
    kv_rows = 2 * nq * lat + 6 * nq
    vmem = pl.BlockSpec(memory_space=pltpu.VMEM)
    return pl.pallas_call(
        functools.partial(shorten_kernel, per_t, nq),
        out_shape=jax.ShapeDtypeStruct((groups_n, kv_rows, CHANNEL_WIDTH), jnp.bfloat16),
        in_specs=[vmem] * 3,
        out_specs=vmem,
        cost_estimate=pl.CostEstimate(
            flops=4 * KERNEL * rows * channels + 6 * rows * rows * channels,
            bytes_accessed=4 * rows * channels + 2 * KERNEL * STRIDE * channels * 4 + 2 * rows * channels * 2,
            transcendentals=0,
        ),
    )(byte_states, qk_kernel, value_kernel)


def up_kernel_fn(copies_n, per_t, nq, qr, lim_ref, ret_ref, x_ref, up_ref, out_ref):
    rows, channels = x_ref.shape
    lat = rows // STRIDE
    lanes = CHANNEL_WIDTH
    blocks = channels // lanes
    row = lax.broadcasted_iota(jnp.int32, (lat, channels), 0)
    prior_one = []
    prior_two = []
    for t in range(STRIDE):
        att_parts = []
        rim_parts = []
        for block in range(blocks):
            g = t * per_t + block // nq
            q = block % nq
            pieces = [ret_ref[g * copies_n + s, pl.ds(q * qr, qr), :] for s in range(copies_n)]
            att_parts.append(pieces[0] if copies_n == 1 else jnp.concatenate(pieces, 0))
            rim_parts.append(ret_ref[g * copies_n + copies_n - 1, pl.ds(nq * qr + 2 * q, 2), :])
        att = jnp.concatenate(att_parts, 1).astype(jnp.float32)
        rim = jnp.concatenate(rim_parts, 1).astype(jnp.float32)
        one = jnp.where(row == 0, rim[1:2], pltpu.roll(att, 1, 0))
        two = jnp.where(row == 0, rim[0:1], jnp.where(row == 1, rim[1:2], pltpu.roll(att, 2, 0)))
        prior_one.append(one)
        prior_two.append(two)
    by_phase = []
    for s in range(STRIDE):
        total = prior_one[0] * up_ref[s, pl.ds(0, 1), :] + prior_two[0] * up_ref[s + STRIDE, pl.ds(0, 1), :]
        for t in range(1, STRIDE):
            total = total + prior_one[t] * up_ref[s, pl.ds(t, 1), :]
            total = total + prior_two[t] * up_ref[s + STRIDE, pl.ds(t, 1), :]
        by_phase.append(total)
    by_phase = jnp.concatenate(by_phase, 0)
    put_row = lax.broadcasted_iota(jnp.int32, (rows, rows), 0)
    put_col = lax.broadcasted_iota(jnp.int32, (rows, rows), 1)
    put = (put_col == (put_row % STRIDE) * lat + put_row // STRIDE).astype(jnp.bfloat16)
    branch = exact_rows(put, by_phase)
    byte_row = lax.broadcasted_iota(jnp.int32, (rows, channels), 0)
    out_ref[...] = x_ref[...] + jnp.where(byte_row < lim_ref[0], branch, 0.0)


def up_and_mix(limit, returned, byte_states, up_kernel, copies_n, per_t, nq, qr):
    rows, channels = byte_states.shape
    vmem = pl.BlockSpec(memory_space=pltpu.VMEM)
    return pl.pallas_call(
        functools.partial(up_kernel_fn, copies_n, per_t, nq, qr),
        out_shape=jax.ShapeDtypeStruct((rows, channels), jnp.float32),
        in_specs=[pl.BlockSpec(memory_space=pltpu.SMEM), vmem, vmem, vmem],
        out_specs=vmem,
        cost_estimate=pl.CostEstimate(
            flops=4 * KERNEL * rows * channels + 6 * rows * rows * channels,
            bytes_accessed=8 * rows * channels + returned.size * 2,
            transcendentals=0,
        ),
    )(limit, returned, byte_states, up_kernel)


def body(byte_states, doc_length, block_ids, qk_kernel, value_kernel, up_kernel):
    rows_here, channels = byte_states.shape
    lat_dev = rows_here // STRIDE
    n_ctx = lax.axis_size("ctx")
    device = lax.axis_index("ctx")
    lat_total = lat_dev * n_ctx
    local_heads = STRIDE * channels // CHANNEL_WIDTH
    copies_n = max(1, n_ctx // local_heads)
    groups_n = n_ctx // copies_n
    head_width = STRIDE * channels // groups_n
    head_here = head_width // CHANNEL_WIDTH
    query_rows = lat_dev // copies_n
    stripe = device % copies_n

    nq = head_here
    per_t = channels // head_width
    both_local = shorten_both(byte_states, qk_kernel, value_kernel, groups_n, per_t, nq)
    kv_rows = both_local.shape[1]
    if copies_n > 1:
        both_local = jnp.broadcast_to(
            both_local[:, None], (groups_n, copies_n, kv_rows, CHANNEL_WIDTH)
        ).reshape(n_ctx, kv_rows, CHANNEL_WIDTH)
    both_all = lax.all_to_all(both_local, "ctx", split_axis=0, concat_axis=0, tiled=True)
    main_kv = both_all[:, : 2 * nq * lat_dev].reshape(n_ctx, 2 * nq, lat_dev, CHANNEL_WIDTH)
    edge = both_all[:, 2 * nq * lat_dev : 2 * nq * lat_dev + 6 * nq].astype(jnp.float32)
    edge = edge.reshape(n_ctx, 3, 2 * nq, CHANNEL_WIDTH)
    own_first = main_kv[:, :, 0].astype(jnp.float32) + edge[:, 0]
    from_before = edge[:, 1] + edge[:, 2]
    from_before = jnp.concatenate([jnp.zeros_like(from_before[:1]), from_before[:-1]], 0)
    first_rows = (own_first + from_before).astype(jnp.bfloat16)
    at_first = lax.broadcasted_iota(jnp.int32, main_kv.shape, 2) == 0
    main_kv = jnp.where(at_first, first_rows[:, :, None, :], main_kv)
    key_all = main_kv[:, :nq]
    value_all = main_kv[:, nq:]
    queries = key_all.reshape(n_ctx, nq, copies_n, query_rows, CHANNEL_WIDTH)[:, :, 0]
    if copies_n > 1:
        queries = lax.dynamic_index_in_dim(
            key_all.reshape(n_ctx, nq, copies_n, query_rows, CHANNEL_WIDTH), stripe, 2, keepdims=False
        )
    query_count = n_ctx * query_rows
    query_heads = queries.transpose(1, 0, 2, 3).reshape(nq, query_count, CHANNEL_WIDTH)
    key_heads = key_all.transpose(1, 0, 2, 3).reshape(nq, lat_total, CHANNEL_WIDTH)
    value_heads = value_all.transpose(1, 0, 2, 3).reshape(nq, lat_total, CHANNEL_WIDTH)
    asking_index = (
        jnp.arange(n_ctx, dtype=jnp.int32)[:, None] * lat_dev
        + stripe * query_rows
        + jnp.arange(query_rows, dtype=jnp.int32)[None, :]
    ).reshape(query_count)
    query_seg = lax.dynamic_index_in_dim(
        block_ids.reshape(n_ctx, copies_n, query_rows), stripe, 1, keepdims=False
    ).reshape(query_count)
    lat_len = doc_length[0] // STRIDE
    sharpness_divisor = jnp.log(asking_index.astype(jnp.float32) + 2.0) / (
        math.sqrt(float(CHANNEL_WIDTH)) * math.sqrt(math.log(float(lat_total)))
    )
    block_len = min(lat_total, max(512, lat_total // 16))
    block_count = lat_total // block_len

    def attend(running, key_start):
        key_block = lax.dynamic_slice_in_dim(key_heads, key_start, block_len, 1)
        value_block = lax.dynamic_slice_in_dim(value_heads, key_start, block_len, 1)
        seg_block = lax.dynamic_slice_in_dim(block_ids, key_start, block_len, 0)
        key_pos = key_start + jnp.arange(block_len, dtype=jnp.int32)
        run_max, run_sum, run_acc = running
        raw_affinity = (
            jnp.einsum("hqd,hkd->hqk", query_heads, key_block, preferred_element_type=jnp.float32)
            * sharpness_divisor[None, :, None]
        )
        visible = (
            (seg_block[None, :] <= query_seg[:, None])
            & (key_pos[None, :] < lat_len)
            & ((key_pos[None, :] != asking_index[:, None]) | (asking_index[:, None] == 0))
        )
        new_max = jnp.maximum(
            run_max, jnp.max(jnp.where(visible[None], raw_affinity, -1e30), axis=2)
        )
        weights = jnp.where(visible[None], jnp.exp(raw_affinity - new_max[:, :, None]), 0.0)
        factor = jnp.exp(run_max - new_max)
        new_sum = run_sum * factor + jnp.sum(weights, axis=2)
        new_acc = run_acc * factor[:, :, None] + jnp.einsum(
            "hqk,hkd->hqd",
            weights.astype(jnp.bfloat16),
            value_block,
            preferred_element_type=jnp.float32,
        )
        updated = (new_max, new_sum, new_acc)
        return (updated, None)

    initial = (
        jnp.full((head_here, query_count), -1e30, jnp.float32),
        jnp.zeros((head_here, query_count), jnp.float32),
        jnp.zeros((head_here, query_count, CHANNEL_WIDTH), jnp.float32),
    )
    finals, unused = lax.scan(attend, initial, jnp.arange(block_count, dtype=jnp.int32) * block_len)
    attended = (finals[2] / finals[1][:, :, None]).astype(jnp.bfloat16)
    attended = attended.reshape(nq, n_ctx, query_rows, CHANNEL_WIDTH).transpose(1, 0, 2, 3)
    rim_out = jnp.concatenate(
        [jnp.zeros((1, nq, 2, CHANNEL_WIDTH), jnp.bfloat16), attended[:-1, :, query_rows - 2 :]], 0
    )
    main_rows = nq * query_rows
    used_rows = main_rows + 2 * nq
    ret_rows = used_rows
    outgoing = jnp.concatenate(
        [
            attended.reshape(n_ctx, main_rows, CHANNEL_WIDTH),
            rim_out.reshape(n_ctx, 2 * nq, CHANNEL_WIDTH),
            jnp.zeros((n_ctx, ret_rows - used_rows, CHANNEL_WIDTH), jnp.bfloat16),
        ],
        1,
    )
    returned = lax.all_to_all(outgoing, "ctx", split_axis=0, concat_axis=0, tiled=True)
    limit = (doc_length[0] - device * rows_here).reshape(1).astype(jnp.int32)
    return up_and_mix(limit, returned, byte_states, up_kernel, copies_n, per_t, nq, query_rows)

def solution(mesh):
    return jax.shard_map(
        body,
        mesh=mesh,
        in_specs=(
            P(("groups", "ctx"), "head"),
            P("groups"),
            P("groups"),
            P(None, None, "head"),
            P(None, None, "head"),
            P(None, None, "head"),
        ),
        out_specs=P(("groups", "ctx"), "head"),
        check_vma=False,
    )
```

```python
import functools
import math

import jax
import jax.numpy as jnp
from jax import lax
from jax.experimental import pallas as pl
from jax.experimental.pallas import tpu as pltpu
from jax.sharding import PartitionSpec as P

CHANNEL_WIDTH = 128
STRIDE = 4
KERNEL = 8


def shifted(x, axis, by):
    devices = lax.axis_size(axis)
    pairs = [(i, i + by) for i in range(devices) if 0 <= i + by < devices]
    return lax.ppermute(x, axis, pairs)


def three_bf16(value):
    hi = value.astype(jnp.bfloat16)
    rest = value - hi.astype(jnp.float32)
    mid = rest.astype(jnp.bfloat16)
    lo = (rest - mid.astype(jnp.float32)).astype(jnp.bfloat16)
    return hi, mid, lo


def exact_rows(select, value):
    total = None
    for piece in three_bf16(value):
        part = jnp.dot(select, piece, preferred_element_type=jnp.float32)
        total = part if total is None else total + part
    return total


def split_pair(value):
    hi = value.astype(jnp.bfloat16)
    lo = (value - hi.astype(jnp.float32)).astype(jnp.bfloat16)
    return hi, lo


def shorten_kernel(per_t, nq, x_ref, qk_ref, vk_ref, out_ref):
    rows, channels = x_ref.shape
    lat = rows // STRIDE
    lanes = CHANNEL_WIDTH
    blocks = channels // lanes
    pick_row = lax.broadcasted_iota(jnp.int32, (rows, rows), 0)
    pick_col = lax.broadcasted_iota(jnp.int32, (rows, rows), 1)
    pick = (pick_col == (pick_row % lat) * STRIDE + pick_row // lat).astype(jnp.bfloat16)
    by_phase = exact_rows(pick, x_ref[...])
    phase = [by_phase[s * lat : (s + 1) * lat] for s in range(STRIDE)]
    first_row = lax.broadcasted_iota(jnp.int32, (lat, channels), 0) == 0
    edge_rows = -(-6 * nq // 8) * 8
    edge_row = lax.broadcasted_iota(jnp.int32, (edge_rows, lanes), 0)
    edge = [jnp.zeros((edge_rows, lanes), jnp.float32) for _ in range(STRIDE * per_t)]
    for which, kern_ref in enumerate((qk_ref, vk_ref)):
        for t in range(STRIDE):
            own = phase[0] * kern_ref[STRIDE, pl.ds(t, 1), :]
            before = phase[0] * kern_ref[0, pl.ds(t, 1), :]
            for s in range(1, STRIDE):
                own = own + phase[s] * kern_ref[STRIDE + s, pl.ds(t, 1), :]
                before = before + phase[s] * kern_ref[s, pl.ds(t, 1), :]
            total = own + jnp.where(first_row, 0.0, pltpu.roll(before, 1, 0))
            total = total.astype(jnp.bfloat16)
            own_hi, own_lo = split_pair(own[0:1])
            next_hi, next_lo = split_pair(before[lat - 1 : lat])
            for block in range(blocks):
                lane = slice(block * lanes, (block + 1) * lanes)
                g = t * per_t + block // nq
                slot = which * nq + block % nq
                out_ref[g, pl.ds(slot * lat, lat), :] = total[:, lane]
                for e, piece in enumerate((own_lo, next_hi, next_lo)):
                    edge[g] = jnp.where(edge_row == e * 2 * nq + slot, piece[:, lane].astype(jnp.float32), edge[g])
    for g in range(STRIDE * per_t):
        out_ref[g, pl.ds(2 * nq * lat, 6 * nq), :] = edge[g][: 6 * nq].astype(jnp.bfloat16)


def shorten_both(byte_states, qk_kernel, value_kernel, groups_n, per_t, nq):
    rows, channels = byte_states.shape
    lat = rows // STRIDE
    kv_rows = 2 * nq * lat + 6 * nq
    vmem = pl.BlockSpec(memory_space=pltpu.VMEM)
    return pl.pallas_call(
        functools.partial(shorten_kernel, per_t, nq),
        out_shape=jax.ShapeDtypeStruct((groups_n, kv_rows, CHANNEL_WIDTH), jnp.bfloat16),
        in_specs=[vmem] * 3,
        out_specs=vmem,
        cost_estimate=pl.CostEstimate(
            flops=4 * KERNEL * rows * channels + 6 * rows * rows * channels,
            bytes_accessed=4 * rows * channels + 2 * KERNEL * STRIDE * channels * 4 + 2 * rows * channels * 2,
            transcendentals=0,
        ),
    )(byte_states, qk_kernel, value_kernel)


def up_kernel_fn(copies_n, per_t, nq, qr, lim_ref, ret_ref, x_ref, up_ref, out_ref):
    rows, channels = x_ref.shape
    lat = rows // STRIDE
    lanes = CHANNEL_WIDTH
    blocks = channels // lanes
    row = lax.broadcasted_iota(jnp.int32, (lat, channels), 0)
    prior_one = []
    prior_two = []
    for t in range(STRIDE):
        att_parts = []
        rim_parts = []
        for block in range(blocks):
            g = t * per_t + block // nq
            q = block % nq
            pieces = [ret_ref[g * copies_n + s, pl.ds(q * qr, qr), :] for s in range(copies_n)]
            att_parts.append(pieces[0] if copies_n == 1 else jnp.concatenate(pieces, 0))
            rim_parts.append(ret_ref[g * copies_n + copies_n - 1, pl.ds(nq * qr + 2 * q, 2), :])
        att = jnp.concatenate(att_parts, 1).astype(jnp.float32)
        rim = jnp.concatenate(rim_parts, 1).astype(jnp.float32)
        one = jnp.where(row == 0, rim[1:2], pltpu.roll(att, 1, 0))
        two = jnp.where(row == 0, rim[0:1], jnp.where(row == 1, rim[1:2], pltpu.roll(att, 2, 0)))
        prior_one.append(one)
        prior_two.append(two)
    by_phase = []
    for s in range(STRIDE):
        total = prior_one[0] * up_ref[s, pl.ds(0, 1), :] + prior_two[0] * up_ref[s + STRIDE, pl.ds(0, 1), :]
        for t in range(1, STRIDE):
            total = total + prior_one[t] * up_ref[s, pl.ds(t, 1), :]
            total = total + prior_two[t] * up_ref[s + STRIDE, pl.ds(t, 1), :]
        by_phase.append(total)
    by_phase = jnp.concatenate(by_phase, 0)
    put_row = lax.broadcasted_iota(jnp.int32, (rows, rows), 0)
    put_col = lax.broadcasted_iota(jnp.int32, (rows, rows), 1)
    put = (put_col == (put_row % STRIDE) * lat + put_row // STRIDE).astype(jnp.bfloat16)
    branch = exact_rows(put, by_phase)
    byte_row = lax.broadcasted_iota(jnp.int32, (rows, channels), 0)
    out_ref[...] = x_ref[...] + jnp.where(byte_row < lim_ref[0], branch, 0.0)


def up_and_mix(limit, returned, byte_states, up_kernel, copies_n, per_t, nq, qr):
    rows, channels = byte_states.shape
    vmem = pl.BlockSpec(memory_space=pltpu.VMEM)
    return pl.pallas_call(
        functools.partial(up_kernel_fn, copies_n, per_t, nq, qr),
        out_shape=jax.ShapeDtypeStruct((rows, channels), jnp.float32),
        in_specs=[pl.BlockSpec(memory_space=pltpu.SMEM), vmem, vmem, vmem],
        out_specs=vmem,
        cost_estimate=pl.CostEstimate(
            flops=4 * KERNEL * rows * channels + 6 * rows * rows * channels,
            bytes_accessed=8 * rows * channels + returned.size * 4,
            transcendentals=0,
        ),
    )(limit, returned, byte_states, up_kernel)


def body(byte_states, doc_length, block_ids, qk_kernel, value_kernel, up_kernel):
    rows_here, channels = byte_states.shape
    lat_dev = rows_here // STRIDE
    n_ctx = lax.axis_size("ctx")
    device = lax.axis_index("ctx")
    lat_total = lat_dev * n_ctx
    local_heads = STRIDE * channels // CHANNEL_WIDTH
    copies_n = max(1, n_ctx // local_heads)
    groups_n = n_ctx // copies_n
    head_width = STRIDE * channels // groups_n
    head_here = head_width // CHANNEL_WIDTH
    query_rows = lat_dev // copies_n
    stripe = device % copies_n

    nq = head_here
    per_t = channels // head_width
    both_local = shorten_both(byte_states, qk_kernel, value_kernel, groups_n, per_t, nq)
    kv_rows = both_local.shape[1]
    if copies_n > 1:
        both_local = jnp.broadcast_to(
            both_local[:, None], (groups_n, copies_n, kv_rows, CHANNEL_WIDTH)
        ).reshape(n_ctx, kv_rows, CHANNEL_WIDTH)
    both_all = lax.all_to_all(both_local, "ctx", split_axis=0, concat_axis=0, tiled=True)
    main_kv = both_all[:, : 2 * nq * lat_dev].reshape(n_ctx, 2 * nq, lat_dev, CHANNEL_WIDTH)
    edge = both_all[:, 2 * nq * lat_dev : 2 * nq * lat_dev + 6 * nq].astype(jnp.float32)
    edge = edge.reshape(n_ctx, 3, 2 * nq, CHANNEL_WIDTH)
    own_first = main_kv[:, :, 0].astype(jnp.float32) + edge[:, 0]
    from_before = edge[:, 1] + edge[:, 2]
    from_before = jnp.concatenate([jnp.zeros_like(from_before[:1]), from_before[:-1]], 0)
    first_rows = (own_first + from_before).astype(jnp.bfloat16)
    at_first = lax.broadcasted_iota(jnp.int32, main_kv.shape, 2) == 0
    main_kv = jnp.where(at_first, first_rows[:, :, None, :], main_kv)
    key_all = main_kv[:, :nq]
    value_all = main_kv[:, nq:]
    queries = key_all.reshape(n_ctx, nq, copies_n, query_rows, CHANNEL_WIDTH)[:, :, 0]
    if copies_n > 1:
        queries = lax.dynamic_index_in_dim(
            key_all.reshape(n_ctx, nq, copies_n, query_rows, CHANNEL_WIDTH), stripe, 2, keepdims=False
        )
    query_count = n_ctx * query_rows
    query_heads = queries.transpose(1, 0, 2, 3).reshape(nq, query_count, CHANNEL_WIDTH)
    key_heads = key_all.transpose(1, 0, 2, 3).reshape(nq, lat_total, CHANNEL_WIDTH)
    value_heads = value_all.transpose(1, 0, 2, 3).reshape(nq, lat_total, CHANNEL_WIDTH)
    asking_index = (
        jnp.arange(n_ctx, dtype=jnp.int32)[:, None] * lat_dev
        + stripe * query_rows
        + jnp.arange(query_rows, dtype=jnp.int32)[None, :]
    ).reshape(query_count)
    query_seg = lax.dynamic_index_in_dim(
        block_ids.reshape(n_ctx, copies_n, query_rows), stripe, 1, keepdims=False
    ).reshape(query_count)
    lat_len = doc_length[0] // STRIDE
    sharpness_divisor = jnp.log(asking_index.astype(jnp.float32) + 2.0) / (
        math.sqrt(float(CHANNEL_WIDTH)) * math.sqrt(math.log(float(lat_total)))
    )
    block_len = min(lat_total, max(512, lat_total // 16))
    block_count = lat_total // block_len

    def attend(running, key_start):
        key_block = lax.dynamic_slice_in_dim(key_heads, key_start, block_len, 1)
        value_block = lax.dynamic_slice_in_dim(value_heads, key_start, block_len, 1)
        seg_block = lax.dynamic_slice_in_dim(block_ids, key_start, block_len, 0)
        key_pos = key_start + jnp.arange(block_len, dtype=jnp.int32)
        run_max, run_sum, run_acc = running
        raw_affinity = (
            jnp.einsum("hqd,hkd->hqk", query_heads, key_block, preferred_element_type=jnp.float32)
            * sharpness_divisor[None, :, None]
        )
        visible = (
            (seg_block[None, :] <= query_seg[:, None])
            & (key_pos[None, :] < lat_len)
            & ((key_pos[None, :] != asking_index[:, None]) | (asking_index[:, None] == 0))
        )
        new_max = jnp.maximum(
            run_max, jnp.max(jnp.where(visible[None], raw_affinity, -1e30), axis=2)
        )
        weights = jnp.where(visible[None], jnp.exp(raw_affinity - new_max[:, :, None]), 0.0)
        factor = jnp.exp(run_max - new_max)
        new_sum = run_sum * factor + jnp.sum(weights, axis=2)
        new_acc = run_acc * factor[:, :, None] + jnp.einsum(
            "hqk,hkd->hqd",
            weights.astype(jnp.bfloat16),
            value_block,
            preferred_element_type=jnp.float32,
        )
        updated = (new_max, new_sum, new_acc)
        return (updated, None)

    initial = (
        jnp.full((head_here, query_count), -1e30, jnp.float32),
        jnp.zeros((head_here, query_count), jnp.float32),
        jnp.zeros((head_here, query_count, CHANNEL_WIDTH), jnp.float32),
    )
    finals, unused = lax.scan(attend, initial, jnp.arange(block_count, dtype=jnp.int32) * block_len)
    attended = (finals[2] / finals[1][:, :, None]).astype(jnp.bfloat16)
    attended = attended.reshape(nq, n_ctx, query_rows, CHANNEL_WIDTH).transpose(1, 0, 2, 3)
    rim_out = jnp.concatenate(
        [jnp.zeros((1, nq, 2, CHANNEL_WIDTH), jnp.bfloat16), attended[:-1, :, query_rows - 2 :]], 0
    )
    main_rows = nq * query_rows
    used_rows = main_rows + 2 * nq
    ret_rows = used_rows
    outgoing = jnp.concatenate(
        [
            attended.reshape(n_ctx, main_rows, CHANNEL_WIDTH),
            rim_out.reshape(n_ctx, 2 * nq, CHANNEL_WIDTH),
            jnp.zeros((n_ctx, ret_rows - used_rows, CHANNEL_WIDTH), jnp.bfloat16),
        ],
        1,
    )
    returned = lax.all_to_all(outgoing, "ctx", split_axis=0, concat_axis=0, tiled=True)
    limit = (doc_length[0] - device * rows_here).reshape(1).astype(jnp.int32)
    return up_and_mix(
        limit, returned.astype(jnp.float32), byte_states, up_kernel, copies_n, per_t, nq, query_rows
    )

def solution(mesh):
    return jax.shard_map(
        body,
        mesh=mesh,
        in_specs=(
            P(("groups", "ctx"), "head"),
            P("groups"),
            P("groups"),
            P(None, None, "head"),
            P(None, None, "head"),
            P(None, None, "head"),
        ),
        out_specs=P(("groups", "ctx"), "head"),
        check_vma=False,
    )
```

```python
import functools
import math

import jax
import jax.numpy as jnp
from jax import lax
from jax.experimental import pallas as pl
from jax.experimental.pallas import tpu as pltpu
from jax.sharding import PartitionSpec as P

CHANNEL_WIDTH = 128
STRIDE = 4
KERNEL = 8


def shifted(x, axis, by):
    devices = lax.axis_size(axis)
    pairs = [(i, i + by) for i in range(devices) if 0 <= i + by < devices]
    return lax.ppermute(x, axis, pairs)


def three_bf16(value):
    hi = value.astype(jnp.bfloat16)
    rest = value - hi.astype(jnp.float32)
    mid = rest.astype(jnp.bfloat16)
    lo = (rest - mid.astype(jnp.float32)).astype(jnp.bfloat16)
    return hi, mid, lo


def exact_rows(select, value):
    total = None
    for piece in three_bf16(value):
        part = jnp.dot(select, piece, preferred_element_type=jnp.float32)
        total = part if total is None else total + part
    return total


def split_pair(value):
    hi = value.astype(jnp.bfloat16)
    lo = (value - hi.astype(jnp.float32)).astype(jnp.bfloat16)
    return hi, lo


def shorten_kernel(per_t, nq, x_ref, qk_ref, vk_ref, out_ref, taps_ref):
    rows, channels = x_ref.shape
    lat = rows // STRIDE
    lanes = CHANNEL_WIDTH
    blocks = channels // lanes
    pick_row = lax.broadcasted_iota(jnp.int32, (rows, rows), 0)
    pick_col = lax.broadcasted_iota(jnp.int32, (rows, rows), 1)
    pick = (pick_col == (pick_row % lat) * STRIDE + pick_row // lat).astype(jnp.bfloat16)
    by_phase = exact_rows(pick, x_ref[...])
    first_row = lax.broadcasted_iota(jnp.int32, (lat, channels), 0) == 0
    phase = []
    for s in range(STRIDE):
        current = by_phase[s * lat : (s + 1) * lat]
        phase.append(current)
        taps_ref[STRIDE + s] = current
        taps_ref[s] = jnp.where(first_row, 0.0, pltpu.roll(current, 1, 0))
    kerns = (qk_ref, vk_ref)
    chunk = 16

    def rows_of(r, carry):
        start = pl.multiple_of(r * chunk, chunk)
        for block in range(blocks):
            lane = pl.ds(block * lanes, lanes)
            taps = [taps_ref[k, pl.ds(start, chunk), lane] for k in range(KERNEL)]
            for which, kern_ref in enumerate(kerns):
                slot = which * nq + block % nq
                for t in range(STRIDE):
                    total = taps[0] * kern_ref[0, pl.ds(t, 1), lane]
                    for k in range(1, KERNEL):
                        total = total + taps[k] * kern_ref[k, pl.ds(t, 1), lane]
                    g = t * per_t + block // nq
                    out_ref[g, pl.ds(pl.multiple_of(slot * lat + start, chunk), chunk), :] = total.astype(
                        jnp.bfloat16
                    )
        return carry

    lax.fori_loop(0, lat // chunk, rows_of, 0)
    edge_rows = -(-6 * nq // 8) * 8
    edge_row = lax.broadcasted_iota(jnp.int32, (edge_rows, lanes), 0)
    edge = [jnp.zeros((edge_rows, lanes), jnp.float32) for _ in range(STRIDE * per_t)]
    for which, kern_ref in enumerate(kerns):
        for t in range(STRIDE):
            own = phase[0][0:1] * kern_ref[STRIDE, pl.ds(t, 1), :]
            before = phase[0][lat - 1 : lat] * kern_ref[0, pl.ds(t, 1), :]
            for s in range(1, STRIDE):
                own = own + phase[s][0:1] * kern_ref[STRIDE + s, pl.ds(t, 1), :]
                before = before + phase[s][lat - 1 : lat] * kern_ref[s, pl.ds(t, 1), :]
            own_hi, own_lo = split_pair(own)
            next_hi, next_lo = split_pair(before)
            for block in range(blocks):
                lane = slice(block * lanes, (block + 1) * lanes)
                g = t * per_t + block // nq
                slot = which * nq + block % nq
                for e, piece in enumerate((own_lo, next_hi, next_lo)):
                    edge[g] = jnp.where(edge_row == e * 2 * nq + slot, piece[:, lane].astype(jnp.float32), edge[g])
    for g in range(STRIDE * per_t):
        out_ref[g, pl.ds(2 * nq * lat, 6 * nq), :] = edge[g][: 6 * nq].astype(jnp.bfloat16)


def shorten_both(byte_states, qk_kernel, value_kernel, groups_n, per_t, nq):
    rows, channels = byte_states.shape
    lat = rows // STRIDE
    kv_rows = 2 * nq * lat + 6 * nq
    vmem = pl.BlockSpec(memory_space=pltpu.VMEM)
    return pl.pallas_call(
        functools.partial(shorten_kernel, per_t, nq),
        out_shape=jax.ShapeDtypeStruct((groups_n, kv_rows, CHANNEL_WIDTH), jnp.bfloat16),
        in_specs=[vmem] * 3,
        out_specs=vmem,
        scratch_shapes=[pltpu.VMEM((KERNEL, lat, channels), jnp.float32)],
        cost_estimate=pl.CostEstimate(
            flops=4 * KERNEL * rows * channels + 6 * rows * rows * channels,
            bytes_accessed=4 * rows * channels + 2 * KERNEL * STRIDE * channels * 4 + 2 * rows * channels * 2,
            transcendentals=0,
        ),
    )(byte_states, qk_kernel, value_kernel)


def up_kernel_fn(copies_n, per_t, nq, qr, lim_ref, ret_ref, x_ref, up_ref, out_ref):
    rows, channels = x_ref.shape
    lat = rows // STRIDE
    lanes = CHANNEL_WIDTH
    blocks = channels // lanes
    row = lax.broadcasted_iota(jnp.int32, (lat, channels), 0)
    prior_one = []
    prior_two = []
    for t in range(STRIDE):
        att_parts = []
        rim_parts = []
        for block in range(blocks):
            g = t * per_t + block // nq
            q = block % nq
            pieces = [ret_ref[g * copies_n + s, pl.ds(q * qr, qr), :] for s in range(copies_n)]
            att_parts.append(pieces[0] if copies_n == 1 else jnp.concatenate(pieces, 0))
            rim_parts.append(ret_ref[g * copies_n + copies_n - 1, pl.ds(nq * qr + 2 * q, 2), :])
        att = jnp.concatenate(att_parts, 1).astype(jnp.float32)
        rim = jnp.concatenate(rim_parts, 1).astype(jnp.float32)
        one = jnp.where(row == 0, rim[1:2], pltpu.roll(att, 1, 0))
        two = jnp.where(row == 0, rim[0:1], jnp.where(row == 1, rim[1:2], pltpu.roll(att, 2, 0)))
        prior_one.append(one)
        prior_two.append(two)
    by_phase = []
    for s in range(STRIDE):
        total = prior_one[0] * up_ref[s, pl.ds(0, 1), :] + prior_two[0] * up_ref[s + STRIDE, pl.ds(0, 1), :]
        for t in range(1, STRIDE):
            total = total + prior_one[t] * up_ref[s, pl.ds(t, 1), :]
            total = total + prior_two[t] * up_ref[s + STRIDE, pl.ds(t, 1), :]
        by_phase.append(total)
    by_phase = jnp.concatenate(by_phase, 0)
    put_row = lax.broadcasted_iota(jnp.int32, (rows, rows), 0)
    put_col = lax.broadcasted_iota(jnp.int32, (rows, rows), 1)
    put = (put_col == (put_row % STRIDE) * lat + put_row // STRIDE).astype(jnp.bfloat16)
    branch = exact_rows(put, by_phase)
    byte_row = lax.broadcasted_iota(jnp.int32, (rows, channels), 0)
    out_ref[...] = x_ref[...] + jnp.where(byte_row < lim_ref[0], branch, 0.0)


def up_and_mix(limit, returned, byte_states, up_kernel, copies_n, per_t, nq, qr):
    rows, channels = byte_states.shape
    vmem = pl.BlockSpec(memory_space=pltpu.VMEM)
    return pl.pallas_call(
        functools.partial(up_kernel_fn, copies_n, per_t, nq, qr),
        out_shape=jax.ShapeDtypeStruct((rows, channels), jnp.float32),
        in_specs=[pl.BlockSpec(memory_space=pltpu.SMEM), vmem, vmem, vmem],
        out_specs=vmem,
        cost_estimate=pl.CostEstimate(
            flops=4 * KERNEL * rows * channels + 6 * rows * rows * channels,
            bytes_accessed=8 * rows * channels + returned.size * 2,
            transcendentals=0,
        ),
    )(limit, returned, byte_states, up_kernel)


def body(byte_states, doc_length, block_ids, qk_kernel, value_kernel, up_kernel):
    rows_here, channels = byte_states.shape
    lat_dev = rows_here // STRIDE
    n_ctx = lax.axis_size("ctx")
    device = lax.axis_index("ctx")
    lat_total = lat_dev * n_ctx
    local_heads = STRIDE * channels // CHANNEL_WIDTH
    copies_n = max(1, n_ctx // local_heads)
    groups_n = n_ctx // copies_n
    head_width = STRIDE * channels // groups_n
    head_here = head_width // CHANNEL_WIDTH
    query_rows = lat_dev // copies_n
    stripe = device % copies_n

    nq = head_here
    per_t = channels // head_width
    both_local = shorten_both(byte_states, qk_kernel, value_kernel, groups_n, per_t, nq)
    kv_rows = both_local.shape[1]
    if copies_n > 1:
        both_local = jnp.broadcast_to(
            both_local[:, None], (groups_n, copies_n, kv_rows, CHANNEL_WIDTH)
        ).reshape(n_ctx, kv_rows, CHANNEL_WIDTH)
    both_all = lax.all_to_all(both_local, "ctx", split_axis=0, concat_axis=0, tiled=True)
    main_kv = both_all[:, : 2 * nq * lat_dev].reshape(n_ctx, 2 * nq, lat_dev, CHANNEL_WIDTH)
    edge = both_all[:, 2 * nq * lat_dev : 2 * nq * lat_dev + 6 * nq].astype(jnp.float32)
    edge = edge.reshape(n_ctx, 3, 2 * nq, CHANNEL_WIDTH)
    own_first = main_kv[:, :, 0].astype(jnp.float32) + edge[:, 0]
    from_before = edge[:, 1] + edge[:, 2]
    from_before = jnp.concatenate([jnp.zeros_like(from_before[:1]), from_before[:-1]], 0)
    first_rows = (own_first + from_before).astype(jnp.bfloat16)
    at_first = lax.broadcasted_iota(jnp.int32, main_kv.shape, 2) == 0
    main_kv = jnp.where(at_first, first_rows[:, :, None, :], main_kv)
    key_all = main_kv[:, :nq]
    value_all = main_kv[:, nq:]
    queries = key_all.reshape(n_ctx, nq, copies_n, query_rows, CHANNEL_WIDTH)[:, :, 0]
    if copies_n > 1:
        queries = lax.dynamic_index_in_dim(
            key_all.reshape(n_ctx, nq, copies_n, query_rows, CHANNEL_WIDTH), stripe, 2, keepdims=False
        )
    query_count = n_ctx * query_rows
    query_heads = queries.transpose(1, 0, 2, 3).reshape(nq, query_count, CHANNEL_WIDTH)
    key_heads = key_all.transpose(1, 0, 2, 3).reshape(nq, lat_total, CHANNEL_WIDTH)
    value_heads = value_all.transpose(1, 0, 2, 3).reshape(nq, lat_total, CHANNEL_WIDTH)
    asking_index = (
        jnp.arange(n_ctx, dtype=jnp.int32)[:, None] * lat_dev
        + stripe * query_rows
        + jnp.arange(query_rows, dtype=jnp.int32)[None, :]
    ).reshape(query_count)
    query_seg = lax.dynamic_index_in_dim(
        block_ids.reshape(n_ctx, copies_n, query_rows), stripe, 1, keepdims=False
    ).reshape(query_count)
    lat_len = doc_length[0] // STRIDE
    sharpness_divisor = jnp.log(asking_index.astype(jnp.float32) + 2.0) / (
        math.sqrt(float(CHANNEL_WIDTH)) * math.sqrt(math.log(float(lat_total)))
    )
    block_len = min(lat_total, max(512, lat_total // 16))
    block_count = lat_total // block_len

    def attend(running, key_start):
        key_block = lax.dynamic_slice_in_dim(key_heads, key_start, block_len, 1)
        value_block = lax.dynamic_slice_in_dim(value_heads, key_start, block_len, 1)
        seg_block = lax.dynamic_slice_in_dim(block_ids, key_start, block_len, 0)
        key_pos = key_start + jnp.arange(block_len, dtype=jnp.int32)
        run_max, run_sum, run_acc = running
        raw_affinity = (
            jnp.einsum("hqd,hkd->hqk", query_heads, key_block, preferred_element_type=jnp.float32)
            * sharpness_divisor[None, :, None]
        )
        visible = (
            (seg_block[None, :] <= query_seg[:, None])
            & (key_pos[None, :] < lat_len)
            & ((key_pos[None, :] != asking_index[:, None]) | (asking_index[:, None] == 0))
        )
        new_max = jnp.maximum(
            run_max, jnp.max(jnp.where(visible[None], raw_affinity, -1e30), axis=2)
        )
        weights = jnp.where(visible[None], jnp.exp(raw_affinity - new_max[:, :, None]), 0.0)
        factor = jnp.exp(run_max - new_max)
        new_sum = run_sum * factor + jnp.sum(weights, axis=2)
        new_acc = run_acc * factor[:, :, None] + jnp.einsum(
            "hqk,hkd->hqd",
            weights.astype(jnp.bfloat16),
            value_block,
            preferred_element_type=jnp.float32,
        )
        updated = (new_max, new_sum, new_acc)
        return (updated, None)

    initial = (
        jnp.full((head_here, query_count), -1e30, jnp.float32),
        jnp.zeros((head_here, query_count), jnp.float32),
        jnp.zeros((head_here, query_count, CHANNEL_WIDTH), jnp.float32),
    )
    finals, unused = lax.scan(attend, initial, jnp.arange(block_count, dtype=jnp.int32) * block_len)
    attended = (finals[2] / finals[1][:, :, None]).astype(jnp.bfloat16)
    attended = attended.reshape(nq, n_ctx, query_rows, CHANNEL_WIDTH).transpose(1, 0, 2, 3)
    rim_out = jnp.concatenate(
        [jnp.zeros((1, nq, 2, CHANNEL_WIDTH), jnp.bfloat16), attended[:-1, :, query_rows - 2 :]], 0
    )
    main_rows = nq * query_rows
    used_rows = main_rows + 2 * nq
    ret_rows = used_rows
    outgoing = jnp.concatenate(
        [
            attended.reshape(n_ctx, main_rows, CHANNEL_WIDTH),
            rim_out.reshape(n_ctx, 2 * nq, CHANNEL_WIDTH),
            jnp.zeros((n_ctx, ret_rows - used_rows, CHANNEL_WIDTH), jnp.bfloat16),
        ],
        1,
    )
    returned = lax.all_to_all(outgoing, "ctx", split_axis=0, concat_axis=0, tiled=True)
    limit = (doc_length[0] - device * rows_here).reshape(1).astype(jnp.int32)
    return up_and_mix(limit, returned, byte_states, up_kernel, copies_n, per_t, nq, query_rows)

def solution(mesh):
    return jax.shard_map(
        body,
        mesh=mesh,
        in_specs=(
            P(("groups", "ctx"), "head"),
            P("groups"),
            P("groups"),
            P(None, None, "head"),
            P(None, None, "head"),
            P(None, None, "head"),
        ),
        out_specs=P(("groups", "ctx"), "head"),
        check_vma=False,
    )
```

```python
import functools
import math

import jax
import jax.numpy as jnp
from jax import lax
from jax.experimental import pallas as pl
from jax.experimental.pallas import tpu as pltpu
from jax.sharding import PartitionSpec as P

CHANNEL_WIDTH = 128
STRIDE = 4
KERNEL = 8


def shifted(x, axis, by):
    devices = lax.axis_size(axis)
    pairs = [(i, i + by) for i in range(devices) if 0 <= i + by < devices]
    return lax.ppermute(x, axis, pairs)


def three_bf16(value):
    hi = value.astype(jnp.bfloat16)
    rest = value - hi.astype(jnp.float32)
    mid = rest.astype(jnp.bfloat16)
    lo = (rest - mid.astype(jnp.float32)).astype(jnp.bfloat16)
    return hi, mid, lo


def exact_rows(select, value):
    total = None
    for piece in three_bf16(value):
        part = jnp.dot(select, piece, preferred_element_type=jnp.float32)
        total = part if total is None else total + part
    return total


def split_pair(value):
    hi = value.astype(jnp.bfloat16)
    lo = (value - hi.astype(jnp.float32)).astype(jnp.bfloat16)
    return hi, lo


def shorten_kernel(per_t, nq, x_ref, qk_ref, vk_ref, out_ref, taps_ref):
    rows, channels = x_ref.shape
    lat = rows // STRIDE
    lanes = CHANNEL_WIDTH
    blocks = channels // lanes
    pick_row = lax.broadcasted_iota(jnp.int32, (rows, rows), 0)
    pick_col = lax.broadcasted_iota(jnp.int32, (rows, rows), 1)
    pick = (pick_col == (pick_row % lat) * STRIDE + pick_row // lat).astype(jnp.bfloat16)
    by_phase = exact_rows(pick, x_ref[...])
    first_row = lax.broadcasted_iota(jnp.int32, (lat, channels), 0) == 0
    phase = []
    for s in range(STRIDE):
        current = by_phase[s * lat : (s + 1) * lat]
        phase.append(current)
        taps_ref[STRIDE + s] = current
        taps_ref[s] = jnp.where(first_row, 0.0, pltpu.roll(current, 1, 0))
    kerns = (qk_ref, vk_ref)
    chunk = 16

    def rows_of(r, carry):
        start = pl.multiple_of(r * chunk, chunk)
        for block in range(blocks):
            lane = pl.ds(block * lanes, lanes)
            taps = [taps_ref[k, pl.ds(start, chunk), lane] for k in range(KERNEL)]
            for which, kern_ref in enumerate(kerns):
                slot = which * nq + block % nq
                for t in range(STRIDE):
                    total = taps[0] * kern_ref[0, pl.ds(t, 1), lane]
                    for k in range(1, KERNEL):
                        total = total + taps[k] * kern_ref[k, pl.ds(t, 1), lane]
                    g = t * per_t + block // nq
                    out_ref[g, pl.ds(pl.multiple_of(slot * lat + start, chunk), chunk), :] = total.astype(
                        jnp.bfloat16
                    )
        return carry

    lax.fori_loop(0, lat // chunk, rows_of, 0)
    edge_rows = -(-6 * nq // 8) * 8
    edge_row = lax.broadcasted_iota(jnp.int32, (edge_rows, lanes), 0)
    edge = [jnp.zeros((edge_rows, lanes), jnp.float32) for _ in range(STRIDE * per_t)]
    for which, kern_ref in enumerate(kerns):
        for t in range(STRIDE):
            own = phase[0][0:1] * kern_ref[STRIDE, pl.ds(t, 1), :]
            before = phase[0][lat - 1 : lat] * kern_ref[0, pl.ds(t, 1), :]
            for s in range(1, STRIDE):
                own = own + phase[s][0:1] * kern_ref[STRIDE + s, pl.ds(t, 1), :]
                before = before + phase[s][lat - 1 : lat] * kern_ref[s, pl.ds(t, 1), :]
            own_hi, own_lo = split_pair(own)
            next_hi, next_lo = split_pair(before)
            for block in range(blocks):
                lane = slice(block * lanes, (block + 1) * lanes)
                g = t * per_t + block // nq
                slot = which * nq + block % nq
                for e, piece in enumerate((own_lo, next_hi, next_lo)):
                    edge[g] = jnp.where(edge_row == e * 2 * nq + slot, piece[:, lane].astype(jnp.float32), edge[g])
    for g in range(STRIDE * per_t):
        out_ref[g, pl.ds(2 * nq * lat, 6 * nq), :] = edge[g][: 6 * nq].astype(jnp.bfloat16)


def shorten_both(byte_states, qk_kernel, value_kernel, groups_n, per_t, nq):
    rows, channels = byte_states.shape
    lat = rows // STRIDE
    kv_rows = 2 * nq * lat + 6 * nq
    vmem = pl.BlockSpec(memory_space=pltpu.VMEM)
    return pl.pallas_call(
        functools.partial(shorten_kernel, per_t, nq),
        out_shape=jax.ShapeDtypeStruct((groups_n, kv_rows, CHANNEL_WIDTH), jnp.bfloat16),
        in_specs=[vmem] * 3,
        out_specs=vmem,
        scratch_shapes=[pltpu.VMEM((KERNEL, lat, channels), jnp.float32)],
        cost_estimate=pl.CostEstimate(
            flops=4 * KERNEL * rows * channels + 6 * rows * rows * channels,
            bytes_accessed=4 * rows * channels + 2 * KERNEL * STRIDE * channels * 4 + 2 * rows * channels * 2,
            transcendentals=0,
        ),
    )(byte_states, qk_kernel, value_kernel)


def up_kernel_fn(copies_n, per_t, nq, qr, lim_ref, ret_ref, x_ref, up_ref, out_ref, prior_ref, phase_ref):
    rows, channels = x_ref.shape
    lat = rows // STRIDE
    lanes = CHANNEL_WIDTH
    blocks = channels // lanes
    row = lax.broadcasted_iota(jnp.int32, (lat, channels), 0)
    for t in range(STRIDE):
        att_parts = []
        rim_parts = []
        for block in range(blocks):
            g = t * per_t + block // nq
            q = block % nq
            pieces = [ret_ref[g * copies_n + s, pl.ds(q * qr, qr), :] for s in range(copies_n)]
            att_parts.append(pieces[0] if copies_n == 1 else jnp.concatenate(pieces, 0))
            rim_parts.append(ret_ref[g * copies_n + copies_n - 1, pl.ds(nq * qr + 2 * q, 2), :])
        att = jnp.concatenate(att_parts, 1).astype(jnp.float32)
        rim = jnp.concatenate(rim_parts, 1).astype(jnp.float32)
        prior_ref[t] = jnp.where(row == 0, rim[1:2], pltpu.roll(att, 1, 0))
        prior_ref[STRIDE + t] = jnp.where(row == 0, rim[0:1], jnp.where(row == 1, rim[1:2], pltpu.roll(att, 2, 0)))
    chunk = 16

    def rows_of(r, carry):
        start = pl.multiple_of(r * chunk, chunk)
        for block in range(blocks):
            lane = pl.ds(block * lanes, lanes)
            one = [prior_ref[t, pl.ds(start, chunk), lane] for t in range(STRIDE)]
            two = [prior_ref[STRIDE + t, pl.ds(start, chunk), lane] for t in range(STRIDE)]
            for s in range(STRIDE):
                total = one[0] * up_ref[s, pl.ds(0, 1), lane] + two[0] * up_ref[s + STRIDE, pl.ds(0, 1), lane]
                for t in range(1, STRIDE):
                    total = total + one[t] * up_ref[s, pl.ds(t, 1), lane]
                    total = total + two[t] * up_ref[s + STRIDE, pl.ds(t, 1), lane]
                phase_ref[pl.ds(pl.multiple_of(s * lat + start, chunk), chunk), lane] = total
        return carry

    lax.fori_loop(0, lat // chunk, rows_of, 0)
    by_phase = phase_ref[...]
    put_row = lax.broadcasted_iota(jnp.int32, (rows, rows), 0)
    put_col = lax.broadcasted_iota(jnp.int32, (rows, rows), 1)
    put = (put_col == (put_row % STRIDE) * lat + put_row // STRIDE).astype(jnp.bfloat16)
    branch = exact_rows(put, by_phase)
    byte_row = lax.broadcasted_iota(jnp.int32, (rows, channels), 0)
    out_ref[...] = x_ref[...] + jnp.where(byte_row < lim_ref[0], branch, 0.0)


def up_and_mix(limit, returned, byte_states, up_kernel, copies_n, per_t, nq, qr):
    rows, channels = byte_states.shape
    vmem = pl.BlockSpec(memory_space=pltpu.VMEM)
    return pl.pallas_call(
        functools.partial(up_kernel_fn, copies_n, per_t, nq, qr),
        out_shape=jax.ShapeDtypeStruct((rows, channels), jnp.float32),
        in_specs=[pl.BlockSpec(memory_space=pltpu.SMEM), vmem, vmem, vmem],
        out_specs=vmem,
        scratch_shapes=[
            pltpu.VMEM((2 * STRIDE, rows // STRIDE, channels), jnp.float32),
            pltpu.VMEM((rows, channels), jnp.float32),
        ],
        cost_estimate=pl.CostEstimate(
            flops=4 * KERNEL * rows * channels + 6 * rows * rows * channels,
            bytes_accessed=8 * rows * channels + returned.size * 2,
            transcendentals=0,
        ),
    )(limit, returned, byte_states, up_kernel)


def body(byte_states, doc_length, block_ids, qk_kernel, value_kernel, up_kernel):
    rows_here, channels = byte_states.shape
    lat_dev = rows_here // STRIDE
    n_ctx = lax.axis_size("ctx")
    device = lax.axis_index("ctx")
    lat_total = lat_dev * n_ctx
    local_heads = STRIDE * channels // CHANNEL_WIDTH
    copies_n = max(1, n_ctx // local_heads)
    groups_n = n_ctx // copies_n
    head_width = STRIDE * channels // groups_n
    head_here = head_width // CHANNEL_WIDTH
    query_rows = lat_dev // copies_n
    stripe = device % copies_n

    nq = head_here
    per_t = channels // head_width
    both_local = shorten_both(byte_states, qk_kernel, value_kernel, groups_n, per_t, nq)
    kv_rows = both_local.shape[1]
    if copies_n > 1:
        both_local = jnp.broadcast_to(
            both_local[:, None], (groups_n, copies_n, kv_rows, CHANNEL_WIDTH)
        ).reshape(n_ctx, kv_rows, CHANNEL_WIDTH)
    both_all = lax.all_to_all(both_local, "ctx", split_axis=0, concat_axis=0, tiled=True)
    main_kv = both_all[:, : 2 * nq * lat_dev].reshape(n_ctx, 2 * nq, lat_dev, CHANNEL_WIDTH)
    edge = both_all[:, 2 * nq * lat_dev : 2 * nq * lat_dev + 6 * nq].astype(jnp.float32)
    edge = edge.reshape(n_ctx, 3, 2 * nq, CHANNEL_WIDTH)
    own_first = main_kv[:, :, 0].astype(jnp.float32) + edge[:, 0]
    from_before = edge[:, 1] + edge[:, 2]
    from_before = jnp.concatenate([jnp.zeros_like(from_before[:1]), from_before[:-1]], 0)
    first_rows = (own_first + from_before).astype(jnp.bfloat16)
    at_first = lax.broadcasted_iota(jnp.int32, main_kv.shape, 2) == 0
    main_kv = jnp.where(at_first, first_rows[:, :, None, :], main_kv)
    key_all = main_kv[:, :nq]
    value_all = main_kv[:, nq:]
    queries = key_all.reshape(n_ctx, nq, copies_n, query_rows, CHANNEL_WIDTH)[:, :, 0]
    if copies_n > 1:
        queries = lax.dynamic_index_in_dim(
            key_all.reshape(n_ctx, nq, copies_n, query_rows, CHANNEL_WIDTH), stripe, 2, keepdims=False
        )
    query_count = n_ctx * query_rows
    query_heads = queries.transpose(1, 0, 2, 3).reshape(nq, query_count, CHANNEL_WIDTH)
    key_heads = key_all.transpose(1, 0, 2, 3).reshape(nq, lat_total, CHANNEL_WIDTH)
    value_heads = value_all.transpose(1, 0, 2, 3).reshape(nq, lat_total, CHANNEL_WIDTH)
    asking_index = (
        jnp.arange(n_ctx, dtype=jnp.int32)[:, None] * lat_dev
        + stripe * query_rows
        + jnp.arange(query_rows, dtype=jnp.int32)[None, :]
    ).reshape(query_count)
    query_seg = lax.dynamic_index_in_dim(
        block_ids.reshape(n_ctx, copies_n, query_rows), stripe, 1, keepdims=False
    ).reshape(query_count)
    lat_len = doc_length[0] // STRIDE
    sharpness_divisor = jnp.log(asking_index.astype(jnp.float32) + 2.0) / (
        math.sqrt(float(CHANNEL_WIDTH)) * math.sqrt(math.log(float(lat_total)))
    )
    block_len = min(lat_total, max(512, lat_total // 16))
    block_count = lat_total // block_len

    def attend(running, key_start):
        key_block = lax.dynamic_slice_in_dim(key_heads, key_start, block_len, 1)
        value_block = lax.dynamic_slice_in_dim(value_heads, key_start, block_len, 1)
        seg_block = lax.dynamic_slice_in_dim(block_ids, key_start, block_len, 0)
        key_pos = key_start + jnp.arange(block_len, dtype=jnp.int32)
        run_max, run_sum, run_acc = running
        raw_affinity = (
            jnp.einsum("hqd,hkd->hqk", query_heads, key_block, preferred_element_type=jnp.float32)
            * sharpness_divisor[None, :, None]
        )
        visible = (
            (seg_block[None, :] <= query_seg[:, None])
            & (key_pos[None, :] < lat_len)
            & ((key_pos[None, :] != asking_index[:, None]) | (asking_index[:, None] == 0))
        )
        new_max = jnp.maximum(
            run_max, jnp.max(jnp.where(visible[None], raw_affinity, -1e30), axis=2)
        )
        weights = jnp.where(visible[None], jnp.exp(raw_affinity - new_max[:, :, None]), 0.0)
        factor = jnp.exp(run_max - new_max)
        new_sum = run_sum * factor + jnp.sum(weights, axis=2)
        new_acc = run_acc * factor[:, :, None] + jnp.einsum(
            "hqk,hkd->hqd",
            weights.astype(jnp.bfloat16),
            value_block,
            preferred_element_type=jnp.float32,
        )
        updated = (new_max, new_sum, new_acc)
        return (updated, None)

    initial = (
        jnp.full((head_here, query_count), -1e30, jnp.float32),
        jnp.zeros((head_here, query_count), jnp.float32),
        jnp.zeros((head_here, query_count, CHANNEL_WIDTH), jnp.float32),
    )
    finals, unused = lax.scan(attend, initial, jnp.arange(block_count, dtype=jnp.int32) * block_len)
    attended = (finals[2] / finals[1][:, :, None]).astype(jnp.bfloat16)
    attended = attended.reshape(nq, n_ctx, query_rows, CHANNEL_WIDTH).transpose(1, 0, 2, 3)
    rim_out = jnp.concatenate(
        [jnp.zeros((1, nq, 2, CHANNEL_WIDTH), jnp.bfloat16), attended[:-1, :, query_rows - 2 :]], 0
    )
    main_rows = nq * query_rows
    used_rows = main_rows + 2 * nq
    ret_rows = used_rows
    outgoing = jnp.concatenate(
        [
            attended.reshape(n_ctx, main_rows, CHANNEL_WIDTH),
            rim_out.reshape(n_ctx, 2 * nq, CHANNEL_WIDTH),
            jnp.zeros((n_ctx, ret_rows - used_rows, CHANNEL_WIDTH), jnp.bfloat16),
        ],
        1,
    )
    returned = lax.all_to_all(outgoing, "ctx", split_axis=0, concat_axis=0, tiled=True)
    limit = (doc_length[0] - device * rows_here).reshape(1).astype(jnp.int32)
    return up_and_mix(limit, returned, byte_states, up_kernel, copies_n, per_t, nq, query_rows)

def solution(mesh):
    return jax.shard_map(
        body,
        mesh=mesh,
        in_specs=(
            P(("groups", "ctx"), "head"),
            P("groups"),
            P("groups"),
            P(None, None, "head"),
            P(None, None, "head"),
            P(None, None, "head"),
        ),
        out_specs=P(("groups", "ctx"), "head"),
        check_vma=False,
    )
```

```python
import functools
import math

import jax
import jax.numpy as jnp
from jax import lax
from jax.experimental import pallas as pl
from jax.experimental.pallas import tpu as pltpu
from jax.sharding import PartitionSpec as P

CHANNEL_WIDTH = 128
STRIDE = 4
KERNEL = 8


def shifted(x, axis, by):
    devices = lax.axis_size(axis)
    pairs = [(i, i + by) for i in range(devices) if 0 <= i + by < devices]
    return lax.ppermute(x, axis, pairs)


def three_bf16(value):
    hi = value.astype(jnp.bfloat16)
    rest = value - hi.astype(jnp.float32)
    mid = rest.astype(jnp.bfloat16)
    lo = (rest - mid.astype(jnp.float32)).astype(jnp.bfloat16)
    return hi, mid, lo


def exact_rows(select, value):
    total = None
    for piece in three_bf16(value):
        part = jnp.dot(select, piece, preferred_element_type=jnp.float32)
        total = part if total is None else total + part
    return total


def split_pair(value):
    hi = value.astype(jnp.bfloat16)
    lo = (value - hi.astype(jnp.float32)).astype(jnp.bfloat16)
    return hi, lo


def shorten_kernel(per_t, nq, x_ref, qk_ref, vk_ref, out_ref):
    rows, channels = x_ref.shape
    lat = rows // STRIDE
    lanes = CHANNEL_WIDTH
    blocks = channels // lanes
    pick_row = lax.broadcasted_iota(jnp.int32, (rows, rows), 0)
    pick_col = lax.broadcasted_iota(jnp.int32, (rows, rows), 1)
    pick = (pick_col == (pick_row % lat) * STRIDE + pick_row // lat).astype(jnp.bfloat16)
    by_phase = exact_rows(pick, x_ref[...])
    phase = [by_phase[s * lat : (s + 1) * lat] for s in range(STRIDE)]
    first_row = lax.broadcasted_iota(jnp.int32, (lat, channels), 0) == 0
    edge_rows = -(-2 * nq // 8) * 8
    edge_row = lax.broadcasted_iota(jnp.int32, (edge_rows, lanes), 0)
    edge = [jnp.zeros((edge_rows, lanes), jnp.float32) for _ in range(STRIDE * per_t)]
    for which, kern_ref in enumerate((qk_ref, vk_ref)):
        for t in range(STRIDE):
            own = phase[0] * kern_ref[STRIDE, pl.ds(t, 1), :]
            before = phase[0] * kern_ref[0, pl.ds(t, 1), :]
            for s in range(1, STRIDE):
                own = own + phase[s] * kern_ref[STRIDE + s, pl.ds(t, 1), :]
                before = before + phase[s] * kern_ref[s, pl.ds(t, 1), :]
            total = own + jnp.where(first_row, 0.0, pltpu.roll(before, 1, 0))
            total = total.astype(jnp.bfloat16)
            own_hi, own_lo = split_pair(own[0:1])
            next_hi, next_lo = split_pair(before[lat - 1 : lat])
            for block in range(blocks):
                lane = slice(block * lanes, (block + 1) * lanes)
                g = t * per_t + block // nq
                slot = which * nq + block % nq
                out_ref[g, pl.ds(slot * lat, lat), :] = total[:, lane]
                for e, piece in enumerate((next_hi,)):
                    edge[g] = jnp.where(edge_row == e * 2 * nq + slot, piece[:, lane].astype(jnp.float32), edge[g])
    for g in range(STRIDE * per_t):
        out_ref[g, pl.ds(2 * nq * lat, 2 * nq), :] = edge[g][: 2 * nq].astype(jnp.bfloat16)


def shorten_both(byte_states, qk_kernel, value_kernel, groups_n, per_t, nq):
    rows, channels = byte_states.shape
    lat = rows // STRIDE
    kv_rows = 2 * nq * lat + 2 * nq
    vmem = pl.BlockSpec(memory_space=pltpu.VMEM)
    return pl.pallas_call(
        functools.partial(shorten_kernel, per_t, nq),
        out_shape=jax.ShapeDtypeStruct((groups_n, kv_rows, CHANNEL_WIDTH), jnp.bfloat16),
        in_specs=[vmem] * 3,
        out_specs=vmem,
        cost_estimate=pl.CostEstimate(
            flops=4 * KERNEL * rows * channels + 6 * rows * rows * channels,
            bytes_accessed=4 * rows * channels + 2 * KERNEL * STRIDE * channels * 4 + 2 * rows * channels * 2,
            transcendentals=0,
        ),
    )(byte_states, qk_kernel, value_kernel)


def up_kernel_fn(copies_n, per_t, nq, qr, lim_ref, ret_ref, x_ref, up_ref, out_ref):
    rows, channels = x_ref.shape
    lat = rows // STRIDE
    lanes = CHANNEL_WIDTH
    blocks = channels // lanes
    row = lax.broadcasted_iota(jnp.int32, (lat, channels), 0)
    prior_one = []
    prior_two = []
    for t in range(STRIDE):
        att_parts = []
        rim_parts = []
        for block in range(blocks):
            g = t * per_t + block // nq
            q = block % nq
            pieces = [ret_ref[g * copies_n + s, pl.ds(q * qr, qr), :] for s in range(copies_n)]
            att_parts.append(pieces[0] if copies_n == 1 else jnp.concatenate(pieces, 0))
            rim_parts.append(ret_ref[g * copies_n + copies_n - 1, pl.ds(nq * qr + 2 * q, 2), :])
        att = jnp.concatenate(att_parts, 1).astype(jnp.float32)
        rim = jnp.concatenate(rim_parts, 1).astype(jnp.float32)
        one = jnp.where(row == 0, rim[1:2], pltpu.roll(att, 1, 0))
        two = jnp.where(row == 0, rim[0:1], jnp.where(row == 1, rim[1:2], pltpu.roll(att, 2, 0)))
        prior_one.append(one)
        prior_two.append(two)
    by_phase = []
    for s in range(STRIDE):
        total = prior_one[0] * up_ref[s, pl.ds(0, 1), :] + prior_two[0] * up_ref[s + STRIDE, pl.ds(0, 1), :]
        for t in range(1, STRIDE):
            total = total + prior_one[t] * up_ref[s, pl.ds(t, 1), :]
            total = total + prior_two[t] * up_ref[s + STRIDE, pl.ds(t, 1), :]
        by_phase.append(total)
    by_phase = jnp.concatenate(by_phase, 0)
    put_row = lax.broadcasted_iota(jnp.int32, (rows, rows), 0)
    put_col = lax.broadcasted_iota(jnp.int32, (rows, rows), 1)
    put = (put_col == (put_row % STRIDE) * lat + put_row // STRIDE).astype(jnp.bfloat16)
    branch = exact_rows(put, by_phase)
    byte_row = lax.broadcasted_iota(jnp.int32, (rows, channels), 0)
    out_ref[...] = x_ref[...] + jnp.where(byte_row < lim_ref[0], branch, 0.0)


def up_and_mix(limit, returned, byte_states, up_kernel, copies_n, per_t, nq, qr):
    rows, channels = byte_states.shape
    vmem = pl.BlockSpec(memory_space=pltpu.VMEM)
    return pl.pallas_call(
        functools.partial(up_kernel_fn, copies_n, per_t, nq, qr),
        out_shape=jax.ShapeDtypeStruct((rows, channels), jnp.float32),
        in_specs=[pl.BlockSpec(memory_space=pltpu.SMEM), vmem, vmem, vmem],
        out_specs=vmem,
        cost_estimate=pl.CostEstimate(
            flops=4 * KERNEL * rows * channels + 6 * rows * rows * channels,
            bytes_accessed=8 * rows * channels + returned.size * 2,
            transcendentals=0,
        ),
    )(limit, returned, byte_states, up_kernel)


def body(byte_states, doc_length, block_ids, qk_kernel, value_kernel, up_kernel):
    rows_here, channels = byte_states.shape
    lat_dev = rows_here // STRIDE
    n_ctx = lax.axis_size("ctx")
    device = lax.axis_index("ctx")
    lat_total = lat_dev * n_ctx
    local_heads = STRIDE * channels // CHANNEL_WIDTH
    copies_n = max(1, n_ctx // local_heads)
    groups_n = n_ctx // copies_n
    head_width = STRIDE * channels // groups_n
    head_here = head_width // CHANNEL_WIDTH
    query_rows = lat_dev // copies_n
    stripe = device % copies_n

    nq = head_here
    per_t = channels // head_width
    both_local = shorten_both(byte_states, qk_kernel, value_kernel, groups_n, per_t, nq)
    kv_rows = both_local.shape[1]
    if copies_n > 1:
        both_local = jnp.broadcast_to(
            both_local[:, None], (groups_n, copies_n, kv_rows, CHANNEL_WIDTH)
        ).reshape(n_ctx, kv_rows, CHANNEL_WIDTH)
    both_all = lax.all_to_all(both_local, "ctx", split_axis=0, concat_axis=0, tiled=True)
    main_kv = both_all[:, : 2 * nq * lat_dev].reshape(n_ctx, 2 * nq, lat_dev, CHANNEL_WIDTH)
    edge = both_all[:, 2 * nq * lat_dev : 2 * nq * lat_dev + 2 * nq].astype(jnp.float32)
    own_first = main_kv[:, :, 0].astype(jnp.float32)
    from_before = edge
    from_before = jnp.concatenate([jnp.zeros_like(from_before[:1]), from_before[:-1]], 0)
    first_rows = (own_first + from_before).astype(jnp.bfloat16)
    at_first = lax.broadcasted_iota(jnp.int32, main_kv.shape, 2) == 0
    main_kv = jnp.where(at_first, first_rows[:, :, None, :], main_kv)
    key_all = main_kv[:, :nq]
    value_all = main_kv[:, nq:]
    queries = key_all.reshape(n_ctx, nq, copies_n, query_rows, CHANNEL_WIDTH)[:, :, 0]
    if copies_n > 1:
        queries = lax.dynamic_index_in_dim(
            key_all.reshape(n_ctx, nq, copies_n, query_rows, CHANNEL_WIDTH), stripe, 2, keepdims=False
        )
    query_count = n_ctx * query_rows
    query_heads = queries.transpose(1, 0, 2, 3).reshape(nq, query_count, CHANNEL_WIDTH)
    key_heads = key_all.transpose(1, 0, 2, 3).reshape(nq, lat_total, CHANNEL_WIDTH)
    value_heads = value_all.transpose(1, 0, 2, 3).reshape(nq, lat_total, CHANNEL_WIDTH)
    asking_index = (
        jnp.arange(n_ctx, dtype=jnp.int32)[:, None] * lat_dev
        + stripe * query_rows
        + jnp.arange(query_rows, dtype=jnp.int32)[None, :]
    ).reshape(query_count)
    query_seg = lax.dynamic_index_in_dim(
        block_ids.reshape(n_ctx, copies_n, query_rows), stripe, 1, keepdims=False
    ).reshape(query_count)
    lat_len = doc_length[0] // STRIDE
    sharpness_divisor = jnp.log(asking_index.astype(jnp.float32) + 2.0) / (
        math.sqrt(float(CHANNEL_WIDTH)) * math.sqrt(math.log(float(lat_total)))
    )
    block_len = min(lat_total, max(512, lat_total // 16))
    block_count = lat_total // block_len

    def attend(running, key_start):
        key_block = lax.dynamic_slice_in_dim(key_heads, key_start, block_len, 1)
        value_block = lax.dynamic_slice_in_dim(value_heads, key_start, block_len, 1)
        seg_block = lax.dynamic_slice_in_dim(block_ids, key_start, block_len, 0)
        key_pos = key_start + jnp.arange(block_len, dtype=jnp.int32)
        run_max, run_sum, run_acc = running
        raw_affinity = (
            jnp.einsum("hqd,hkd->hqk", query_heads, key_block, preferred_element_type=jnp.float32)
            * sharpness_divisor[None, :, None]
        )
        visible = (
            (seg_block[None, :] <= query_seg[:, None])
            & (key_pos[None, :] < lat_len)
            & ((key_pos[None, :] != asking_index[:, None]) | (asking_index[:, None] == 0))
        )
        new_max = jnp.maximum(
            run_max, jnp.max(jnp.where(visible[None], raw_affinity, -1e30), axis=2)
        )
        weights = jnp.where(visible[None], jnp.exp(raw_affinity - new_max[:, :, None]), 0.0)
        factor = jnp.exp(run_max - new_max)
        new_sum = run_sum * factor + jnp.sum(weights, axis=2)
        new_acc = run_acc * factor[:, :, None] + jnp.einsum(
            "hqk,hkd->hqd",
            weights.astype(jnp.bfloat16),
            value_block,
            preferred_element_type=jnp.float32,
        )
        updated = (new_max, new_sum, new_acc)
        return (updated, None)

    initial = (
        jnp.full((head_here, query_count), -1e30, jnp.float32),
        jnp.zeros((head_here, query_count), jnp.float32),
        jnp.zeros((head_here, query_count, CHANNEL_WIDTH), jnp.float32),
    )
    finals, unused = lax.scan(attend, initial, jnp.arange(block_count, dtype=jnp.int32) * block_len)
    attended = (finals[2] / finals[1][:, :, None]).astype(jnp.bfloat16)
    attended = attended.reshape(nq, n_ctx, query_rows, CHANNEL_WIDTH).transpose(1, 0, 2, 3)
    rim_out = jnp.concatenate(
        [jnp.zeros((1, nq, 2, CHANNEL_WIDTH), jnp.bfloat16), attended[:-1, :, query_rows - 2 :]], 0
    )
    main_rows = nq * query_rows
    used_rows = main_rows + 2 * nq
    ret_rows = used_rows
    outgoing = jnp.concatenate(
        [
            attended.reshape(n_ctx, main_rows, CHANNEL_WIDTH),
            rim_out.reshape(n_ctx, 2 * nq, CHANNEL_WIDTH),
            jnp.zeros((n_ctx, ret_rows - used_rows, CHANNEL_WIDTH), jnp.bfloat16),
        ],
        1,
    )
    returned = lax.all_to_all(outgoing, "ctx", split_axis=0, concat_axis=0, tiled=True)
    limit = (doc_length[0] - device * rows_here).reshape(1).astype(jnp.int32)
    return up_and_mix(limit, returned, byte_states, up_kernel, copies_n, per_t, nq, query_rows)

def solution(mesh):
    return jax.shard_map(
        body,
        mesh=mesh,
        in_specs=(
            P(("groups", "ctx"), "head"),
            P("groups"),
            P("groups"),
            P(None, None, "head"),
            P(None, None, "head"),
            P(None, None, "head"),
        ),
        out_specs=P(("groups", "ctx"), "head"),
        check_vma=False,
    )
```
